32 devices in a mesh: tm: 2 (over x), space: 16 (over z, y, core).
Axes of the slice: x: 2, y: 2, z: 4, core: 2. Of those that a mesh axis runs over, the one named last changes fastest.
Arguments:
- initial: float32 [2, 64, 128, 256], P(None, None, 'space'), may hold values from -12 to 12
- x_velocity: float32 [64, 128, 256], P(None, 'space'), may hold values from -4 to 4
- y_velocity: float32 [64, 128, 256], P(None, 'space'), may hold values from -1 to 1
- h_diffusion: float32 [64, 128, 256], P(None, 'space'), may hold values from 0.1 to 0.5
- v_diffusion: float32 [64, 128, 256], P(None, 'space'), may hold values from 0.05 to 0.5
- coupling: float32 [2, 2], replicated, may hold values from -0.5 to 0.5
Outputs:
- slab_end: float32 [2, 2, 64, 128, 256], P('tm', None, None, 'space')
The draws below stay inside these ranges and needn't reach their ends.
All inputs are finite; a program needn't handle non-finite values.
Results may differ from the reference program's by a relative error of at most 0.00002.
Values sent between devices are 32-bit elements; how exact they have to be, the bound alone decides.
No kernel may reach another device: no remote copies, remote signals or barrier semaphores. Data moves between devices by JAX's collectives and lax.ppermute only.
A program may use at most 64 MiB of HBM per device.

```python
import math
import jax
import jax.numpy as jnp
from jax import lax

TRACERS = 2
NZ = 64
NY = 256
ITERS = 2
NX = 128
N_TM = 2


def levels(own_key, extent, cuts, low, high):
    loudness, own = 1.0, jax.random.fold_in(own_key, 6)
    for position, shards_of in cuts:
        steps = jnp.exp(jax.random.uniform(jax.random.fold_in(own, position), (shards_of,), jnp.float32, low / len(cuts), high / len(cuts)))
        loudness = loudness * jnp.repeat(steps, extent[position] // shards_of).reshape([-1 if axis == position else 1 for axis in range(len(extent))])
    return loudness


def normal_values(own_key, dims, deviation, bound, split=(), dtype=jnp.bfloat16):
    loudness = levels(own_key, dims, split, -0.22, 0.18) if split else 1.0
    drawn = jax.random.normal(own_key, dims, jnp.float32) * deviation * loudness
    return jnp.minimum(jnp.maximum(drawn, -bound), bound).astype(dtype)


def setup_inputs(seed: int = 0) -> dict:
    seeds = jax.random.split(jax.random.key(seed), 7)
    return {
        "initial": normal_values(seeds[0], (TRACERS, NZ, NX, NY), 2.5, 12.0, ((2, 16),), jnp.float32),
        "x_velocity": jnp.clip(jax.random.uniform(seeds[1], (NZ, NX, NY), jnp.float32, -4.0, 4.0) * levels(seeds[1], (NZ, NX, NY), ((1, 16),), -0.4, 0.0), -4.0, 4.0),
        "y_velocity": jnp.clip(jax.random.uniform(seeds[2], (NZ, NX, NY), jnp.float32, -1.0, 1.0) * levels(seeds[2], (NZ, NX, NY), ((1, 16),), -0.4, 0.0), -1.0, 1.0),
        "h_diffusion": jnp.clip(jnp.exp(math.log(0.5) - 1.609438 * jax.random.uniform(seeds[3], (NZ, NX, NY), jnp.float32) ** levels(seeds[3], (NZ, NX, NY), ((1, 16),), -0.2, 0.2)), 0.1, 0.5),
        "v_diffusion": jnp.clip(jnp.exp(math.log(0.5) - 2.3025851 * jax.random.uniform(seeds[4], (NZ, NX, NY), jnp.float32) ** levels(seeds[4], (NZ, NX, NY), ((1, 16),), -0.2, 0.2)), 0.05, 0.5),
        "coupling": jnp.clip(jax.random.uniform(seeds[5], (TRACERS, TRACERS), jnp.float32, -0.5, 0.5), -0.5, 0.5),
    }


slab_step = 0.5
half_step = 0.25


def tendency(padded, x_speed, y_speed, h_spread, v_spread, coupling, x_spacing, z_spacing):
    middle = padded[..., 1:-1, :]
    eastward = padded[..., 2:, :]
    westward = padded[..., :-2, :]
    y_widths = [(0, 0)] * (middle.ndim - 1) + [(1, 1)]
    y_padded = jnp.pad(middle, y_widths)
    northward = y_padded[..., 2:]
    southward = y_padded[..., :-2]
    z_widths = [(0, 0)] * (middle.ndim - 3) + [(1, 1), (0, 0), (0, 0)]
    z_padded = jnp.pad(middle, z_widths)
    upward = z_padded[..., 2:, :, :]
    downward = z_padded[..., :-2, :, :]
    advection = x_speed * (eastward - westward) / (2.0 * x_spacing) + y_speed * (northward - southward) * 0.5
    diffusion = h_spread * ((eastward - 2.0 * middle + westward) / (x_spacing * x_spacing) + (northward - 2.0 * middle + southward))
    vertical = v_spread * (upward - 2.0 * middle + downward) / (z_spacing * z_spacing)
    reaction = coupling[:, 0].reshape(-1, 1, 1, 1) * middle[..., 0:1, :, :, :]
    for column in range(1, coupling.shape[1]):
        reaction = reaction + coupling[:, column].reshape(-1, 1, 1, 1) * middle[..., column:column + 1, :, :, :]
    return diffusion + vertical - advection + reaction


def shrink(field):
    shape = field.shape
    blocks = field.reshape(shape[:-3] + (shape[-3] // 2, 2, shape[-2] // 2, 2, shape[-1]))
    return (blocks[..., 0, :, 0, :] + blocks[..., 1, :, 0, :] + blocks[..., 0, :, 1, :] + blocks[..., 1, :, 1, :]) * 0.25


def expand(field):
    return jnp.repeat(jnp.repeat(field, 2, axis=-3), 2, axis=-2)


def pad_along_x(field):
    widths = [(0, 0)] * (field.ndim - 2) + [(1, 1), (0, 0)]
    return jnp.pad(field, widths)


def reference(initial, x_velocity, y_velocity, h_diffusion, v_diffusion, coupling):
    coarse_x = shrink(x_velocity)
    coarse_y = shrink(y_velocity)
    coarse_h = shrink(h_diffusion)
    coarse_v = shrink(v_diffusion)

    def fine_one(field):
        return tendency(pad_along_x(field), x_velocity, y_velocity, h_diffusion, v_diffusion, coupling, 1.0, 1.0)

    def coarse_one(field):
        return tendency(pad_along_x(field), coarse_x, coarse_y, coarse_h, coarse_v, coupling, 2.0, 2.0)

    def fine(field):
        return lax.map(fine_one, field)

    def coarse(field):
        return lax.map(coarse_one, field)

    slabs = N_TM
    spread = jnp.broadcast_to(initial, (slabs,) + initial.shape)
    first_rate = jnp.broadcast_to(fine_one(initial), (slabs,) + initial.shape)
    slope_zero, slope_one, slope_two = first_rate, first_rate, first_rate
    coarse_first = shrink(initial)
    start = spread
    result = spread
    for sweep in range(ITERS):
        node_zero = start
        rate_zero = fine(node_zero)
        node_one = node_zero + half_step * (rate_zero - slope_zero) + slab_step * (slope_zero * (5.0 / 24.0) + slope_one * (1.0 / 3.0) - slope_two * (1.0 / 24.0))
        rate_one = fine(node_one)
        node_two = node_one + half_step * (rate_one - slope_one) + slab_step * (slope_zero * (-1.0 / 24.0) + slope_one * (1.0 / 3.0) + slope_two * (5.0 / 24.0))
        rate_two = fine(node_two)
        coarse_zero = shrink(node_zero)
        coarse_end = shrink(node_two)
        source = shrink(slab_step * (rate_zero + 4.0 * rate_one + rate_two) / 6.0)
        offset = source - slab_step * coarse(coarse_zero)

        def chain(carried, extra):
            after = carried + slab_step * coarse_one(carried) + extra
            return after, (carried, after)

        ignored, (begins, finals) = lax.scan(chain, coarse_first, offset)
        delta_zero = begins - coarse_zero
        delta_one = finals - coarse_end
        fixed_zero = node_zero + expand(delta_zero)
        fixed_one = node_one + expand((delta_zero + delta_one) * 0.5)
        fixed_two = node_two + expand(delta_one)
        result = fixed_two
        if sweep + 1 < ITERS:
            slope_zero = fine(fixed_zero)
            slope_one = fine(fixed_one)
            slope_two = fine(fixed_two)
            start = jnp.concatenate([initial[None], fixed_two[:-1]], axis=0)
    return result
```

```python
import jax
import jax.numpy as jnp
from jax import lax
from jax.sharding import PartitionSpec as P

ITERS = 2


slab_step = 0.5
half_step = 0.25


def shift_pairs(count, steps):
    return [(i, i + steps) for i in range(max(0, -steps), min(count, count - steps))]


def exchange(to_right, to_left):
    count = lax.axis_size("space")
    before = lax.ppermute(to_right, "space", shift_pairs(count, 1))
    after = lax.ppermute(to_left, "space", shift_pairs(count, -1))
    return before, after


def lo(field, width=1):
    return field[..., :width, :]


def hi(field, width=1):
    return field[..., field.shape[-2] - width:, :]


def halo_of(field):
    return exchange(hi(field), lo(field))


def tendency(field, halo, x_speed, y_speed, h_spread, v_spread, coupling, x_spacing, z_spacing):
    padded = jnp.concatenate([halo[0], field, halo[1]], axis=-2)
    middle = padded[..., 1:-1, :]
    eastward = padded[..., 2:, :]
    westward = padded[..., :-2, :]
    y_widths = [(0, 0)] * (middle.ndim - 1) + [(1, 1)]
    y_padded = jnp.pad(middle, y_widths)
    northward = y_padded[..., 2:]
    southward = y_padded[..., :-2]
    z_widths = [(0, 0)] * (middle.ndim - 3) + [(1, 1), (0, 0), (0, 0)]
    z_padded = jnp.pad(middle, z_widths)
    upward = z_padded[..., 2:, :, :]
    downward = z_padded[..., :-2, :, :]
    advection = (
        x_speed * (eastward - westward) / (2.0 * x_spacing)
        + y_speed * (northward - southward) * 0.5
    )
    diffusion = h_spread * (
        (eastward - 2.0 * middle + westward) / (x_spacing * x_spacing)
        + (northward - 2.0 * middle + southward)
    )
    vertical = v_spread * (upward - 2.0 * middle + downward) / (z_spacing * z_spacing)
    reaction = coupling[:, 0].reshape(-1, 1, 1, 1) * middle[..., 0:1, :, :, :]
    reaction = reaction + coupling[:, 1].reshape(-1, 1, 1, 1) * middle[..., 1:2, :, :, :]
    return diffusion + vertical - advection + reaction


def shrink(field):
    shape = field.shape
    blocks = field.reshape(shape[:-3] + (shape[-3] // 2, 2, shape[-2] // 2, 2, shape[-1]))
    return (
        blocks[..., 0, :, 0, :]
        + blocks[..., 1, :, 0, :]
        + blocks[..., 0, :, 1, :]
        + blocks[..., 1, :, 1, :]
    ) * 0.25


def expand(field):
    return jnp.repeat(jnp.repeat(field, 2, axis=-3), 2, axis=-2)


def expand_z(field):
    return jnp.repeat(field, 2, axis=-3)


def pick(items, index):
    out = items[0]
    for k in range(1, len(items)):
        out = jax.tree.map(lambda new, old: jnp.where(index == k, new, old), items[k], out)
    return out


def pair_map(fn, *pairs):
    return tuple(fn(*parts) for parts in zip(*pairs))


def body(initial, x_velocity, y_velocity, h_diffusion, v_diffusion, coupling):
    coarse_x = shrink(x_velocity)
    coarse_y = shrink(y_velocity)
    coarse_h = shrink(h_diffusion)
    coarse_v = shrink(v_diffusion)
    slabs = lax.axis_size("tm")
    columns = lax.axis_size("space")
    slab = lax.axis_index("tm")
    first = slab == 0

    def fine_rate(field, halo):
        return tendency(
            field, halo, x_velocity, y_velocity, h_diffusion, v_diffusion, coupling, 1.0, 1.0
        )

    def coarse_rate(field, halo):
        return tendency(field, halo, coarse_x, coarse_y, coarse_h, coarse_v, coupling, 2.0, 2.0)

    def first_node(node_zero, rate_zero, s0, s1, s2):
        return (
            node_zero
            + half_step * (rate_zero - s0)
            + slab_step * (s0 * (5.0 / 24.0) + s1 * (1.0 / 3.0) - s2 * (1.0 / 24.0))
        )

    def second_node(node_one, rate_one, s0, s1, s2):
        return (
            node_one
            + half_step * (rate_one - s1)
            + slab_step * (s0 * (-1.0 / 24.0) + s1 * (1.0 / 3.0) + s2 * (5.0 / 24.0))
        )

    coarse_first = shrink(initial)
    (init_b, first_b), (init_a, first_a) = exchange(
        (hi(initial), hi(coarse_first)), (lo(initial), lo(coarse_first))
    )
    halo_zero = (init_b, init_a)
    halo_first = (first_b, first_a)
    first_rate = fine_rate(initial, halo_zero)
    coarse_first_rate = coarse_rate(coarse_first, halo_first)

    node_zero = initial
    rate_zero = first_rate
    node_one = first_node(node_zero, rate_zero, first_rate, first_rate, first_rate)
    halo_one = halo_of(node_one)
    rate_one = fine_rate(node_one, halo_one)
    node_two = second_node(node_one, rate_one, first_rate, first_rate, first_rate)
    two_b, two_a = exchange(hi(node_two, 2), lo(node_two, 2))
    halo_two = (hi(two_b), lo(two_a))
    coarse_end = shrink(node_two)
    halo_end = (shrink(two_b), shrink(two_a))
    rate_two = fine_rate(node_two, halo_two)
    source = shrink(slab_step * (rate_zero + 4.0 * rate_one + rate_two) / 6.0)
    offset = source - slab_step * coarse_first_rate

    chain = [coarse_first]
    chain_halo = [halo_first]
    rate = coarse_first_rate
    for count in range(slabs):
        after = chain[-1] + slab_step * rate + offset
        after_halo = halo_of(after)
        chain.append(after)
        chain_halo.append(after_halo)
        if count + 1 < slabs:
            rate = coarse_rate(after, after_halo)
    begins = pick(chain, slab)
    finals = pick(chain, slab + 1)
    begins_halo = pick(chain_halo, slab)
    finals_halo = pick(chain_halo, slab + 1)

    delta_zero = begins - coarse_first
    delta_one = finals - coarse_end
    fixed_zero = node_zero + expand(delta_zero)
    fixed_one = node_one + expand((delta_zero + delta_one) * 0.5)
    fixed_two = node_two + expand(delta_one)
    halo_dz = pair_map(lambda y, v: y - v, begins_halo, halo_first)
    halo_d1 = pair_map(lambda y, v: y - v, finals_halo, halo_end)
    halo_f0 = pair_map(lambda w, d: w + expand_z(d), halo_zero, halo_dz)
    halo_f1 = pair_map(
        lambda w, d0, d1: w + expand_z((d0 + d1) * 0.5), halo_one, halo_dz, halo_d1
    )
    halo_f2 = pair_map(lambda w, d: w + expand_z(d), halo_two, halo_d1)

    earlier_delta = begins - coarse_end
    earlier_end = node_two + expand(earlier_delta)
    halo_earlier_delta = pair_map(lambda y, v: y - v, begins_halo, halo_end)
    halo_earlier = pair_map(lambda w, d: w + expand_z(d), halo_two, halo_earlier_delta)
    wide_earlier = (
        two_b + expand(halo_earlier_delta[0]),
        two_a + expand(halo_earlier_delta[1]),
    )
    start = jnp.where(first, initial, earlier_end)
    halo_start = pair_map(lambda a, b: jnp.where(first, a, b), halo_zero, halo_earlier)
    halo_start_coarse = pair_map(
        lambda a, w: jnp.where(first, a, shrink(w)), halo_first, wide_earlier
    )

    slope_zero = fine_rate(fixed_zero, halo_f0)
    slope_one = fine_rate(fixed_one, halo_f1)
    slope_two = fine_rate(fixed_two, halo_f2)
    node_zero = start
    rate_zero = fine_rate(node_zero, halo_start)
    node_one = first_node(node_zero, rate_zero, slope_zero, slope_one, slope_two)
    rate_one = fine_rate(node_one, halo_of(node_one))
    node_two = second_node(node_one, rate_one, slope_zero, slope_one, slope_two)
    rate_two = fine_rate(node_two, halo_of(node_two))
    coarse_zero = shrink(node_zero)
    coarse_end = shrink(node_two)
    source = shrink(slab_step * (rate_zero + 4.0 * rate_one + rate_two) / 6.0)
    offset = source - slab_step * coarse_rate(coarse_zero, halo_start_coarse)

    down = shift_pairs(slabs, 1)
    to_east = [
        (t * columns + c, (t + 1) * columns + c + 1)
        for t in range(slabs - 1)
        for c in range(columns - 1)
    ]
    to_west = [
        (t * columns + c, (t + 1) * columns + c - 1)
        for t in range(slabs - 1)
        for c in range(1, columns)
    ]
    carried = coarse_first
    carried_halo = halo_first
    rate = coarse_first_rate
    for count in range(slabs - 1):
        after = carried + slab_step * rate + offset
        passed = lax.ppermute(after, "tm", down)
        passed_b = lax.ppermute(hi(after), ("tm", "space"), to_east)
        passed_a = lax.ppermute(lo(after), ("tm", "space"), to_west)
        carried = jnp.where(first, coarse_first, passed)
        carried_halo = pair_map(
            lambda a, b: jnp.where(first, a, b), halo_first, (passed_b, passed_a)
        )
        rate = coarse_rate(carried, carried_halo)
    finals = carried + slab_step * rate + offset
    result = node_two + expand(finals - coarse_end)
    return result[None]


def solution(mesh):
    return jax.shard_map(
        body,
        mesh=mesh,
        in_specs=(
            P(None, None, "space", None),
            P(None, "space", None),
            P(None, "space", None),
            P(None, "space", None),
            P(None, "space", None),
            P(),
        ),
        out_specs=P("tm", None, None, "space", None),
        check_vma=False,
    )
```

```python
import jax
import jax.numpy as jnp
from jax import lax
from jax.sharding import PartitionSpec as P

ITERS = 2


slab_step = 0.5
half_step = 0.25


def shift_pairs(count, steps):
    return [(i, i + steps) for i in range(max(0, -steps), min(count, count - steps))]


def exchange(to_right, to_left):
    count = lax.axis_size("space")
    before = lax.ppermute(to_right, "space", shift_pairs(count, 1))
    after = lax.ppermute(to_left, "space", shift_pairs(count, -1))
    return before, after


def lo(field, width=1):
    return field[..., :width, :]


def hi(field, width=1):
    return field[..., field.shape[-2] - width:, :]


def halo_of(field):
    return exchange(hi(field), lo(field))


def tendency(field, halo, x_speed, y_speed, h_spread, v_spread, coupling, x_spacing, z_spacing):
    reach = int(x_spacing)
    padded = jnp.concatenate([halo[0]] * reach + [field] + [halo[1]] * reach, axis=-2)
    width = field.shape[-2]
    middle = field
    eastward = padded[..., 2 * reach:, :]
    westward = padded[..., :width, :]
    y_widths = [(0, 0)] * (middle.ndim - 1) + [(1, 1)]
    y_padded = jnp.pad(middle, y_widths)
    northward = y_padded[..., 2:]
    southward = y_padded[..., :-2]
    z_widths = [(0, 0)] * (middle.ndim - 3) + [(1, 1), (0, 0), (0, 0)]
    z_padded = jnp.pad(middle, z_widths)
    upward = z_padded[..., 2:, :, :]
    downward = z_padded[..., :-2, :, :]
    advection = (
        x_speed * (eastward - westward) / (2.0 * x_spacing)
        + y_speed * (northward - southward) * 0.5
    )
    diffusion = h_spread * (
        (eastward - 2.0 * middle + westward) / (x_spacing * x_spacing)
        + (northward - 2.0 * middle + southward)
    )
    vertical = v_spread * (upward - 2.0 * middle + downward) / (z_spacing * z_spacing)
    reaction = coupling[:, 0].reshape(-1, 1, 1, 1) * middle[..., 0:1, :, :, :]
    reaction = reaction + coupling[:, 1].reshape(-1, 1, 1, 1) * middle[..., 1:2, :, :, :]
    return diffusion + vertical - advection + reaction


def pair_sum(field):
    row = lax.broadcasted_iota(jnp.int32, field.shape, field.ndim - 2)
    partner = jnp.where(
        row % 2 == 0, jnp.roll(field, -1, axis=-2), jnp.roll(field, 1, axis=-2)
    )
    return field + partner


def shrink(field):
    levels = field[..., 0::2, :, :] + field[..., 1::2, :, :]
    return pair_sum(levels) * 0.25


def expand(field):
    return jnp.repeat(field, 2, axis=-3)


def expand_z(field):
    return jnp.repeat(field, 2, axis=-3)


def pick(items, index):
    out = items[0]
    for k in range(1, len(items)):
        out = jax.tree.map(lambda new, old: jnp.where(index == k, new, old), items[k], out)
    return out


def pair_map(fn, *pairs):
    return tuple(fn(*parts) for parts in zip(*pairs))


def body(initial, x_velocity, y_velocity, h_diffusion, v_diffusion, coupling):
    coarse_x = shrink(x_velocity)
    coarse_y = shrink(y_velocity)
    coarse_h = shrink(h_diffusion)
    coarse_v = shrink(v_diffusion)
    slabs = lax.axis_size("tm")
    columns = lax.axis_size("space")
    slab = lax.axis_index("tm")
    first = slab == 0

    def fine_rate(field, halo):
        return tendency(
            field, halo, x_velocity, y_velocity, h_diffusion, v_diffusion, coupling, 1.0, 1.0
        )

    def coarse_rate(field, halo):
        return tendency(field, halo, coarse_x, coarse_y, coarse_h, coarse_v, coupling, 2.0, 2.0)

    def first_node(node_zero, rate_zero, s0, s1, s2):
        return (
            node_zero
            + half_step * (rate_zero - s0)
            + slab_step * (s0 * (5.0 / 24.0) + s1 * (1.0 / 3.0) - s2 * (1.0 / 24.0))
        )

    def second_node(node_one, rate_one, s0, s1, s2):
        return (
            node_one
            + half_step * (rate_one - s1)
            + slab_step * (s0 * (-1.0 / 24.0) + s1 * (1.0 / 3.0) + s2 * (5.0 / 24.0))
        )

    coarse_first = shrink(initial)
    (init_b, first_b), (init_a, first_a) = exchange(
        (hi(initial), hi(coarse_first)), (lo(initial), lo(coarse_first))
    )
    halo_zero = (init_b, init_a)
    halo_first = (first_b, first_a)
    first_rate = fine_rate(initial, halo_zero)
    coarse_first_rate = coarse_rate(coarse_first, halo_first)

    node_zero = initial
    rate_zero = first_rate
    node_one = first_node(node_zero, rate_zero, first_rate, first_rate, first_rate)
    halo_one = halo_of(node_one)
    rate_one = fine_rate(node_one, halo_one)
    node_two = second_node(node_one, rate_one, first_rate, first_rate, first_rate)
    two_b, two_a = exchange(hi(node_two, 2), lo(node_two, 2))
    halo_two = (hi(two_b), lo(two_a))
    coarse_end = shrink(node_two)
    halo_end = (hi(shrink(two_b)), lo(shrink(two_a)))
    rate_two = fine_rate(node_two, halo_two)
    source = shrink(slab_step * (rate_zero + 4.0 * rate_one + rate_two) / 6.0)
    offset = source - slab_step * coarse_first_rate

    chain = [coarse_first]
    chain_halo = [halo_first]
    rate = coarse_first_rate
    for count in range(slabs):
        after = chain[-1] + slab_step * rate + offset
        after_halo = halo_of(after)
        chain.append(after)
        chain_halo.append(after_halo)
        if count + 1 < slabs:
            rate = coarse_rate(after, after_halo)
    begins = pick(chain, slab)
    finals = pick(chain, slab + 1)
    begins_halo = pick(chain_halo, slab)
    finals_halo = pick(chain_halo, slab + 1)

    delta_zero = begins - coarse_first
    delta_one = finals - coarse_end
    fixed_zero = node_zero + expand(delta_zero)
    fixed_one = node_one + expand((delta_zero + delta_one) * 0.5)
    fixed_two = node_two + expand(delta_one)
    halo_dz = pair_map(lambda y, v: y - v, begins_halo, halo_first)
    halo_d1 = pair_map(lambda y, v: y - v, finals_halo, halo_end)
    halo_f0 = pair_map(lambda w, d: w + expand_z(d), halo_zero, halo_dz)
    halo_f1 = pair_map(
        lambda w, d0, d1: w + expand_z((d0 + d1) * 0.5), halo_one, halo_dz, halo_d1
    )
    halo_f2 = pair_map(lambda w, d: w + expand_z(d), halo_two, halo_d1)

    earlier_delta = begins - coarse_end
    earlier_end = node_two + expand(earlier_delta)
    halo_earlier_delta = pair_map(lambda y, v: y - v, begins_halo, halo_end)
    halo_earlier = pair_map(lambda w, d: w + expand_z(d), halo_two, halo_earlier_delta)
    wide_earlier = (
        two_b + expand(halo_earlier_delta[0]),
        two_a + expand(halo_earlier_delta[1]),
    )
    start = jnp.where(first, initial, earlier_end)
    halo_start = pair_map(lambda a, b: jnp.where(first, a, b), halo_zero, halo_earlier)
    halo_start_coarse = pair_map(
        lambda a, w: jnp.where(first, a, lo(shrink(w))), halo_first, wide_earlier
    )

    slope_zero = fine_rate(fixed_zero, halo_f0)
    slope_one = fine_rate(fixed_one, halo_f1)
    slope_two = fine_rate(fixed_two, halo_f2)
    node_zero = start
    rate_zero = fine_rate(node_zero, halo_start)
    node_one = first_node(node_zero, rate_zero, slope_zero, slope_one, slope_two)
    rate_one = fine_rate(node_one, halo_of(node_one))
    node_two = second_node(node_one, rate_one, slope_zero, slope_one, slope_two)
    rate_two = fine_rate(node_two, halo_of(node_two))
    coarse_zero = shrink(node_zero)
    coarse_end = shrink(node_two)
    source = shrink(slab_step * (rate_zero + 4.0 * rate_one + rate_two) / 6.0)
    offset = source - slab_step * coarse_rate(coarse_zero, halo_start_coarse)

    down = shift_pairs(slabs, 1)
    to_east = [
        (t * columns + c, (t + 1) * columns + c + 1)
        for t in range(slabs - 1)
        for c in range(columns - 1)
    ]
    to_west = [
        (t * columns + c, (t + 1) * columns + c - 1)
        for t in range(slabs - 1)
        for c in range(1, columns)
    ]
    carried = coarse_first
    carried_halo = halo_first
    rate = coarse_first_rate
    for count in range(slabs - 1):
        after = carried + slab_step * rate + offset
        passed = lax.ppermute(after, "tm", down)
        passed_b = lax.ppermute(hi(after), ("tm", "space"), to_east)
        passed_a = lax.ppermute(lo(after), ("tm", "space"), to_west)
        carried = jnp.where(first, coarse_first, passed)
        carried_halo = pair_map(
            lambda a, b: jnp.where(first, a, b), halo_first, (passed_b, passed_a)
        )
        rate = coarse_rate(carried, carried_halo)
    finals = carried + slab_step * rate + offset
    result = node_two + expand(finals - coarse_end)
    return result[None]


def solution(mesh):
    return jax.shard_map(
        body,
        mesh=mesh,
        in_specs=(
            P(None, None, "space", None),
            P(None, "space", None),
            P(None, "space", None),
            P(None, "space", None),
            P(None, "space", None),
            P(),
        ),
        out_specs=P("tm", None, None, "space", None),
        check_vma=False,
    )
```

```python
import functools

import jax
import jax.numpy as jnp
from jax import lax
from jax.experimental import pallas as pl
from jax.experimental.pallas import tpu as pltpu
from jax.sharding import PartitionSpec as P

ITERS = 2


slab_step = 0.5
half_step = 0.25


def shift_pairs(count, steps):
    return [(i, i + steps) for i in range(max(0, -steps), min(count, count - steps))]


def exchange(to_right, to_left):
    count = lax.axis_size("space")
    before = lax.ppermute(to_right, "space", shift_pairs(count, 1))
    after = lax.ppermute(to_left, "space", shift_pairs(count, -1))
    return before, after


def lo(field, width=1):
    return field[..., :width, :]


def hi(field, width=1):
    return field[..., field.shape[-2] - width:, :]


def halo_of(field):
    return exchange(hi(field), lo(field))


def tendency(field, halo, x_speed, y_speed, h_spread, v_spread, coupling, x_spacing, z_spacing):
    reach = int(x_spacing)
    padded = jnp.concatenate([halo[0]] * reach + [field] + [halo[1]] * reach, axis=-2)
    width = field.shape[-2]
    middle = field
    eastward = padded[..., 2 * reach:, :]
    westward = padded[..., :width, :]
    y_widths = [(0, 0)] * (middle.ndim - 1) + [(1, 1)]
    y_padded = jnp.pad(middle, y_widths)
    northward = y_padded[..., 2:]
    southward = y_padded[..., :-2]
    z_widths = [(0, 0)] * (middle.ndim - 3) + [(1, 1), (0, 0), (0, 0)]
    z_padded = jnp.pad(middle, z_widths)
    upward = z_padded[..., 2:, :, :]
    downward = z_padded[..., :-2, :, :]
    advection = (
        x_speed * (eastward - westward) / (2.0 * x_spacing)
        + y_speed * (northward - southward) * 0.5
    )
    diffusion = h_spread * (
        (eastward - 2.0 * middle + westward) / (x_spacing * x_spacing)
        + (northward - 2.0 * middle + southward)
    )
    vertical = v_spread * (upward - 2.0 * middle + downward) / (z_spacing * z_spacing)
    reaction = coupling[:, 0].reshape(-1, 1, 1, 1) * middle[..., 0:1, :, :, :]
    reaction = reaction + coupling[:, 1].reshape(-1, 1, 1, 1) * middle[..., 1:2, :, :, :]
    return diffusion + vertical - advection + reaction


def _tendency_kernel(k_ref, f_ref, hb_ref, ha_ref, a_ref, b_ref, kh_ref, kv_ref, o_ref, *, reach, spacing):
    levels, width, lanes = f_ref.shape[1], f_ref.shape[2], f_ref.shape[3]
    row = lax.broadcasted_iota(jnp.int32, (width, lanes), 0)
    col = lax.broadcasted_iota(jnp.int32, (width, lanes), 1)
    east_edge = row >= width - reach
    west_edge = row < reach
    north_edge = col == lanes - 1
    south_edge = col == 0
    half_inv = 1.0 / (2.0 * spacing)
    square_inv = 1.0 / (spacing * spacing)
    rates = [[k_ref[t, d] for d in range(2)] for t in range(2)]

    def level(z, carry):
        above = jnp.minimum(z + 1, levels - 1)
        below = jnp.maximum(z - 1, 0)
        has_above = z + 1 < levels
        has_below = z > 0
        a = a_ref[z]
        b = b_ref[z]
        kh = kh_ref[z]
        kv = kv_ref[z]
        cs = [f_ref[t, z] for t in range(2)]
        for t in range(2):
            c = cs[t]
            up = jnp.where(has_above, f_ref[t, above], 0.0)
            down = jnp.where(has_below, f_ref[t, below], 0.0)
            east = jnp.where(east_edge, ha_ref[t, z], pltpu.roll(c, width - reach, 0))
            west = jnp.where(west_edge, hb_ref[t, z], pltpu.roll(c, reach, 0))
            north = jnp.where(north_edge, 0.0, pltpu.roll(c, lanes - 1, 1))
            south = jnp.where(south_edge, 0.0, pltpu.roll(c, 1, 1))
            advection = a * (east - west) * half_inv + b * (north - south) * 0.5
            diffusion = kh * ((east - 2.0 * c + west) * square_inv + (north - 2.0 * c + south))
            vertical = kv * (up - 2.0 * c + down) * square_inv
            reaction = rates[t][0] * cs[0] + rates[t][1] * cs[1]
            o_ref[t, z] = diffusion + vertical - advection + reaction
        return carry

    lax.fori_loop(0, levels, level, 0)


def tendency_kernel(field, halo, a, b, kh, kv, coupling, spacing):
    reach = int(spacing)
    vmem = pl.BlockSpec(memory_space=pltpu.VMEM)
    return pl.pallas_call(
        functools.partial(_tendency_kernel, reach=reach, spacing=float(spacing)),
        out_shape=jax.ShapeDtypeStruct(field.shape, field.dtype),
        in_specs=[pl.BlockSpec(memory_space=pltpu.SMEM)] + [vmem] * 7,
        out_specs=vmem,
    )(coupling, field, halo[0], halo[1], a, b, kh, kv)


def pair_sum(field):
    row = lax.broadcasted_iota(jnp.int32, field.shape, field.ndim - 2)
    partner = jnp.where(
        row % 2 == 0, jnp.roll(field, -1, axis=-2), jnp.roll(field, 1, axis=-2)
    )
    return field + partner


def shrink(field):
    levels = field[..., 0::2, :, :] + field[..., 1::2, :, :]
    return pair_sum(levels) * 0.25


def expand(field):
    return jnp.repeat(field, 2, axis=-3)


def expand_z(field):
    return jnp.repeat(field, 2, axis=-3)


def pick(items, index):
    out = items[0]
    for k in range(1, len(items)):
        out = jax.tree.map(lambda new, old: jnp.where(index == k, new, old), items[k], out)
    return out


def pair_map(fn, *pairs):
    return tuple(fn(*parts) for parts in zip(*pairs))


def body(initial, x_velocity, y_velocity, h_diffusion, v_diffusion, coupling):
    coarse_x = shrink(x_velocity)
    coarse_y = shrink(y_velocity)
    coarse_h = shrink(h_diffusion)
    coarse_v = shrink(v_diffusion)
    slabs = lax.axis_size("tm")
    columns = lax.axis_size("space")
    slab = lax.axis_index("tm")
    first = slab == 0

    def fine_rate(field, halo):
        return tendency_kernel(
            field, halo, x_velocity, y_velocity, h_diffusion, v_diffusion, coupling, 1.0
        )

    def coarse_rate(field, halo):
        return tendency_kernel(field, halo, coarse_x, coarse_y, coarse_h, coarse_v, coupling, 2.0)

    def first_node(node_zero, rate_zero, s0, s1, s2):
        return (
            node_zero
            + half_step * (rate_zero - s0)
            + slab_step * (s0 * (5.0 / 24.0) + s1 * (1.0 / 3.0) - s2 * (1.0 / 24.0))
        )

    def second_node(node_one, rate_one, s0, s1, s2):
        return (
            node_one
            + half_step * (rate_one - s1)
            + slab_step * (s0 * (-1.0 / 24.0) + s1 * (1.0 / 3.0) + s2 * (5.0 / 24.0))
        )

    coarse_first = shrink(initial)
    (init_b, first_b), (init_a, first_a) = exchange(
        (hi(initial), hi(coarse_first)), (lo(initial), lo(coarse_first))
    )
    halo_zero = (init_b, init_a)
    halo_first = (first_b, first_a)
    first_rate = fine_rate(initial, halo_zero)
    coarse_first_rate = coarse_rate(coarse_first, halo_first)

    node_zero = initial
    rate_zero = first_rate
    node_one = first_node(node_zero, rate_zero, first_rate, first_rate, first_rate)
    halo_one = halo_of(node_one)
    rate_one = fine_rate(node_one, halo_one)
    node_two = second_node(node_one, rate_one, first_rate, first_rate, first_rate)
    two_b, two_a = exchange(hi(node_two, 2), lo(node_two, 2))
    halo_two = (hi(two_b), lo(two_a))
    coarse_end = shrink(node_two)
    halo_end = (hi(shrink(two_b)), lo(shrink(two_a)))
    rate_two = fine_rate(node_two, halo_two)
    source = shrink(slab_step * (rate_zero + 4.0 * rate_one + rate_two) / 6.0)
    offset = source - slab_step * coarse_first_rate

    chain = [coarse_first]
    chain_halo = [halo_first]
    rate = coarse_first_rate
    for count in range(slabs):
        after = chain[-1] + slab_step * rate + offset
        after_halo = halo_of(after)
        chain.append(after)
        chain_halo.append(after_halo)
        if count + 1 < slabs:
            rate = coarse_rate(after, after_halo)
    begins = pick(chain, slab)
    finals = pick(chain, slab + 1)
    begins_halo = pick(chain_halo, slab)
    finals_halo = pick(chain_halo, slab + 1)

    delta_zero = begins - coarse_first
    delta_one = finals - coarse_end
    fixed_zero = node_zero + expand(delta_zero)
    fixed_one = node_one + expand((delta_zero + delta_one) * 0.5)
    fixed_two = node_two + expand(delta_one)
    halo_dz = pair_map(lambda y, v: y - v, begins_halo, halo_first)
    halo_d1 = pair_map(lambda y, v: y - v, finals_halo, halo_end)
    halo_f0 = pair_map(lambda w, d: w + expand_z(d), halo_zero, halo_dz)
    halo_f1 = pair_map(
        lambda w, d0, d1: w + expand_z((d0 + d1) * 0.5), halo_one, halo_dz, halo_d1
    )
    halo_f2 = pair_map(lambda w, d: w + expand_z(d), halo_two, halo_d1)

    earlier_delta = begins - coarse_end
    earlier_end = node_two + expand(earlier_delta)
    halo_earlier_delta = pair_map(lambda y, v: y - v, begins_halo, halo_end)
    halo_earlier = pair_map(lambda w, d: w + expand_z(d), halo_two, halo_earlier_delta)
    wide_earlier = (
        two_b + expand(halo_earlier_delta[0]),
        two_a + expand(halo_earlier_delta[1]),
    )
    start = jnp.where(first, initial, earlier_end)
    halo_start = pair_map(lambda a, b: jnp.where(first, a, b), halo_zero, halo_earlier)
    halo_start_coarse = pair_map(
        lambda a, w: jnp.where(first, a, lo(shrink(w))), halo_first, wide_earlier
    )

    slope_zero = fine_rate(fixed_zero, halo_f0)
    slope_one = fine_rate(fixed_one, halo_f1)
    slope_two = fine_rate(fixed_two, halo_f2)
    node_zero = start
    rate_zero = fine_rate(node_zero, halo_start)
    node_one = first_node(node_zero, rate_zero, slope_zero, slope_one, slope_two)
    rate_one = fine_rate(node_one, halo_of(node_one))
    node_two = second_node(node_one, rate_one, slope_zero, slope_one, slope_two)
    rate_two = fine_rate(node_two, halo_of(node_two))
    coarse_zero = shrink(node_zero)
    coarse_end = shrink(node_two)
    source = shrink(slab_step * (rate_zero + 4.0 * rate_one + rate_two) / 6.0)
    offset = source - slab_step * coarse_rate(coarse_zero, halo_start_coarse)

    down = shift_pairs(slabs, 1)
    to_east = [
        (t * columns + c, (t + 1) * columns + c + 1)
        for t in range(slabs - 1)
        for c in range(columns - 1)
    ]
    to_west = [
        (t * columns + c, (t + 1) * columns + c - 1)
        for t in range(slabs - 1)
        for c in range(1, columns)
    ]
    carried = coarse_first
    carried_halo = halo_first
    rate = coarse_first_rate
    for count in range(slabs - 1):
        after = carried + slab_step * rate + offset
        passed = lax.ppermute(after, "tm", down)
        passed_b = lax.ppermute(hi(after), ("tm", "space"), to_east)
        passed_a = lax.ppermute(lo(after), ("tm", "space"), to_west)
        carried = jnp.where(first, coarse_first, passed)
        carried_halo = pair_map(
            lambda a, b: jnp.where(first, a, b), halo_first, (passed_b, passed_a)
        )
        rate = coarse_rate(carried, carried_halo)
    finals = carried + slab_step * rate + offset
    result = node_two + expand(finals - coarse_end)
    return result[None]


def solution(mesh):
    return jax.shard_map(
        body,
        mesh=mesh,
        in_specs=(
            P(None, None, "space", None),
            P(None, "space", None),
            P(None, "space", None),
            P(None, "space", None),
            P(None, "space", None),
            P(),
        ),
        out_specs=P("tm", None, None, "space", None),
        check_vma=False,
    )
```

```python
import functools

import jax
import jax.numpy as jnp
from jax import lax
from jax.experimental import pallas as pl
from jax.experimental.pallas import tpu as pltpu
from jax.sharding import PartitionSpec as P

ITERS = 2


slab_step = 0.5
half_step = 0.25


def shift_pairs(count, steps):
    return [(i, i + steps) for i in range(max(0, -steps), min(count, count - steps))]


def exchange(to_right, to_left):
    count = lax.axis_size("space")
    before = lax.ppermute(to_right, "space", shift_pairs(count, 1))
    after = lax.ppermute(to_left, "space", shift_pairs(count, -1))
    return before, after


def lo(field, width=1):
    return field[..., :width, :]


def hi(field, width=1):
    return field[..., field.shape[-2] - width:, :]


def halo_of(field):
    return exchange(hi(field), lo(field))


def tendency(field, halo, x_speed, y_speed, h_spread, v_spread, coupling, x_spacing, z_spacing):
    reach = int(x_spacing)
    padded = jnp.concatenate([halo[0]] * reach + [field] + [halo[1]] * reach, axis=-2)
    width = field.shape[-2]
    middle = field
    eastward = padded[..., 2 * reach:, :]
    westward = padded[..., :width, :]
    y_widths = [(0, 0)] * (middle.ndim - 1) + [(1, 1)]
    y_padded = jnp.pad(middle, y_widths)
    northward = y_padded[..., 2:]
    southward = y_padded[..., :-2]
    z_widths = [(0, 0)] * (middle.ndim - 3) + [(1, 1), (0, 0), (0, 0)]
    z_padded = jnp.pad(middle, z_widths)
    upward = z_padded[..., 2:, :, :]
    downward = z_padded[..., :-2, :, :]
    advection = (
        x_speed * (eastward - westward) / (2.0 * x_spacing)
        + y_speed * (northward - southward) * 0.5
    )
    diffusion = h_spread * (
        (eastward - 2.0 * middle + westward) / (x_spacing * x_spacing)
        + (northward - 2.0 * middle + southward)
    )
    vertical = v_spread * (upward - 2.0 * middle + downward) / (z_spacing * z_spacing)
    reaction = coupling[:, 0].reshape(-1, 1, 1, 1) * middle[..., 0:1, :, :, :]
    reaction = reaction + coupling[:, 1].reshape(-1, 1, 1, 1) * middle[..., 1:2, :, :, :]
    return diffusion + vertical - advection + reaction


def _tendency_kernel(
    k_ref, f_ref, below_ref, above_ref, hb_ref, ha_ref, a_ref, b_ref, kh_ref, kv_ref, o_ref,
    *, reach, spacing
):
    block, width, lanes = f_ref.shape[1], f_ref.shape[2], f_ref.shape[3]
    step = pl.program_id(0)
    has_below = step > 0
    has_above = step < pl.num_programs(0) - 1
    row = lax.broadcasted_iota(jnp.int32, (width, lanes), 0)
    col = lax.broadcasted_iota(jnp.int32, (width, lanes), 1)
    east_edge = row >= width - reach
    west_edge = row < reach
    north_edge = col == lanes - 1
    south_edge = col == 0
    half_inv = 1.0 / (2.0 * spacing)
    square_inv = 1.0 / (spacing * spacing)
    rates = [[k_ref[t, d] for d in range(2)] for t in range(2)]
    for z in range(block):
        a = a_ref[z]
        b = b_ref[z]
        kh = kh_ref[z]
        kv = kv_ref[z]
        cs = [f_ref[t, z] for t in range(2)]
        for t in range(2):
            c = cs[t]
            if z + 1 < block:
                up = f_ref[t, z + 1]
            else:
                up = jnp.where(has_above, above_ref[t, 0], 0.0)
            if z > 0:
                down = f_ref[t, z - 1]
            else:
                down = jnp.where(has_below, below_ref[t, 0], 0.0)
            east = jnp.where(east_edge, ha_ref[t, z], pltpu.roll(c, width - reach, 0))
            west = jnp.where(west_edge, hb_ref[t, z], pltpu.roll(c, reach, 0))
            north = jnp.where(north_edge, 0.0, pltpu.roll(c, lanes - 1, 1))
            south = jnp.where(south_edge, 0.0, pltpu.roll(c, 1, 1))
            advection = a * (east - west) * half_inv + b * (north - south) * 0.5
            diffusion = kh * ((east - 2.0 * c + west) * square_inv + (north - 2.0 * c + south))
            vertical = kv * (up - 2.0 * c + down) * square_inv
            reaction = rates[t][0] * cs[0] + rates[t][1] * cs[1]
            o_ref[t, z] = diffusion + vertical - advection + reaction


def tendency_kernel(field, halo, a, b, kh, kv, coupling, spacing):
    tracers, levels, width, lanes = field.shape
    block = min(16, levels)
    steps = levels // block
    whole = pl.BlockSpec((tracers, block, width, lanes), lambda i: (0, i, 0, 0))
    below = pl.BlockSpec(
        (tracers, 1, width, lanes), lambda i: (0, jnp.maximum(i * block - 1, 0), 0, 0)
    )
    above = pl.BlockSpec(
        (tracers, 1, width, lanes),
        lambda i: (0, jnp.minimum((i + 1) * block, levels - 1), 0, 0),
    )
    side = pl.BlockSpec((tracers, block, 1, lanes), lambda i: (0, i, 0, 0))
    grid_of = pl.BlockSpec((block, width, lanes), lambda i: (i, 0, 0))
    return pl.pallas_call(
        functools.partial(_tendency_kernel, reach=int(spacing), spacing=float(spacing)),
        out_shape=jax.ShapeDtypeStruct(field.shape, field.dtype),
        grid=(steps,),
        in_specs=[pl.BlockSpec(memory_space=pltpu.SMEM), whole, below, above, side, side]
        + [grid_of] * 4,
        out_specs=whole,
    )(coupling, field, field, field, halo[0], halo[1], a, b, kh, kv)


def pair_sum(field):
    row = lax.broadcasted_iota(jnp.int32, field.shape, field.ndim - 2)
    partner = jnp.where(
        row % 2 == 0, jnp.roll(field, -1, axis=-2), jnp.roll(field, 1, axis=-2)
    )
    return field + partner


def shrink(field):
    levels = field[..., 0::2, :, :] + field[..., 1::2, :, :]
    return pair_sum(levels) * 0.25


def expand(field):
    return jnp.repeat(field, 2, axis=-3)


def expand_z(field):
    return jnp.repeat(field, 2, axis=-3)


def pick(items, index):
    out = items[0]
    for k in range(1, len(items)):
        out = jax.tree.map(lambda new, old: jnp.where(index == k, new, old), items[k], out)
    return out


def pair_map(fn, *pairs):
    return tuple(fn(*parts) for parts in zip(*pairs))


def body(initial, x_velocity, y_velocity, h_diffusion, v_diffusion, coupling):
    coarse_x = shrink(x_velocity)
    coarse_y = shrink(y_velocity)
    coarse_h = shrink(h_diffusion)
    coarse_v = shrink(v_diffusion)
    slabs = lax.axis_size("tm")
    columns = lax.axis_size("space")
    slab = lax.axis_index("tm")
    first = slab == 0

    def fine_rate(field, halo):
        return tendency_kernel(
            field, halo, x_velocity, y_velocity, h_diffusion, v_diffusion, coupling, 1.0
        )

    def coarse_rate(field, halo):
        return tendency_kernel(field, halo, coarse_x, coarse_y, coarse_h, coarse_v, coupling, 2.0)

    def first_node(node_zero, rate_zero, s0, s1, s2):
        return (
            node_zero
            + half_step * (rate_zero - s0)
            + slab_step * (s0 * (5.0 / 24.0) + s1 * (1.0 / 3.0) - s2 * (1.0 / 24.0))
        )

    def second_node(node_one, rate_one, s0, s1, s2):
        return (
            node_one
            + half_step * (rate_one - s1)
            + slab_step * (s0 * (-1.0 / 24.0) + s1 * (1.0 / 3.0) + s2 * (5.0 / 24.0))
        )

    coarse_first = shrink(initial)
    (init_b, first_b), (init_a, first_a) = exchange(
        (hi(initial), hi(coarse_first)), (lo(initial), lo(coarse_first))
    )
    halo_zero = (init_b, init_a)
    halo_first = (first_b, first_a)
    first_rate = fine_rate(initial, halo_zero)
    coarse_first_rate = coarse_rate(coarse_first, halo_first)

    node_zero = initial
    rate_zero = first_rate
    node_one = first_node(node_zero, rate_zero, first_rate, first_rate, first_rate)
    halo_one = halo_of(node_one)
    rate_one = fine_rate(node_one, halo_one)
    node_two = second_node(node_one, rate_one, first_rate, first_rate, first_rate)
    two_b, two_a = exchange(hi(node_two, 2), lo(node_two, 2))
    halo_two = (hi(two_b), lo(two_a))
    coarse_end = shrink(node_two)
    halo_end = (hi(shrink(two_b)), lo(shrink(two_a)))
    rate_two = fine_rate(node_two, halo_two)
    source = shrink(slab_step * (rate_zero + 4.0 * rate_one + rate_two) / 6.0)
    offset = source - slab_step * coarse_first_rate

    chain = [coarse_first]
    chain_halo = [halo_first]
    rate = coarse_first_rate
    for count in range(slabs):
        after = chain[-1] + slab_step * rate + offset
        after_halo = halo_of(after)
        chain.append(after)
        chain_halo.append(after_halo)
        if count + 1 < slabs:
            rate = coarse_rate(after, after_halo)
    begins = pick(chain, slab)
    finals = pick(chain, slab + 1)
    begins_halo = pick(chain_halo, slab)
    finals_halo = pick(chain_halo, slab + 1)

    delta_zero = begins - coarse_first
    delta_one = finals - coarse_end
    fixed_zero = node_zero + expand(delta_zero)
    fixed_one = node_one + expand((delta_zero + delta_one) * 0.5)
    fixed_two = node_two + expand(delta_one)
    halo_dz = pair_map(lambda y, v: y - v, begins_halo, halo_first)
    halo_d1 = pair_map(lambda y, v: y - v, finals_halo, halo_end)
    halo_f0 = pair_map(lambda w, d: w + expand_z(d), halo_zero, halo_dz)
    halo_f1 = pair_map(
        lambda w, d0, d1: w + expand_z((d0 + d1) * 0.5), halo_one, halo_dz, halo_d1
    )
    halo_f2 = pair_map(lambda w, d: w + expand_z(d), halo_two, halo_d1)

    earlier_delta = begins - coarse_end
    earlier_end = node_two + expand(earlier_delta)
    halo_earlier_delta = pair_map(lambda y, v: y - v, begins_halo, halo_end)
    halo_earlier = pair_map(lambda w, d: w + expand_z(d), halo_two, halo_earlier_delta)
    wide_earlier = (
        two_b + expand(halo_earlier_delta[0]),
        two_a + expand(halo_earlier_delta[1]),
    )
    start = jnp.where(first, initial, earlier_end)
    halo_start = pair_map(lambda a, b: jnp.where(first, a, b), halo_zero, halo_earlier)
    halo_start_coarse = pair_map(
        lambda a, w: jnp.where(first, a, lo(shrink(w))), halo_first, wide_earlier
    )

    slope_zero = fine_rate(fixed_zero, halo_f0)
    slope_one = fine_rate(fixed_one, halo_f1)
    slope_two = fine_rate(fixed_two, halo_f2)
    node_zero = start
    rate_zero = fine_rate(node_zero, halo_start)
    node_one = first_node(node_zero, rate_zero, slope_zero, slope_one, slope_two)
    rate_one = fine_rate(node_one, halo_of(node_one))
    node_two = second_node(node_one, rate_one, slope_zero, slope_one, slope_two)
    rate_two = fine_rate(node_two, halo_of(node_two))
    coarse_zero = shrink(node_zero)
    coarse_end = shrink(node_two)
    source = shrink(slab_step * (rate_zero + 4.0 * rate_one + rate_two) / 6.0)
    offset = source - slab_step * coarse_rate(coarse_zero, halo_start_coarse)

    down = shift_pairs(slabs, 1)
    to_east = [
        (t * columns + c, (t + 1) * columns + c + 1)
        for t in range(slabs - 1)
        for c in range(columns - 1)
    ]
    to_west = [
        (t * columns + c, (t + 1) * columns + c - 1)
        for t in range(slabs - 1)
        for c in range(1, columns)
    ]
    carried = coarse_first
    carried_halo = halo_first
    rate = coarse_first_rate
    for count in range(slabs - 1):
        after = carried + slab_step * rate + offset
        passed = lax.ppermute(after, "tm", down)
        passed_b = lax.ppermute(hi(after), ("tm", "space"), to_east)
        passed_a = lax.ppermute(lo(after), ("tm", "space"), to_west)
        carried = jnp.where(first, coarse_first, passed)
        carried_halo = pair_map(
            lambda a, b: jnp.where(first, a, b), halo_first, (passed_b, passed_a)
        )
        rate = coarse_rate(carried, carried_halo)
    finals = carried + slab_step * rate + offset
    result = node_two + expand(finals - coarse_end)
    return result[None]


def solution(mesh):
    return jax.shard_map(
        body,
        mesh=mesh,
        in_specs=(
            P(None, None, "space", None),
            P(None, "space", None),
            P(None, "space", None),
            P(None, "space", None),
            P(None, "space", None),
            P(),
        ),
        out_specs=P("tm", None, None, "space", None),
        check_vma=False,
    )
```

```python
import jax
import jax.numpy as jnp
from jax import lax
from jax.sharding import PartitionSpec as P

ITERS = 2


slab_step = 0.5
half_step = 0.25


def shift_pairs(count, steps):
    return [(i, i + steps) for i in range(max(0, -steps), min(count, count - steps))]


def exchange(to_right, to_left):
    count = lax.axis_size("space")
    before = lax.ppermute(to_right, "space", shift_pairs(count, 1))
    after = lax.ppermute(to_left, "space", shift_pairs(count, -1))
    return before, after


def lo(field, width=None):
    if width is None:
        return field[..., 0, :]
    return field[..., :width, :]


def hi(field, width=None):
    if width is None:
        return field[..., field.shape[-2] - 1, :]
    return field[..., field.shape[-2] - width:, :]


def across(column, shape):
    dims = tuple(range(len(shape) - 2)) + (len(shape) - 1,)
    return lax.broadcast_in_dim(column, shape, dims)


def halo_of(field):
    return exchange(hi(field), lo(field))


def tendency(field, halo, x_speed, y_speed, h_spread, v_spread, coupling, x_spacing, z_spacing):
    reach = int(x_spacing)
    width = field.shape[-2]
    row = lax.broadcasted_iota(jnp.int32, field.shape, field.ndim - 2)
    middle = field
    eastward = jnp.where(
        row >= width - reach, across(halo[1], field.shape), jnp.roll(field, -reach, axis=-2)
    )
    westward = jnp.where(
        row < reach, across(halo[0], field.shape), jnp.roll(field, reach, axis=-2)
    )
    y_widths = [(0, 0)] * (middle.ndim - 1) + [(1, 1)]
    y_padded = jnp.pad(middle, y_widths)
    northward = y_padded[..., 2:]
    southward = y_padded[..., :-2]
    z_widths = [(0, 0)] * (middle.ndim - 3) + [(1, 1), (0, 0), (0, 0)]
    z_padded = jnp.pad(middle, z_widths)
    upward = z_padded[..., 2:, :, :]
    downward = z_padded[..., :-2, :, :]
    advection = (
        x_speed * (eastward - westward) / (2.0 * x_spacing)
        + y_speed * (northward - southward) * 0.5
    )
    diffusion = h_spread * (
        (eastward - 2.0 * middle + westward) / (x_spacing * x_spacing)
        + (northward - 2.0 * middle + southward)
    )
    vertical = v_spread * (upward - 2.0 * middle + downward) / (z_spacing * z_spacing)
    reaction = coupling[:, 0].reshape(-1, 1, 1, 1) * middle[..., 0:1, :, :, :]
    reaction = reaction + coupling[:, 1].reshape(-1, 1, 1, 1) * middle[..., 1:2, :, :, :]
    return diffusion + vertical - advection + reaction


def pair_sum(field):
    row = lax.broadcasted_iota(jnp.int32, field.shape, field.ndim - 2)
    partner = jnp.where(
        row % 2 == 0, jnp.roll(field, -1, axis=-2), jnp.roll(field, 1, axis=-2)
    )
    return field + partner


def shrink(field):
    levels = field[..., 0::2, :, :] + field[..., 1::2, :, :]
    return pair_sum(levels) * 0.25


def expand(field):
    return jnp.repeat(field, 2, axis=-3)


def expand_z(column):
    return jnp.repeat(column, 2, axis=-2)


def pick(items, index):
    out = items[0]
    for k in range(1, len(items)):
        out = jax.tree.map(lambda new, old: jnp.where(index == k, new, old), items[k], out)
    return out


def pair_map(fn, *pairs):
    return tuple(fn(*parts) for parts in zip(*pairs))


def body(initial, x_velocity, y_velocity, h_diffusion, v_diffusion, coupling):
    coarse_x = shrink(x_velocity)
    coarse_y = shrink(y_velocity)
    coarse_h = shrink(h_diffusion)
    coarse_v = shrink(v_diffusion)
    slabs = lax.axis_size("tm")
    columns = lax.axis_size("space")
    slab = lax.axis_index("tm")
    first = slab == 0

    def fine_rate(field, halo):
        return tendency(
            field, halo, x_velocity, y_velocity, h_diffusion, v_diffusion, coupling, 1.0, 1.0
        )

    def coarse_rate(field, halo):
        return tendency(field, halo, coarse_x, coarse_y, coarse_h, coarse_v, coupling, 2.0, 2.0)

    def first_node(node_zero, rate_zero, s0, s1, s2):
        return (
            node_zero
            + half_step * (rate_zero - s0)
            + slab_step * (s0 * (5.0 / 24.0) + s1 * (1.0 / 3.0) - s2 * (1.0 / 24.0))
        )

    def second_node(node_one, rate_one, s0, s1, s2):
        return (
            node_one
            + half_step * (rate_one - s1)
            + slab_step * (s0 * (-1.0 / 24.0) + s1 * (1.0 / 3.0) + s2 * (5.0 / 24.0))
        )

    coarse_first = shrink(initial)
    (init_b, first_b), (init_a, first_a) = exchange(
        (hi(initial), hi(coarse_first)), (lo(initial), lo(coarse_first))
    )
    halo_zero = (init_b, init_a)
    halo_first = (first_b, first_a)
    first_rate = fine_rate(initial, halo_zero)
    coarse_first_rate = coarse_rate(coarse_first, halo_first)

    node_zero = initial
    rate_zero = first_rate
    node_one = first_node(node_zero, rate_zero, first_rate, first_rate, first_rate)
    halo_one = halo_of(node_one)
    rate_one = fine_rate(node_one, halo_one)
    node_two = second_node(node_one, rate_one, first_rate, first_rate, first_rate)
    two_b, two_a = exchange(hi(node_two, 2), lo(node_two, 2))
    halo_two = (hi(two_b), lo(two_a))
    coarse_end = shrink(node_two)
    halo_end = (hi(shrink(two_b)), lo(shrink(two_a)))
    rate_two = fine_rate(node_two, halo_two)
    source = shrink(slab_step * (rate_zero + 4.0 * rate_one + rate_two) / 6.0)
    offset = source - slab_step * coarse_first_rate

    chain = [coarse_first]
    chain_halo = [halo_first]
    rate = coarse_first_rate
    for count in range(slabs):
        after = chain[-1] + slab_step * rate + offset
        after_halo = halo_of(after)
        chain.append(after)
        chain_halo.append(after_halo)
        if count + 1 < slabs:
            rate = coarse_rate(after, after_halo)
    begins = pick(chain, slab)
    finals = pick(chain, slab + 1)
    begins_halo = pick(chain_halo, slab)
    finals_halo = pick(chain_halo, slab + 1)

    delta_zero = begins - coarse_first
    delta_one = finals - coarse_end
    fixed_zero = node_zero + expand(delta_zero)
    fixed_one = node_one + expand((delta_zero + delta_one) * 0.5)
    fixed_two = node_two + expand(delta_one)
    halo_dz = pair_map(lambda y, v: y - v, begins_halo, halo_first)
    halo_d1 = pair_map(lambda y, v: y - v, finals_halo, halo_end)
    halo_f0 = pair_map(lambda w, d: w + expand_z(d), halo_zero, halo_dz)
    halo_f1 = pair_map(
        lambda w, d0, d1: w + expand_z((d0 + d1) * 0.5), halo_one, halo_dz, halo_d1
    )
    halo_f2 = pair_map(lambda w, d: w + expand_z(d), halo_two, halo_d1)

    earlier_delta = begins - coarse_end
    earlier_end = node_two + expand(earlier_delta)
    halo_earlier_delta = pair_map(lambda y, v: y - v, begins_halo, halo_end)
    halo_earlier = pair_map(lambda w, d: w + expand_z(d), halo_two, halo_earlier_delta)
    wide_earlier = (
        two_b + across(expand_z(halo_earlier_delta[0]), two_b.shape),
        two_a + across(expand_z(halo_earlier_delta[1]), two_a.shape),
    )
    start = jnp.where(first, initial, earlier_end)
    halo_start = pair_map(lambda a, b: jnp.where(first, a, b), halo_zero, halo_earlier)
    halo_start_coarse = pair_map(
        lambda a, w: jnp.where(first, a, lo(shrink(w))), halo_first, wide_earlier
    )

    slope_zero = fine_rate(fixed_zero, halo_f0)
    slope_one = fine_rate(fixed_one, halo_f1)
    slope_two = fine_rate(fixed_two, halo_f2)
    node_zero = start
    rate_zero = fine_rate(node_zero, halo_start)
    node_one = first_node(node_zero, rate_zero, slope_zero, slope_one, slope_two)
    rate_one = fine_rate(node_one, halo_of(node_one))
    node_two = second_node(node_one, rate_one, slope_zero, slope_one, slope_two)
    rate_two = fine_rate(node_two, halo_of(node_two))
    coarse_zero = shrink(node_zero)
    coarse_end = shrink(node_two)
    source = shrink(slab_step * (rate_zero + 4.0 * rate_one + rate_two) / 6.0)
    offset = source - slab_step * coarse_rate(coarse_zero, halo_start_coarse)

    down = shift_pairs(slabs, 1)
    to_east = [
        (t * columns + c, (t + 1) * columns + c + 1)
        for t in range(slabs - 1)
        for c in range(columns - 1)
    ]
    to_west = [
        (t * columns + c, (t + 1) * columns + c - 1)
        for t in range(slabs - 1)
        for c in range(1, columns)
    ]
    carried = coarse_first
    carried_halo = halo_first
    rate = coarse_first_rate
    for count in range(slabs - 1):
        after = carried + slab_step * rate + offset
        passed = lax.ppermute(after, "tm", down)
        passed_b = lax.ppermute(hi(after), ("tm", "space"), to_east)
        passed_a = lax.ppermute(lo(after), ("tm", "space"), to_west)
        carried = jnp.where(first, coarse_first, passed)
        carried_halo = pair_map(
            lambda a, b: jnp.where(first, a, b), halo_first, (passed_b, passed_a)
        )
        rate = coarse_rate(carried, carried_halo)
    finals = carried + slab_step * rate + offset
    result = node_two + expand(finals - coarse_end)
    return result[None]


def solution(mesh):
    return jax.shard_map(
        body,
        mesh=mesh,
        in_specs=(
            P(None, None, "space", None),
            P(None, "space", None),
            P(None, "space", None),
            P(None, "space", None),
            P(None, "space", None),
            P(),
        ),
        out_specs=P("tm", None, None, "space", None),
        check_vma=False,
    )
```

```python
import jax
import jax.numpy as jnp
from jax import lax
from jax.sharding import PartitionSpec as P

ITERS = 2


slab_step = 0.5
half_step = 0.25


def shift_pairs(count, steps):
    return [(i, i + steps) for i in range(max(0, -steps), min(count, count - steps))]


def exchange(to_right, to_left):
    count = lax.axis_size("space")
    before = lax.ppermute(to_right, "space", shift_pairs(count, 1))
    after = lax.ppermute(to_left, "space", shift_pairs(count, -1))
    return before, after


def lo(field, width=1):
    return field[..., :width, :, :]


def hi(field, width=1):
    return field[..., field.shape[-3] - width:, :, :]


def halo_of(field):
    return exchange(hi(field), lo(field))


def tendency(field, halo, x_speed, y_speed, h_spread, v_spread, coupling, x_spacing, z_spacing):
    reach = int(z_spacing)
    middle = field
    eastward = jnp.concatenate([field[..., 1:, :, :], halo[1]], axis=-3)
    westward = jnp.concatenate([halo[0], field[..., :-1, :, :]], axis=-3)
    y_widths = [(0, 0)] * (middle.ndim - 1) + [(1, 1)]
    y_padded = jnp.pad(middle, y_widths)
    northward = y_padded[..., 2:]
    southward = y_padded[..., :-2]
    z_widths = [(0, 0)] * (middle.ndim - 2) + [(reach, reach), (0, 0)]
    z_padded = jnp.pad(middle, z_widths)
    upward = z_padded[..., 2 * reach:, :]
    downward = z_padded[..., : middle.shape[-2], :]
    advection = (
        x_speed * (eastward - westward) / (2.0 * x_spacing)
        + y_speed * (northward - southward) * 0.5
    )
    diffusion = h_spread * (
        (eastward - 2.0 * middle + westward) / (x_spacing * x_spacing)
        + (northward - 2.0 * middle + southward)
    )
    vertical = v_spread * (upward - 2.0 * middle + downward) / (z_spacing * z_spacing)
    reaction = coupling[:, 0].reshape(-1, 1, 1, 1) * middle[..., 0:1, :, :, :]
    reaction = reaction + coupling[:, 1].reshape(-1, 1, 1, 1) * middle[..., 1:2, :, :, :]
    return diffusion + vertical - advection + reaction


def pair_sum(field):
    row = lax.broadcasted_iota(jnp.int32, field.shape, field.ndim - 2)
    partner = jnp.where(
        row % 2 == 0, jnp.roll(field, -1, axis=-2), jnp.roll(field, 1, axis=-2)
    )
    return field + partner


def shrink(field):
    columns = field[..., 0::2, :, :] + field[..., 1::2, :, :]
    return pair_sum(columns) * 0.25


def expand(field):
    return jnp.repeat(field, 2, axis=-3)


def expand_z(column):
    return column


def pick(items, index):
    out = items[0]
    for k in range(1, len(items)):
        out = jax.tree.map(lambda new, old: jnp.where(index == k, new, old), items[k], out)
    return out


def pair_map(fn, *pairs):
    return tuple(fn(*parts) for parts in zip(*pairs))


def body(initial, x_velocity, y_velocity, h_diffusion, v_diffusion, coupling):
    initial = jnp.swapaxes(initial, -3, -2)
    x_velocity = jnp.swapaxes(x_velocity, -3, -2)
    y_velocity = jnp.swapaxes(y_velocity, -3, -2)
    h_diffusion = jnp.swapaxes(h_diffusion, -3, -2)
    v_diffusion = jnp.swapaxes(v_diffusion, -3, -2)
    coarse_x = shrink(x_velocity)
    coarse_y = shrink(y_velocity)
    coarse_h = shrink(h_diffusion)
    coarse_v = shrink(v_diffusion)
    slabs = lax.axis_size("tm")
    columns = lax.axis_size("space")
    slab = lax.axis_index("tm")
    first = slab == 0

    def fine_rate(field, halo):
        return tendency(
            field, halo, x_velocity, y_velocity, h_diffusion, v_diffusion, coupling, 1.0, 1.0
        )

    def coarse_rate(field, halo):
        return tendency(field, halo, coarse_x, coarse_y, coarse_h, coarse_v, coupling, 2.0, 2.0)

    def first_node(node_zero, rate_zero, s0, s1, s2):
        return (
            node_zero
            + half_step * (rate_zero - s0)
            + slab_step * (s0 * (5.0 / 24.0) + s1 * (1.0 / 3.0) - s2 * (1.0 / 24.0))
        )

    def second_node(node_one, rate_one, s0, s1, s2):
        return (
            node_one
            + half_step * (rate_one - s1)
            + slab_step * (s0 * (-1.0 / 24.0) + s1 * (1.0 / 3.0) + s2 * (5.0 / 24.0))
        )

    coarse_first = shrink(initial)
    (init_b, first_b), (init_a, first_a) = exchange(
        (hi(initial), hi(coarse_first)), (lo(initial), lo(coarse_first))
    )
    halo_zero = (init_b, init_a)
    halo_first = (first_b, first_a)
    first_rate = fine_rate(initial, halo_zero)
    coarse_first_rate = coarse_rate(coarse_first, halo_first)

    node_zero = initial
    rate_zero = first_rate
    node_one = first_node(node_zero, rate_zero, first_rate, first_rate, first_rate)
    halo_one = halo_of(node_one)
    rate_one = fine_rate(node_one, halo_one)
    node_two = second_node(node_one, rate_one, first_rate, first_rate, first_rate)
    two_b, two_a = exchange(hi(node_two, 2), lo(node_two, 2))
    halo_two = (hi(two_b), lo(two_a))
    coarse_end = shrink(node_two)
    halo_end = (shrink(two_b), shrink(two_a))
    rate_two = fine_rate(node_two, halo_two)
    source = shrink(slab_step * (rate_zero + 4.0 * rate_one + rate_two) / 6.0)
    offset = source - slab_step * coarse_first_rate

    chain = [coarse_first]
    chain_halo = [halo_first]
    rate = coarse_first_rate
    for count in range(slabs):
        after = chain[-1] + slab_step * rate + offset
        after_halo = halo_of(after)
        chain.append(after)
        chain_halo.append(after_halo)
        if count + 1 < slabs:
            rate = coarse_rate(after, after_halo)
    begins = pick(chain, slab)
    finals = pick(chain, slab + 1)
    begins_halo = pick(chain_halo, slab)
    finals_halo = pick(chain_halo, slab + 1)

    delta_zero = begins - coarse_first
    delta_one = finals - coarse_end
    fixed_zero = node_zero + expand(delta_zero)
    fixed_one = node_one + expand((delta_zero + delta_one) * 0.5)
    fixed_two = node_two + expand(delta_one)
    halo_dz = pair_map(lambda y, v: y - v, begins_halo, halo_first)
    halo_d1 = pair_map(lambda y, v: y - v, finals_halo, halo_end)
    halo_f0 = pair_map(lambda w, d: w + expand_z(d), halo_zero, halo_dz)
    halo_f1 = pair_map(
        lambda w, d0, d1: w + expand_z((d0 + d1) * 0.5), halo_one, halo_dz, halo_d1
    )
    halo_f2 = pair_map(lambda w, d: w + expand_z(d), halo_two, halo_d1)

    earlier_delta = begins - coarse_end
    earlier_end = node_two + expand(earlier_delta)
    halo_earlier_delta = pair_map(lambda y, v: y - v, begins_halo, halo_end)
    halo_earlier = pair_map(lambda w, d: w + expand_z(d), halo_two, halo_earlier_delta)
    wide_earlier = (
        two_b + expand(halo_earlier_delta[0]),
        two_a + expand(halo_earlier_delta[1]),
    )
    start = jnp.where(first, initial, earlier_end)
    halo_start = pair_map(lambda a, b: jnp.where(first, a, b), halo_zero, halo_earlier)
    halo_start_coarse = pair_map(
        lambda a, w: jnp.where(first, a, shrink(w)), halo_first, wide_earlier
    )

    slope_zero = fine_rate(fixed_zero, halo_f0)
    slope_one = fine_rate(fixed_one, halo_f1)
    slope_two = fine_rate(fixed_two, halo_f2)
    node_zero = start
    rate_zero = fine_rate(node_zero, halo_start)
    node_one = first_node(node_zero, rate_zero, slope_zero, slope_one, slope_two)
    rate_one = fine_rate(node_one, halo_of(node_one))
    node_two = second_node(node_one, rate_one, slope_zero, slope_one, slope_two)
    rate_two = fine_rate(node_two, halo_of(node_two))
    coarse_zero = shrink(node_zero)
    coarse_end = shrink(node_two)
    source = shrink(slab_step * (rate_zero + 4.0 * rate_one + rate_two) / 6.0)
    offset = source - slab_step * coarse_rate(coarse_zero, halo_start_coarse)

    down = shift_pairs(slabs, 1)
    to_east = [
        (t * columns + c, (t + 1) * columns + c + 1)
        for t in range(slabs - 1)
        for c in range(columns - 1)
    ]
    to_west = [
        (t * columns + c, (t + 1) * columns + c - 1)
        for t in range(slabs - 1)
        for c in range(1, columns)
    ]
    carried = coarse_first
    carried_halo = halo_first
    rate = coarse_first_rate
    for count in range(slabs - 1):
        after = carried + slab_step * rate + offset
        passed = lax.ppermute(after, "tm", down)
        passed_b = lax.ppermute(hi(after), ("tm", "space"), to_east)
        passed_a = lax.ppermute(lo(after), ("tm", "space"), to_west)
        carried = jnp.where(first, coarse_first, passed)
        carried_halo = pair_map(
            lambda a, b: jnp.where(first, a, b), halo_first, (passed_b, passed_a)
        )
        rate = coarse_rate(carried, carried_halo)
    finals = carried + slab_step * rate + offset
    result = node_two + expand(finals - coarse_end)
    return jnp.swapaxes(result, -3, -2)[None]


def solution(mesh):
    return jax.shard_map(
        body,
        mesh=mesh,
        in_specs=(
            P(None, None, "space", None),
            P(None, "space", None),
            P(None, "space", None),
            P(None, "space", None),
            P(None, "space", None),
            P(),
        ),
        out_specs=P("tm", None, None, "space", None),
        check_vma=False,
    )
```

```python
import jax
import jax.numpy as jnp
from jax import lax
from jax.sharding import PartitionSpec as P

ITERS = 2


slab_step = 0.5
half_step = 0.25


def shift_pairs(count, steps):
    return [(i, i + steps) for i in range(max(0, -steps), min(count, count - steps))]


def exchange(to_right, to_left):
    count = lax.axis_size("space")
    before = lax.ppermute(to_right, "space", shift_pairs(count, 1))
    after = lax.ppermute(to_left, "space", shift_pairs(count, -1))
    return before, after


def lo(field, width=1):
    return field[..., :width, :]


def hi(field, width=1):
    return field[..., field.shape[-2] - width:, :]


def halo_of(field):
    return exchange(hi(field), lo(field))


def tendency(field, halo, x_speed, y_speed, h_spread, v_spread, coupling, x_spacing, z_spacing):
    reach = int(x_spacing)
    padded = jnp.concatenate([halo[0]] * reach + [field] + [halo[1]] * reach, axis=-2)
    width = field.shape[-2]
    middle = field
    eastward = padded[..., 2 * reach:, :]
    westward = padded[..., :width, :]
    y_widths = [(0, 0)] * (middle.ndim - 1) + [(1, 1)]
    y_padded = jnp.pad(middle, y_widths)
    northward = y_padded[..., 2:]
    southward = y_padded[..., :-2]
    z_widths = [(0, 0)] * (middle.ndim - 3) + [(1, 1), (0, 0), (0, 0)]
    z_padded = jnp.pad(middle, z_widths)
    upward = z_padded[..., 2:, :, :]
    downward = z_padded[..., :-2, :, :]
    advection = (
        x_speed * (eastward - westward) / (2.0 * x_spacing)
        + y_speed * (northward - southward) * 0.5
    )
    diffusion = h_spread * (
        (eastward - 2.0 * middle + westward) / (x_spacing * x_spacing)
        + (northward - 2.0 * middle + southward)
    )
    vertical = v_spread * (upward - 2.0 * middle + downward) / (z_spacing * z_spacing)
    own = jnp.stack([coupling[0, 0], coupling[1, 1]]).reshape(-1, 1, 1, 1)
    other = jnp.stack([coupling[0, 1], coupling[1, 0]]).reshape(-1, 1, 1, 1)
    reaction = own * middle + other * middle[::-1]
    return diffusion + vertical - advection + reaction


def pair_sum(field):
    row = lax.broadcasted_iota(jnp.int32, field.shape, field.ndim - 2)
    partner = jnp.where(
        row % 2 == 0, jnp.roll(field, -1, axis=-2), jnp.roll(field, 1, axis=-2)
    )
    return field + partner


def shrink(field):
    levels = field[..., 0::2, :, :] + field[..., 1::2, :, :]
    return pair_sum(levels) * 0.25


def expand(field):
    return jnp.repeat(field, 2, axis=-3)


def expand_z(field):
    return jnp.repeat(field, 2, axis=-3)


def pick(items, index):
    out = items[0]
    for k in range(1, len(items)):
        out = jax.tree.map(lambda new, old: jnp.where(index == k, new, old), items[k], out)
    return out


def pair_map(fn, *pairs):
    return tuple(fn(*parts) for parts in zip(*pairs))


def body(initial, x_velocity, y_velocity, h_diffusion, v_diffusion, coupling):
    coarse_x = shrink(x_velocity)
    coarse_y = shrink(y_velocity)
    coarse_h = shrink(h_diffusion)
    coarse_v = shrink(v_diffusion)
    slabs = lax.axis_size("tm")
    columns = lax.axis_size("space")
    slab = lax.axis_index("tm")
    first = slab == 0

    def fine_rate(field, halo):
        return tendency(
            field, halo, x_velocity, y_velocity, h_diffusion, v_diffusion, coupling, 1.0, 1.0
        )

    def coarse_rate(field, halo):
        return tendency(field, halo, coarse_x, coarse_y, coarse_h, coarse_v, coupling, 2.0, 2.0)

    def first_node(node_zero, rate_zero, s0, s1, s2):
        return (
            node_zero
            + half_step * (rate_zero - s0)
            + slab_step * (s0 * (5.0 / 24.0) + s1 * (1.0 / 3.0) - s2 * (1.0 / 24.0))
        )

    def second_node(node_one, rate_one, s0, s1, s2):
        return (
            node_one
            + half_step * (rate_one - s1)
            + slab_step * (s0 * (-1.0 / 24.0) + s1 * (1.0 / 3.0) + s2 * (5.0 / 24.0))
        )

    coarse_first = shrink(initial)
    levels = initial.shape[-3]

    def joined(fine, coarse):
        return jnp.concatenate([fine, coarse], axis=-3)

    before, after = exchange(
        joined(hi(initial), hi(coarse_first)), joined(lo(initial), lo(coarse_first))
    )
    init_b, first_b = before[..., :levels, :, :], before[..., levels:, :, :]
    init_a, first_a = after[..., :levels, :, :], after[..., levels:, :, :]
    halo_zero = (init_b, init_a)
    halo_first = (first_b, first_a)
    first_rate = fine_rate(initial, halo_zero)
    coarse_first_rate = coarse_rate(coarse_first, halo_first)

    node_zero = initial
    rate_zero = first_rate
    node_one = first_node(node_zero, rate_zero, first_rate, first_rate, first_rate)
    halo_one = halo_of(node_one)
    rate_one = fine_rate(node_one, halo_one)
    node_two = second_node(node_one, rate_one, first_rate, first_rate, first_rate)
    two_b, two_a = exchange(hi(node_two, 2), lo(node_two, 2))
    halo_two = (hi(two_b), lo(two_a))
    coarse_end = shrink(node_two)
    halo_end = (hi(shrink(two_b)), lo(shrink(two_a)))
    rate_two = fine_rate(node_two, halo_two)
    source = shrink(slab_step * (rate_zero + 4.0 * rate_one + rate_two) / 6.0)
    offset = source - slab_step * coarse_first_rate

    chain = [coarse_first]
    chain_halo = [halo_first]
    rate = coarse_first_rate
    for count in range(slabs):
        after = chain[-1] + slab_step * rate + offset
        after_halo = halo_of(after)
        chain.append(after)
        chain_halo.append(after_halo)
        if count + 1 < slabs:
            rate = coarse_rate(after, after_halo)
    begins = pick(chain, slab)
    finals = pick(chain, slab + 1)
    begins_halo = pick(chain_halo, slab)
    finals_halo = pick(chain_halo, slab + 1)

    delta_zero = begins - coarse_first
    delta_one = finals - coarse_end
    fixed_zero = node_zero + expand(delta_zero)
    fixed_one = node_one + expand((delta_zero + delta_one) * 0.5)
    fixed_two = node_two + expand(delta_one)
    halo_dz = pair_map(lambda y, v: y - v, begins_halo, halo_first)
    halo_d1 = pair_map(lambda y, v: y - v, finals_halo, halo_end)
    halo_f0 = pair_map(lambda w, d: w + expand_z(d), halo_zero, halo_dz)
    halo_f1 = pair_map(
        lambda w, d0, d1: w + expand_z((d0 + d1) * 0.5), halo_one, halo_dz, halo_d1
    )
    halo_f2 = pair_map(lambda w, d: w + expand_z(d), halo_two, halo_d1)

    earlier_delta = begins - coarse_end
    earlier_end = node_two + expand(earlier_delta)
    halo_earlier_delta = pair_map(lambda y, v: y - v, begins_halo, halo_end)
    halo_earlier = pair_map(lambda w, d: w + expand_z(d), halo_two, halo_earlier_delta)
    wide_earlier = (
        two_b + expand(halo_earlier_delta[0]),
        two_a + expand(halo_earlier_delta[1]),
    )
    start = jnp.where(first, initial, earlier_end)
    halo_start = pair_map(lambda a, b: jnp.where(first, a, b), halo_zero, halo_earlier)
    halo_start_coarse = pair_map(
        lambda a, w: jnp.where(first, a, lo(shrink(w))), halo_first, wide_earlier
    )

    slope_zero = fine_rate(fixed_zero, halo_f0)
    slope_one = fine_rate(fixed_one, halo_f1)
    slope_two = fine_rate(fixed_two, halo_f2)
    node_zero = start
    rate_zero = fine_rate(node_zero, halo_start)
    node_one = first_node(node_zero, rate_zero, slope_zero, slope_one, slope_two)
    rate_one = fine_rate(node_one, halo_of(node_one))
    node_two = second_node(node_one, rate_one, slope_zero, slope_one, slope_two)
    rate_two = fine_rate(node_two, halo_of(node_two))
    coarse_zero = shrink(node_zero)
    coarse_end = shrink(node_two)
    source = shrink(slab_step * (rate_zero + 4.0 * rate_one + rate_two) / 6.0)
    offset = source - slab_step * coarse_rate(coarse_zero, halo_start_coarse)

    down = shift_pairs(slabs, 1)
    to_east = [
        (t * columns + c, (t + 1) * columns + c + 1)
        for t in range(slabs - 1)
        for c in range(columns - 1)
    ]
    to_west = [
        (t * columns + c, (t + 1) * columns + c - 1)
        for t in range(slabs - 1)
        for c in range(1, columns)
    ]
    carried = coarse_first
    carried_halo = halo_first
    rate = coarse_first_rate
    for count in range(slabs - 1):
        after = carried + slab_step * rate + offset
        passed = lax.ppermute(after, "tm", down)
        passed_b = lax.ppermute(hi(after), ("tm", "space"), to_east)
        passed_a = lax.ppermute(lo(after), ("tm", "space"), to_west)
        carried = jnp.where(first, coarse_first, passed)
        carried_halo = pair_map(
            lambda a, b: jnp.where(first, a, b), halo_first, (passed_b, passed_a)
        )
        rate = coarse_rate(carried, carried_halo)
    finals = carried + slab_step * rate + offset
    result = node_two + expand(finals - coarse_end)
    return result[None]


def solution(mesh):
    return jax.shard_map(
        body,
        mesh=mesh,
        in_specs=(
            P(None, None, "space", None),
            P(None, "space", None),
            P(None, "space", None),
            P(None, "space", None),
            P(None, "space", None),
            P(),
        ),
        out_specs=P("tm", None, None, "space", None),
        check_vma=False,
    )
```

```python
import jax
import jax.numpy as jnp
from jax import lax
from jax.sharding import PartitionSpec as P

ITERS = 2


slab_step = 0.5
half_step = 0.25


def shift_pairs(count, steps):
    return [(i, i + steps) for i in range(max(0, -steps), min(count, count - steps))]


def exchange(to_right, to_left):
    count = lax.axis_size("space")
    before = lax.ppermute(to_right, "space", shift_pairs(count, 1))
    after = lax.ppermute(to_left, "space", shift_pairs(count, -1))
    return before, after


def lo(field, width=1):
    return field[..., :width, :]


def hi(field, width=1):
    return field[..., field.shape[-2] - width:, :]


def halo_of(field):
    return exchange(hi(field), lo(field))


def tendency(field, halo, x_speed, y_speed, h_spread, v_spread, coupling, x_spacing, z_spacing):
    reach = int(x_spacing)
    padded = jnp.concatenate([halo[0]] * reach + [field] + [halo[1]] * reach, axis=-2)
    width = field.shape[-2]
    middle = field
    eastward = padded[..., 2 * reach:, :]
    westward = padded[..., :width, :]
    y_widths = [(0, 0)] * (middle.ndim - 1) + [(1, 1)]
    y_padded = jnp.pad(middle, y_widths)
    northward = y_padded[..., 2:]
    southward = y_padded[..., :-2]
    z_widths = [(0, 0)] * (middle.ndim - 3) + [(1, 1), (0, 0), (0, 0)]
    z_padded = jnp.pad(middle, z_widths)
    upward = z_padded[..., 2:, :, :]
    downward = z_padded[..., :-2, :, :]
    advection = (
        x_speed * (eastward - westward) / (2.0 * x_spacing)
        + y_speed * (northward - southward) * 0.5
    )
    diffusion = h_spread * (
        (eastward - 2.0 * middle + westward) / (x_spacing * x_spacing)
        + (northward - 2.0 * middle + southward)
    )
    vertical = v_spread * (upward - 2.0 * middle + downward) / (z_spacing * z_spacing)
    own = jnp.stack([coupling[0, 0], coupling[1, 1]]).reshape(-1, 1, 1, 1)
    other = jnp.stack([coupling[0, 1], coupling[1, 0]]).reshape(-1, 1, 1, 1)
    reaction = own * middle + other * middle[::-1]
    return diffusion + vertical - advection + reaction


def pair_sum(field):
    row = lax.broadcasted_iota(jnp.int32, field.shape, field.ndim - 2)
    partner = jnp.where(
        row % 2 == 0, jnp.roll(field, -1, axis=-2), jnp.roll(field, 1, axis=-2)
    )
    return field + partner


def shrink(field):
    levels = field[..., 0::2, :, :] + field[..., 1::2, :, :]
    return pair_sum(levels) * 0.25


def expand(field):
    return jnp.repeat(field, 2, axis=-3)


def expand_z(field):
    return jnp.repeat(field, 2, axis=-3)


def pick(items, index):
    out = items[0]
    for k in range(1, len(items)):
        out = jax.tree.map(lambda new, old: jnp.where(index == k, new, old), items[k], out)
    return out


def pair_map(fn, *pairs):
    return tuple(fn(*parts) for parts in zip(*pairs))


def body(initial, x_velocity, y_velocity, h_diffusion, v_diffusion, coupling):
    coarse_x = shrink(x_velocity)
    coarse_y = shrink(y_velocity)
    coarse_h = shrink(h_diffusion)
    coarse_v = shrink(v_diffusion)
    slabs = lax.axis_size("tm")
    columns = lax.axis_size("space")
    slab = lax.axis_index("tm")
    first = slab == 0

    def fine_rate(field, halo):
        return tendency(
            field, halo, x_velocity, y_velocity, h_diffusion, v_diffusion, coupling, 1.0, 1.0
        )

    def coarse_rate(field, halo):
        return tendency(field, halo, coarse_x, coarse_y, coarse_h, coarse_v, coupling, 2.0, 2.0)

    def first_node(node_zero, rate_zero, s0, s1, s2):
        return (
            node_zero
            + half_step * (rate_zero - s0)
            + slab_step * (s0 * (5.0 / 24.0) + s1 * (1.0 / 3.0) - s2 * (1.0 / 24.0))
        )

    def second_node(node_one, rate_one, s0, s1, s2):
        return (
            node_one
            + half_step * (rate_one - s1)
            + slab_step * (s0 * (-1.0 / 24.0) + s1 * (1.0 / 3.0) + s2 * (5.0 / 24.0))
        )

    coarse_first = shrink(initial)
    levels = initial.shape[-3]

    def joined(fine, coarse):
        return jnp.concatenate([fine, coarse], axis=-3)

    coarse_coefs = (coarse_x, coarse_y, coarse_h, coarse_v)
    coarse_levels = coarse_first.shape[-3]

    def coef_edge(edge):
        stacked = jnp.stack([edge(c) for c in coarse_coefs])
        return stacked.reshape((2, -1) + stacked.shape[-2:])

    before, after = exchange(
        joined(joined(hi(initial), hi(coarse_first)), coef_edge(hi)),
        joined(joined(lo(initial), lo(coarse_first)), coef_edge(lo)),
    )
    split = (levels, levels + coarse_levels)

    def parts(received):
        coefs = received[..., split[1]:, :, :].reshape((4, coarse_levels) + received.shape[-2:])
        return (
            received[..., : split[0], :, :],
            received[..., split[0] : split[1], :, :],
            tuple(coefs[k] for k in range(4)),
        )

    init_b, first_b, coefs_b = parts(before)
    init_a, first_a, coefs_a = parts(after)
    halo_zero = (init_b, init_a)
    halo_first = (first_b, first_a)
    first_rate = fine_rate(initial, halo_zero)
    coarse_first_rate = coarse_rate(coarse_first, halo_first)

    node_zero = initial
    rate_zero = first_rate
    node_one = first_node(node_zero, rate_zero, first_rate, first_rate, first_rate)
    halo_one = halo_of(node_one)
    rate_one = fine_rate(node_one, halo_one)
    node_two = second_node(node_one, rate_one, first_rate, first_rate, first_rate)
    two_b, two_a = exchange(hi(node_two, 2), lo(node_two, 2))
    halo_two = (hi(two_b), lo(two_a))
    coarse_end = shrink(node_two)
    halo_end = (hi(shrink(two_b)), lo(shrink(two_a)))
    rate_two = fine_rate(node_two, halo_two)
    source = shrink(slab_step * (rate_zero + 4.0 * rate_one + rate_two) / 6.0)
    offset = source - slab_step * coarse_first_rate

    chain = [coarse_first]
    chain_halo = [halo_first]
    rate = coarse_first_rate
    wide = None
    for count in range(slabs):
        after = chain[-1] + slab_step * rate + offset
        if wide is not None:
            strip_b, strip_a, offset_b, offset_a = wide
            rate_b = tendency(strip_b, (jnp.zeros_like(offset_b), lo(chain[-1])), *coefs_b,
                              coupling, 2.0, 2.0)
            rate_a = tendency(strip_a, (hi(chain[-1]), jnp.zeros_like(offset_a)), *coefs_a,
                              coupling, 2.0, 2.0)
            after_halo = (
                hi(strip_b) + slab_step * hi(rate_b) + offset_b,
                lo(strip_a) + slab_step * lo(rate_a) + offset_a,
            )
        elif count + 2 == slabs:
            packed_b, packed_a = exchange(
                jnp.concatenate([hi(after, 3), hi(offset)], axis=-2),
                jnp.concatenate([lo(after, 3), lo(offset)], axis=-2),
            )
            strip_b, offset_b = packed_b[..., :3, :], packed_b[..., 3:, :]
            strip_a, offset_a = packed_a[..., :3, :], packed_a[..., 3:, :]
            wide = (strip_b, strip_a, offset_b, offset_a)
            after_halo = (hi(strip_b), lo(strip_a))
        else:
            after_halo = halo_of(after)
        chain.append(after)
        chain_halo.append(after_halo)
        if count + 1 < slabs:
            rate = coarse_rate(after, after_halo)
    begins = pick(chain, slab)
    finals = pick(chain, slab + 1)
    begins_halo = pick(chain_halo, slab)
    finals_halo = pick(chain_halo, slab + 1)

    delta_zero = begins - coarse_first
    delta_one = finals - coarse_end
    fixed_zero = node_zero + expand(delta_zero)
    fixed_one = node_one + expand((delta_zero + delta_one) * 0.5)
    fixed_two = node_two + expand(delta_one)
    halo_dz = pair_map(lambda y, v: y - v, begins_halo, halo_first)
    halo_d1 = pair_map(lambda y, v: y - v, finals_halo, halo_end)
    halo_f0 = pair_map(lambda w, d: w + expand_z(d), halo_zero, halo_dz)
    halo_f1 = pair_map(
        lambda w, d0, d1: w + expand_z((d0 + d1) * 0.5), halo_one, halo_dz, halo_d1
    )
    halo_f2 = pair_map(lambda w, d: w + expand_z(d), halo_two, halo_d1)

    earlier_delta = begins - coarse_end
    earlier_end = node_two + expand(earlier_delta)
    halo_earlier_delta = pair_map(lambda y, v: y - v, begins_halo, halo_end)
    halo_earlier = pair_map(lambda w, d: w + expand_z(d), halo_two, halo_earlier_delta)
    wide_earlier = (
        two_b + expand(halo_earlier_delta[0]),
        two_a + expand(halo_earlier_delta[1]),
    )
    start = jnp.where(first, initial, earlier_end)
    halo_start = pair_map(lambda a, b: jnp.where(first, a, b), halo_zero, halo_earlier)
    halo_start_coarse = pair_map(
        lambda a, w: jnp.where(first, a, lo(shrink(w))), halo_first, wide_earlier
    )

    slope_zero = fine_rate(fixed_zero, halo_f0)
    slope_one = fine_rate(fixed_one, halo_f1)
    slope_two = fine_rate(fixed_two, halo_f2)
    node_zero = start
    rate_zero = fine_rate(node_zero, halo_start)
    node_one = first_node(node_zero, rate_zero, slope_zero, slope_one, slope_two)
    rate_one = fine_rate(node_one, halo_of(node_one))
    node_two = second_node(node_one, rate_one, slope_zero, slope_one, slope_two)
    rate_two = fine_rate(node_two, halo_of(node_two))
    coarse_zero = shrink(node_zero)
    coarse_end = shrink(node_two)
    source = shrink(slab_step * (rate_zero + 4.0 * rate_one + rate_two) / 6.0)
    offset = source - slab_step * coarse_rate(coarse_zero, halo_start_coarse)

    down = shift_pairs(slabs, 1)
    to_east = [
        (t * columns + c, (t + 1) * columns + c + 1)
        for t in range(slabs - 1)
        for c in range(columns - 1)
    ]
    to_west = [
        (t * columns + c, (t + 1) * columns + c - 1)
        for t in range(slabs - 1)
        for c in range(1, columns)
    ]
    carried = coarse_first
    carried_halo = halo_first
    rate = coarse_first_rate
    for count in range(slabs - 1):
        after = carried + slab_step * rate + offset
        passed = lax.ppermute(after, "tm", down)
        passed_b = lax.ppermute(hi(after), ("tm", "space"), to_east)
        passed_a = lax.ppermute(lo(after), ("tm", "space"), to_west)
        carried = jnp.where(first, coarse_first, passed)
        carried_halo = pair_map(
            lambda a, b: jnp.where(first, a, b), halo_first, (passed_b, passed_a)
        )
        rate = coarse_rate(carried, carried_halo)
    finals = carried + slab_step * rate + offset
    result = node_two + expand(finals - coarse_end)
    return result[None]


def solution(mesh):
    return jax.shard_map(
        body,
        mesh=mesh,
        in_specs=(
            P(None, None, "space", None),
            P(None, "space", None),
            P(None, "space", None),
            P(None, "space", None),
            P(None, "space", None),
            P(),
        ),
        out_specs=P("tm", None, None, "space", None),
        check_vma=False,
    )
```

```python
import jax
import jax.numpy as jnp
from jax import lax
from jax.sharding import PartitionSpec as P

ITERS = 2


slab_step = 0.5
half_step = 0.25


def shift_pairs(count, steps):
    return [(i, i + steps) for i in range(max(0, -steps), min(count, count - steps))]


def exchange(to_right, to_left):
    count = lax.axis_size("space")
    before = lax.ppermute(to_right, "space", shift_pairs(count, 1))
    after = lax.ppermute(to_left, "space", shift_pairs(count, -1))
    return before, after


def lo(field, width=1):
    return field[..., :width, :]


def hi(field, width=1):
    return field[..., field.shape[-2] - width:, :]


def halo_of(field):
    return exchange(hi(field), lo(field))


def tendency(field, halo, x_speed, y_speed, h_spread, v_spread, coupling, x_spacing, z_spacing):
    reach = int(x_spacing)
    padded = jnp.concatenate([halo[0]] * reach + [field] + [halo[1]] * reach, axis=-2)
    width = field.shape[-2]
    return stencil(
        field, padded[..., 2 * reach:, :], padded[..., :width, :],
        x_speed, y_speed, h_spread, v_spread, coupling, x_spacing, z_spacing,
    )


def stencil(middle, eastward, westward, x_speed, y_speed, h_spread, v_spread, coupling,
            x_spacing, z_spacing):
    y_widths = [(0, 0)] * (middle.ndim - 1) + [(1, 1)]
    y_padded = jnp.pad(middle, y_widths)
    northward = y_padded[..., 2:]
    southward = y_padded[..., :-2]
    z_widths = [(0, 0)] * (middle.ndim - 3) + [(1, 1), (0, 0), (0, 0)]
    z_padded = jnp.pad(middle, z_widths)
    upward = z_padded[..., 2:, :, :]
    downward = z_padded[..., :-2, :, :]
    advection = (
        x_speed * (eastward - westward) / (2.0 * x_spacing)
        + y_speed * (northward - southward) * 0.5
    )
    diffusion = h_spread * (
        (eastward - 2.0 * middle + westward) / (x_spacing * x_spacing)
        + (northward - 2.0 * middle + southward)
    )
    vertical = v_spread * (upward - 2.0 * middle + downward) / (z_spacing * z_spacing)
    own = jnp.stack([coupling[0, 0], coupling[1, 1]]).reshape(-1, 1, 1, 1)
    other = jnp.stack([coupling[0, 1], coupling[1, 0]]).reshape(-1, 1, 1, 1)
    reaction = own * middle + other * middle[::-1]
    return diffusion + vertical - advection + reaction


def pair_sum(field):
    row = lax.broadcasted_iota(jnp.int32, field.shape, field.ndim - 2)
    partner = jnp.where(
        row % 2 == 0, jnp.roll(field, -1, axis=-2), jnp.roll(field, 1, axis=-2)
    )
    return field + partner


def shrink(field):
    levels = field[..., 0::2, :, :] + field[..., 1::2, :, :]
    return pair_sum(levels) * 0.25


def expand(field):
    return jnp.repeat(field, 2, axis=-3)


def expand_z(field):
    return jnp.repeat(field, 2, axis=-3)


def pick(items, index):
    out = items[0]
    for k in range(1, len(items)):
        out = jax.tree.map(lambda new, old: jnp.where(index == k, new, old), items[k], out)
    return out


def pair_map(fn, *pairs):
    return tuple(fn(*parts) for parts in zip(*pairs))


def body(initial, x_velocity, y_velocity, h_diffusion, v_diffusion, coupling):
    coarse_x = shrink(x_velocity)
    coarse_y = shrink(y_velocity)
    coarse_h = shrink(h_diffusion)
    coarse_v = shrink(v_diffusion)
    slabs = lax.axis_size("tm")
    columns = lax.axis_size("space")
    slab = lax.axis_index("tm")
    first = slab == 0

    def fine_rate(field, halo):
        return tendency(
            field, halo, x_velocity, y_velocity, h_diffusion, v_diffusion, coupling, 1.0, 1.0
        )

    def coarse_rate(field, halo):
        return tendency(field, halo, coarse_x, coarse_y, coarse_h, coarse_v, coupling, 2.0, 2.0)

    def first_node(node_zero, rate_zero, s0, s1, s2):
        return (
            node_zero
            + half_step * (rate_zero - s0)
            + slab_step * (s0 * (5.0 / 24.0) + s1 * (1.0 / 3.0) - s2 * (1.0 / 24.0))
        )

    def second_node(node_one, rate_one, s0, s1, s2):
        return (
            node_one
            + half_step * (rate_one - s1)
            + slab_step * (s0 * (-1.0 / 24.0) + s1 * (1.0 / 3.0) + s2 * (5.0 / 24.0))
        )

    coarse_first = shrink(initial)
    levels = initial.shape[-3]

    def joined(fine, coarse):
        return jnp.concatenate([fine, coarse], axis=-3)

    coarse_coefs = (coarse_x, coarse_y, coarse_h, coarse_v)
    coarse_levels = coarse_first.shape[-3]

    def coef_edge(edge):
        stacked = jnp.stack([edge(c) for c in coarse_coefs])
        return stacked.reshape((2, -1) + stacked.shape[-2:])

    before, after = exchange(
        joined(joined(hi(initial), hi(coarse_first)), coef_edge(hi)),
        joined(joined(lo(initial), lo(coarse_first)), coef_edge(lo)),
    )
    split = (levels, levels + coarse_levels)

    def parts(received):
        coefs = received[..., split[1]:, :, :].reshape((4, coarse_levels) + received.shape[-2:])
        return (
            received[..., : split[0], :, :],
            received[..., split[0] : split[1], :, :],
            tuple(coefs[k] for k in range(4)),
        )

    init_b, first_b, coefs_b = parts(before)
    init_a, first_a, coefs_a = parts(after)
    halo_zero = (init_b, init_a)
    halo_first = (first_b, first_a)
    first_rate = fine_rate(initial, halo_zero)
    coarse_first_rate = coarse_rate(coarse_first, halo_first)

    node_zero = initial
    rate_zero = first_rate
    node_one = first_node(node_zero, rate_zero, first_rate, first_rate, first_rate)
    halo_one = halo_of(node_one)
    rate_one = fine_rate(node_one, halo_one)
    node_two = second_node(node_one, rate_one, first_rate, first_rate, first_rate)
    two_b, two_a = exchange(hi(node_two, 2), lo(node_two, 2))
    halo_two = (hi(two_b), lo(two_a))
    coarse_end = shrink(node_two)
    halo_end = (hi(shrink(two_b)), lo(shrink(two_a)))
    rate_two = fine_rate(node_two, halo_two)
    source = shrink(slab_step * (rate_zero + 4.0 * rate_one + rate_two) / 6.0)
    offset = source - slab_step * coarse_first_rate

    chain = [coarse_first]
    chain_halo = [halo_first]
    rate = coarse_first_rate
    wide = None
    for count in range(slabs):
        after = chain[-1] + slab_step * rate + offset
        if wide is not None:
            strip_b, strip_a, offset_b, offset_a = wide
            edge_b = strip_b[..., 2:3, :]
            edge_a = strip_a[..., 0:1, :]
            rate_b = stencil(edge_b, lo(chain[-1]), strip_b[..., 0:1, :], *coefs_b,
                             coupling, 2.0, 2.0)
            rate_a = stencil(edge_a, strip_a[..., 2:3, :], hi(chain[-1]), *coefs_a,
                             coupling, 2.0, 2.0)
            after_halo = (
                edge_b + slab_step * rate_b + offset_b,
                edge_a + slab_step * rate_a + offset_a,
            )
        elif count + 2 == slabs:
            packed_b, packed_a = exchange(
                jnp.concatenate([hi(after, 3), hi(offset)], axis=-2),
                jnp.concatenate([lo(after, 3), lo(offset)], axis=-2),
            )
            strip_b, offset_b = packed_b[..., :3, :], packed_b[..., 3:, :]
            strip_a, offset_a = packed_a[..., :3, :], packed_a[..., 3:, :]
            wide = (strip_b, strip_a, offset_b, offset_a)
            after_halo = (hi(strip_b), lo(strip_a))
        else:
            after_halo = halo_of(after)
        chain.append(after)
        chain_halo.append(after_halo)
        if count + 1 < slabs:
            rate = coarse_rate(after, after_halo)
    begins = pick(chain, slab)
    finals = pick(chain, slab + 1)
    begins_halo = pick(chain_halo, slab)
    finals_halo = pick(chain_halo, slab + 1)

    delta_zero = begins - coarse_first
    delta_one = finals - coarse_end
    fixed_zero = node_zero + expand(delta_zero)
    fixed_one = node_one + expand((delta_zero + delta_one) * 0.5)
    fixed_two = node_two + expand(delta_one)
    halo_dz = pair_map(lambda y, v: y - v, begins_halo, halo_first)
    halo_d1 = pair_map(lambda y, v: y - v, finals_halo, halo_end)
    halo_f0 = pair_map(lambda w, d: w + expand_z(d), halo_zero, halo_dz)
    halo_f1 = pair_map(
        lambda w, d0, d1: w + expand_z((d0 + d1) * 0.5), halo_one, halo_dz, halo_d1
    )
    halo_f2 = pair_map(lambda w, d: w + expand_z(d), halo_two, halo_d1)

    earlier_delta = begins - coarse_end
    earlier_end = node_two + expand(earlier_delta)
    halo_earlier_delta = pair_map(lambda y, v: y - v, begins_halo, halo_end)
    halo_earlier = pair_map(lambda w, d: w + expand_z(d), halo_two, halo_earlier_delta)
    wide_earlier = (
        two_b + expand(halo_earlier_delta[0]),
        two_a + expand(halo_earlier_delta[1]),
    )
    start = jnp.where(first, initial, earlier_end)
    halo_start = pair_map(lambda a, b: jnp.where(first, a, b), halo_zero, halo_earlier)
    halo_start_coarse = pair_map(
        lambda a, w: jnp.where(first, a, lo(shrink(w))), halo_first, wide_earlier
    )

    slope_zero = fine_rate(fixed_zero, halo_f0)
    slope_one = fine_rate(fixed_one, halo_f1)
    slope_two = fine_rate(fixed_two, halo_f2)
    node_zero = start
    rate_zero = fine_rate(node_zero, halo_start)
    node_one = first_node(node_zero, rate_zero, slope_zero, slope_one, slope_two)
    rate_one = fine_rate(node_one, halo_of(node_one))
    node_two = second_node(node_one, rate_one, slope_zero, slope_one, slope_two)
    rate_two = fine_rate(node_two, halo_of(node_two))
    coarse_zero = shrink(node_zero)
    coarse_end = shrink(node_two)
    source = shrink(slab_step * (rate_zero + 4.0 * rate_one + rate_two) / 6.0)
    offset = source - slab_step * coarse_rate(coarse_zero, halo_start_coarse)

    down = shift_pairs(slabs, 1)
    to_east = [
        (t * columns + c, (t + 1) * columns + c + 1)
        for t in range(slabs - 1)
        for c in range(columns - 1)
    ]
    to_west = [
        (t * columns + c, (t + 1) * columns + c - 1)
        for t in range(slabs - 1)
        for c in range(1, columns)
    ]
    carried = coarse_first
    carried_halo = halo_first
    rate = coarse_first_rate
    for count in range(slabs - 1):
        after = carried + slab_step * rate + offset
        passed = lax.ppermute(after, "tm", down)
        passed_b = lax.ppermute(hi(after), ("tm", "space"), to_east)
        passed_a = lax.ppermute(lo(after), ("tm", "space"), to_west)
        carried = jnp.where(first, coarse_first, passed)
        carried_halo = pair_map(
            lambda a, b: jnp.where(first, a, b), halo_first, (passed_b, passed_a)
        )
        rate = coarse_rate(carried, carried_halo)
    finals = carried + slab_step * rate + offset
    result = node_two + expand(finals - coarse_end)
    return result[None]


def solution(mesh):
    return jax.shard_map(
        body,
        mesh=mesh,
        in_specs=(
            P(None, None, "space", None),
            P(None, "space", None),
            P(None, "space", None),
            P(None, "space", None),
            P(None, "space", None),
            P(),
        ),
        out_specs=P("tm", None, None, "space", None),
        check_vma=False,
    )
```

```python
import jax
import jax.numpy as jnp
from jax import lax
from jax.sharding import PartitionSpec as P

ITERS = 2


slab_step = 0.5
half_step = 0.25


def shift_pairs(count, steps):
    return [(i, i + steps) for i in range(max(0, -steps), min(count, count - steps))]


def exchange(to_right, to_left):
    count = lax.axis_size("space")
    before = lax.ppermute(to_right, "space", shift_pairs(count, 1))
    after = lax.ppermute(to_left, "space", shift_pairs(count, -1))
    return before, after


def lo(field, width=1):
    return field[..., :width, :]


def hi(field, width=1):
    return field[..., field.shape[-2] - width:, :]


def pack(before, after):
    return jnp.concatenate([before, after], axis=-2)


def west(halo):
    return halo[..., 0:1, :]


def east(halo):
    return halo[..., 1:2, :]


def halo_of(field):
    return pack(*exchange(hi(field), lo(field)))


def tendency(field, halo, x_speed, y_speed, h_spread, v_spread, coupling, x_spacing, z_spacing):
    reach = int(x_spacing)
    padded = jnp.concatenate([west(halo)] * reach + [field] + [east(halo)] * reach, axis=-2)
    width = field.shape[-2]
    middle = field
    eastward = padded[..., 2 * reach:, :]
    westward = padded[..., :width, :]
    y_widths = [(0, 0)] * (middle.ndim - 1) + [(1, 1)]
    y_padded = jnp.pad(middle, y_widths)
    northward = y_padded[..., 2:]
    southward = y_padded[..., :-2]
    z_widths = [(0, 0)] * (middle.ndim - 3) + [(1, 1), (0, 0), (0, 0)]
    z_padded = jnp.pad(middle, z_widths)
    upward = z_padded[..., 2:, :, :]
    downward = z_padded[..., :-2, :, :]
    advection = (
        x_speed * (eastward - westward) / (2.0 * x_spacing)
        + y_speed * (northward - southward) * 0.5
    )
    diffusion = h_spread * (
        (eastward - 2.0 * middle + westward) / (x_spacing * x_spacing)
        + (northward - 2.0 * middle + southward)
    )
    vertical = v_spread * (upward - 2.0 * middle + downward) / (z_spacing * z_spacing)
    own = jnp.stack([coupling[0, 0], coupling[1, 1]]).reshape(-1, 1, 1, 1)
    other = jnp.stack([coupling[0, 1], coupling[1, 0]]).reshape(-1, 1, 1, 1)
    reaction = own * middle + other * middle[::-1]
    return diffusion + vertical - advection + reaction


def pair_sum(field):
    row = lax.broadcasted_iota(jnp.int32, field.shape, field.ndim - 2)
    partner = jnp.where(
        row % 2 == 0, jnp.roll(field, -1, axis=-2), jnp.roll(field, 1, axis=-2)
    )
    return field + partner


def shrink(field):
    levels = field[..., 0::2, :, :] + field[..., 1::2, :, :]
    return pair_sum(levels) * 0.25


def expand(field):
    return jnp.repeat(field, 2, axis=-3)


def expand_z(field):
    return jnp.repeat(field, 2, axis=-3)


def pick(items, index):
    out = items[0]
    for k in range(1, len(items)):
        out = jax.tree.map(lambda new, old: jnp.where(index == k, new, old), items[k], out)
    return out


def pair_map(fn, *halos):
    return fn(*halos)


def body(initial, x_velocity, y_velocity, h_diffusion, v_diffusion, coupling):
    coarse_x = shrink(x_velocity)
    coarse_y = shrink(y_velocity)
    coarse_h = shrink(h_diffusion)
    coarse_v = shrink(v_diffusion)
    slabs = lax.axis_size("tm")
    columns = lax.axis_size("space")
    slab = lax.axis_index("tm")
    first = slab == 0

    def fine_rate(field, halo):
        return tendency(
            field, halo, x_velocity, y_velocity, h_diffusion, v_diffusion, coupling, 1.0, 1.0
        )

    def coarse_rate(field, halo):
        return tendency(field, halo, coarse_x, coarse_y, coarse_h, coarse_v, coupling, 2.0, 2.0)

    def first_node(node_zero, rate_zero, s0, s1, s2):
        return (
            node_zero
            + half_step * (rate_zero - s0)
            + slab_step * (s0 * (5.0 / 24.0) + s1 * (1.0 / 3.0) - s2 * (1.0 / 24.0))
        )

    def second_node(node_one, rate_one, s0, s1, s2):
        return (
            node_one
            + half_step * (rate_one - s1)
            + slab_step * (s0 * (-1.0 / 24.0) + s1 * (1.0 / 3.0) + s2 * (5.0 / 24.0))
        )

    coarse_first = shrink(initial)
    levels = initial.shape[-3]

    def joined(fine, coarse):
        return jnp.concatenate([fine, coarse], axis=-3)

    before, after = exchange(
        joined(hi(initial), hi(coarse_first)), joined(lo(initial), lo(coarse_first))
    )
    init_b, first_b = before[..., :levels, :, :], before[..., levels:, :, :]
    init_a, first_a = after[..., :levels, :, :], after[..., levels:, :, :]
    halo_zero = pack(init_b, init_a)
    halo_first = pack(first_b, first_a)
    first_rate = fine_rate(initial, halo_zero)
    coarse_first_rate = coarse_rate(coarse_first, halo_first)

    node_zero = initial
    rate_zero = first_rate
    node_one = first_node(node_zero, rate_zero, first_rate, first_rate, first_rate)
    halo_one = halo_of(node_one)
    rate_one = fine_rate(node_one, halo_one)
    node_two = second_node(node_one, rate_one, first_rate, first_rate, first_rate)
    two_b, two_a = exchange(hi(node_two, 2), lo(node_two, 2))
    halo_two = pack(hi(two_b), lo(two_a))
    coarse_end = shrink(node_two)
    halo_end = pack(hi(shrink(two_b)), lo(shrink(two_a)))
    rate_two = fine_rate(node_two, halo_two)
    source = shrink(slab_step * (rate_zero + 4.0 * rate_one + rate_two) / 6.0)
    offset = source - slab_step * coarse_first_rate

    chain = [coarse_first]
    chain_halo = [halo_first]
    rate = coarse_first_rate
    for count in range(slabs):
        after = chain[-1] + slab_step * rate + offset
        after_halo = halo_of(after)
        chain.append(after)
        chain_halo.append(after_halo)
        if count + 1 < slabs:
            rate = coarse_rate(after, after_halo)
    begins = pick(chain, slab)
    finals = pick(chain, slab + 1)
    begins_halo = pick(chain_halo, slab)
    finals_halo = pick(chain_halo, slab + 1)

    delta_zero = begins - coarse_first
    delta_one = finals - coarse_end
    fixed_zero = node_zero + expand(delta_zero)
    fixed_one = node_one + expand((delta_zero + delta_one) * 0.5)
    fixed_two = node_two + expand(delta_one)
    halo_dz = pair_map(lambda y, v: y - v, begins_halo, halo_first)
    halo_d1 = pair_map(lambda y, v: y - v, finals_halo, halo_end)
    halo_f0 = pair_map(lambda w, d: w + expand_z(d), halo_zero, halo_dz)
    halo_f1 = pair_map(
        lambda w, d0, d1: w + expand_z((d0 + d1) * 0.5), halo_one, halo_dz, halo_d1
    )
    halo_f2 = pair_map(lambda w, d: w + expand_z(d), halo_two, halo_d1)

    earlier_delta = begins - coarse_end
    earlier_end = node_two + expand(earlier_delta)
    halo_earlier_delta = pair_map(lambda y, v: y - v, begins_halo, halo_end)
    halo_earlier = pair_map(lambda w, d: w + expand_z(d), halo_two, halo_earlier_delta)
    wide_earlier = (
        two_b + expand(west(halo_earlier_delta)),
        two_a + expand(east(halo_earlier_delta)),
    )
    start = jnp.where(first, initial, earlier_end)
    halo_start = pair_map(lambda a, b: jnp.where(first, a, b), halo_zero, halo_earlier)
    halo_start_coarse = jnp.where(
        first, halo_first, pack(lo(shrink(wide_earlier[0])), lo(shrink(wide_earlier[1])))
    )

    slope_zero = fine_rate(fixed_zero, halo_f0)
    slope_one = fine_rate(fixed_one, halo_f1)
    slope_two = fine_rate(fixed_two, halo_f2)
    node_zero = start
    rate_zero = fine_rate(node_zero, halo_start)
    node_one = first_node(node_zero, rate_zero, slope_zero, slope_one, slope_two)
    rate_one = fine_rate(node_one, halo_of(node_one))
    node_two = second_node(node_one, rate_one, slope_zero, slope_one, slope_two)
    rate_two = fine_rate(node_two, halo_of(node_two))
    coarse_zero = shrink(node_zero)
    coarse_end = shrink(node_two)
    source = shrink(slab_step * (rate_zero + 4.0 * rate_one + rate_two) / 6.0)
    offset = source - slab_step * coarse_rate(coarse_zero, halo_start_coarse)

    down = shift_pairs(slabs, 1)
    to_east = [
        (t * columns + c, (t + 1) * columns + c + 1)
        for t in range(slabs - 1)
        for c in range(columns - 1)
    ]
    to_west = [
        (t * columns + c, (t + 1) * columns + c - 1)
        for t in range(slabs - 1)
        for c in range(1, columns)
    ]
    carried = coarse_first
    carried_halo = halo_first
    rate = coarse_first_rate
    for count in range(slabs - 1):
        after = carried + slab_step * rate + offset
        passed = lax.ppermute(after, "tm", down)
        passed_b = lax.ppermute(hi(after), ("tm", "space"), to_east)
        passed_a = lax.ppermute(lo(after), ("tm", "space"), to_west)
        carried = jnp.where(first, coarse_first, passed)
        carried_halo = jnp.where(first, halo_first, pack(passed_b, passed_a))
        rate = coarse_rate(carried, carried_halo)
    finals = carried + slab_step * rate + offset
    result = node_two + expand(finals - coarse_end)
    return result[None]


def solution(mesh):
    return jax.shard_map(
        body,
        mesh=mesh,
        in_specs=(
            P(None, None, "space", None),
            P(None, "space", None),
            P(None, "space", None),
            P(None, "space", None),
            P(None, "space", None),
            P(),
        ),
        out_specs=P("tm", None, None, "space", None),
        check_vma=False,
    )
```

```python
import jax
import jax.numpy as jnp
from jax import lax
from jax.sharding import PartitionSpec as P

ITERS = 2


slab_step = 0.5
half_step = 0.25


def shift_pairs(count, steps):
    return [(i, i + steps) for i in range(max(0, -steps), min(count, count - steps))]


def exchange(to_right, to_left):
    count = lax.axis_size("space")
    before = lax.ppermute(to_right, "space", shift_pairs(count, 1))
    after = lax.ppermute(to_left, "space", shift_pairs(count, -1))
    return before, after


def lo(field, width=1):
    return field[..., :width, :]


def hi(field, width=1):
    return field[..., field.shape[-2] - width:, :]


def pack(before, after):
    return jnp.concatenate([before, after], axis=-2)


def west(halo):
    return halo[..., 0:1, :]


def east(halo):
    return halo[..., 1:2, :]


def halo_of(field):
    return pack(*exchange(hi(field), lo(field)))


def tendency(field, halo, x_speed, y_speed, h_spread, v_spread, coupling, x_spacing, z_spacing):
    reach = int(x_spacing)
    padded = jnp.concatenate([west(halo)] * reach + [field] + [east(halo)] * reach, axis=-2)
    width = field.shape[-2]
    return stencil(
        field, padded[..., 2 * reach:, :], padded[..., :width, :],
        x_speed, y_speed, h_spread, v_spread, coupling, x_spacing, z_spacing,
    )


def stencil(middle, eastward, westward, x_speed, y_speed, h_spread, v_spread, coupling,
            x_spacing, z_spacing):
    y_widths = [(0, 0)] * (middle.ndim - 1) + [(1, 1)]
    y_padded = jnp.pad(middle, y_widths)
    northward = y_padded[..., 2:]
    southward = y_padded[..., :-2]
    z_widths = [(0, 0)] * (middle.ndim - 3) + [(1, 1), (0, 0), (0, 0)]
    z_padded = jnp.pad(middle, z_widths)
    upward = z_padded[..., 2:, :, :]
    downward = z_padded[..., :-2, :, :]
    advection = (
        x_speed * (eastward - westward) / (2.0 * x_spacing)
        + y_speed * (northward - southward) * 0.5
    )
    diffusion = h_spread * (
        (eastward - 2.0 * middle + westward) / (x_spacing * x_spacing)
        + (northward - 2.0 * middle + southward)
    )
    vertical = v_spread * (upward - 2.0 * middle + downward) / (z_spacing * z_spacing)
    own = jnp.stack([coupling[0, 0], coupling[1, 1]]).reshape(-1, 1, 1, 1)
    other = jnp.stack([coupling[0, 1], coupling[1, 0]]).reshape(-1, 1, 1, 1)
    reaction = own * middle + other * middle[::-1]
    return diffusion + vertical - advection + reaction


def pair_sum(field):
    row = lax.broadcasted_iota(jnp.int32, field.shape, field.ndim - 2)
    partner = jnp.where(
        row % 2 == 0, jnp.roll(field, -1, axis=-2), jnp.roll(field, 1, axis=-2)
    )
    return field + partner


def shrink(field):
    levels = field[..., 0::2, :, :] + field[..., 1::2, :, :]
    return pair_sum(levels) * 0.25


def expand(field):
    return jnp.repeat(field, 2, axis=-3)


def expand_z(field):
    return jnp.repeat(field, 2, axis=-3)


def pick(items, index):
    out = items[0]
    for k in range(1, len(items)):
        out = jax.tree.map(lambda new, old: jnp.where(index == k, new, old), items[k], out)
    return out


def pair_map(fn, *halos):
    return fn(*halos)


def body(initial, x_velocity, y_velocity, h_diffusion, v_diffusion, coupling):
    coarse_x = shrink(x_velocity)
    coarse_y = shrink(y_velocity)
    coarse_h = shrink(h_diffusion)
    coarse_v = shrink(v_diffusion)
    slabs = lax.axis_size("tm")
    columns = lax.axis_size("space")
    slab = lax.axis_index("tm")
    first = slab == 0

    def fine_rate(field, halo):
        return tendency(
            field, halo, x_velocity, y_velocity, h_diffusion, v_diffusion, coupling, 1.0, 1.0
        )

    def coarse_rate(field, halo):
        return tendency(field, halo, coarse_x, coarse_y, coarse_h, coarse_v, coupling, 2.0, 2.0)

    def first_node(node_zero, rate_zero, s0, s1, s2):
        return (
            node_zero
            + half_step * (rate_zero - s0)
            + slab_step * (s0 * (5.0 / 24.0) + s1 * (1.0 / 3.0) - s2 * (1.0 / 24.0))
        )

    def second_node(node_one, rate_one, s0, s1, s2):
        return (
            node_one
            + half_step * (rate_one - s1)
            + slab_step * (s0 * (-1.0 / 24.0) + s1 * (1.0 / 3.0) + s2 * (5.0 / 24.0))
        )

    coarse_first = shrink(initial)
    levels = initial.shape[-3]

    def joined(fine, coarse):
        return jnp.concatenate([fine, coarse], axis=-3)

    coarse_coefs = (coarse_x, coarse_y, coarse_h, coarse_v)
    coarse_levels = coarse_first.shape[-3]

    def coef_edge(edge):
        stacked = jnp.stack([edge(c) for c in coarse_coefs])
        return stacked.reshape((2, -1) + stacked.shape[-2:])

    before, after = exchange(
        joined(joined(hi(initial), hi(coarse_first)), coef_edge(hi)),
        joined(joined(lo(initial), lo(coarse_first)), coef_edge(lo)),
    )
    split = (levels, levels + coarse_levels)
    init_b, first_b = before[..., : split[0], :, :], before[..., split[0] : split[1], :, :]
    init_a, first_a = after[..., : split[0], :, :], after[..., split[0] : split[1], :, :]
    edge_coefs = pack(before[..., split[1] :, :, :], after[..., split[1] :, :, :])
    edge_coefs = edge_coefs.reshape((4, coarse_levels) + edge_coefs.shape[-2:])
    halo_zero = pack(init_b, init_a)
    halo_first = pack(first_b, first_a)
    first_rate = fine_rate(initial, halo_zero)
    coarse_first_rate = coarse_rate(coarse_first, halo_first)

    node_zero = initial
    rate_zero = first_rate
    node_one = first_node(node_zero, rate_zero, first_rate, first_rate, first_rate)
    halo_one = halo_of(node_one)
    rate_one = fine_rate(node_one, halo_one)
    node_two = second_node(node_one, rate_one, first_rate, first_rate, first_rate)
    two_b, two_a = exchange(hi(node_two, 2), lo(node_two, 2))
    halo_two = pack(hi(two_b), lo(two_a))
    coarse_end = shrink(node_two)
    halo_end = pack(hi(shrink(two_b)), lo(shrink(two_a)))
    rate_two = fine_rate(node_two, halo_two)
    source = shrink(slab_step * (rate_zero + 4.0 * rate_one + rate_two) / 6.0)
    offset = source - slab_step * coarse_first_rate

    chain = [coarse_first]
    chain_halo = [halo_first]
    rate = coarse_first_rate
    wide = None
    for count in range(slabs):
        after = chain[-1] + slab_step * rate + offset
        if wide is not None:
            strip_b, strip_a, offset_edge = wide
            edge = pack(strip_b[..., 2:3, :], strip_a[..., 0:1, :])
            edge_rate = stencil(
                edge,
                pack(lo(chain[-1]), strip_a[..., 2:3, :]),
                pack(strip_b[..., 0:1, :], hi(chain[-1])),
                *(edge_coefs[k] for k in range(4)),
                coupling, 2.0, 2.0,
            )
            after_halo = edge + slab_step * edge_rate + offset_edge
        elif count + 2 == slabs:
            packed_b, packed_a = exchange(
                jnp.concatenate([hi(after, 3), hi(offset)], axis=-2),
                jnp.concatenate([lo(after, 3), lo(offset)], axis=-2),
            )
            strip_b, strip_a = packed_b[..., :3, :], packed_a[..., :3, :]
            wide = (strip_b, strip_a, pack(packed_b[..., 3:, :], packed_a[..., 3:, :]))
            after_halo = pack(strip_b[..., 2:3, :], strip_a[..., 0:1, :])
        else:
            after_halo = halo_of(after)
        chain.append(after)
        chain_halo.append(after_halo)
        if count + 1 < slabs:
            rate = coarse_rate(after, after_halo)
    begins = pick(chain, slab)
    finals = pick(chain, slab + 1)
    begins_halo = pick(chain_halo, slab)
    finals_halo = pick(chain_halo, slab + 1)

    delta_zero = begins - coarse_first
    delta_one = finals - coarse_end
    fixed_zero = node_zero + expand(delta_zero)
    fixed_one = node_one + expand((delta_zero + delta_one) * 0.5)
    fixed_two = node_two + expand(delta_one)
    halo_dz = pair_map(lambda y, v: y - v, begins_halo, halo_first)
    halo_d1 = pair_map(lambda y, v: y - v, finals_halo, halo_end)
    halo_f0 = pair_map(lambda w, d: w + expand_z(d), halo_zero, halo_dz)
    halo_f1 = pair_map(
        lambda w, d0, d1: w + expand_z((d0 + d1) * 0.5), halo_one, halo_dz, halo_d1
    )
    halo_f2 = pair_map(lambda w, d: w + expand_z(d), halo_two, halo_d1)

    earlier_delta = begins - coarse_end
    earlier_end = node_two + expand(earlier_delta)
    halo_earlier_delta = pair_map(lambda y, v: y - v, begins_halo, halo_end)
    halo_earlier = pair_map(lambda w, d: w + expand_z(d), halo_two, halo_earlier_delta)
    wide_earlier = (
        two_b + expand(west(halo_earlier_delta)),
        two_a + expand(east(halo_earlier_delta)),
    )
    start = jnp.where(first, initial, earlier_end)
    halo_start = pair_map(lambda a, b: jnp.where(first, a, b), halo_zero, halo_earlier)
    halo_start_coarse = jnp.where(
        first, halo_first, pack(lo(shrink(wide_earlier[0])), lo(shrink(wide_earlier[1])))
    )

    slope_zero = fine_rate(fixed_zero, halo_f0)
    slope_one = fine_rate(fixed_one, halo_f1)
    slope_two = fine_rate(fixed_two, halo_f2)
    node_zero = start
    rate_zero = fine_rate(node_zero, halo_start)
    node_one = first_node(node_zero, rate_zero, slope_zero, slope_one, slope_two)
    rate_one = fine_rate(node_one, halo_of(node_one))
    node_two = second_node(node_one, rate_one, slope_zero, slope_one, slope_two)
    rate_two = fine_rate(node_two, halo_of(node_two))
    coarse_zero = shrink(node_zero)
    coarse_end = shrink(node_two)
    source = shrink(slab_step * (rate_zero + 4.0 * rate_one + rate_two) / 6.0)
    offset = source - slab_step * coarse_rate(coarse_zero, halo_start_coarse)

    down = shift_pairs(slabs, 1)
    to_east = [
        (t * columns + c, (t + 1) * columns + c + 1)
        for t in range(slabs - 1)
        for c in range(columns - 1)
    ]
    to_west = [
        (t * columns + c, (t + 1) * columns + c - 1)
        for t in range(slabs - 1)
        for c in range(1, columns)
    ]
    carried = coarse_first
    carried_halo = halo_first
    rate = coarse_first_rate
    for count in range(slabs - 1):
        after = carried + slab_step * rate + offset
        passed = lax.ppermute(after, "tm", down)
        passed_b = lax.ppermute(hi(after), ("tm", "space"), to_east)
        passed_a = lax.ppermute(lo(after), ("tm", "space"), to_west)
        carried = jnp.where(first, coarse_first, passed)
        carried_halo = jnp.where(first, halo_first, pack(passed_b, passed_a))
        rate = coarse_rate(carried, carried_halo)
    finals = carried + slab_step * rate + offset
    result = node_two + expand(finals - coarse_end)
    return result[None]


def solution(mesh):
    return jax.shard_map(
        body,
        mesh=mesh,
        in_specs=(
            P(None, None, "space", None),
            P(None, "space", None),
            P(None, "space", None),
            P(None, "space", None),
            P(None, "space", None),
            P(),
        ),
        out_specs=P("tm", None, None, "space", None),
        check_vma=False,
    )
```

```python
import jax
import jax.numpy as jnp
from jax import lax
from jax.sharding import PartitionSpec as P

ITERS = 2


slab_step = 0.5
half_step = 0.25


def shift_pairs(count, steps):
    return [(i, i + steps) for i in range(max(0, -steps), min(count, count - steps))]


def exchange(to_right, to_left):
    count = lax.axis_size("space")
    before = lax.ppermute(to_right, "space", shift_pairs(count, 1))
    after = lax.ppermute(to_left, "space", shift_pairs(count, -1))
    return before, after


def lo(field, width=1):
    return field[..., :width, :]


def hi(field, width=1):
    return field[..., field.shape[-2] - width:, :]


def pack(before, after):
    return jnp.concatenate([before, after], axis=-2)


def west(halo):
    return halo[..., 0:1, :]


def east(halo):
    return halo[..., 1:2, :]


def halo_of(field):
    return pack(*exchange(hi(field), lo(field)))


def tendency(field, halo, x_speed, y_speed, h_spread, v_spread, coupling, x_spacing, z_spacing):
    reach = int(x_spacing)
    padded = jnp.concatenate([west(halo)] * reach + [field] + [east(halo)] * reach, axis=-2)
    width = field.shape[-2]
    return stencil(
        field, padded[..., 2 * reach:, :], padded[..., :width, :],
        x_speed, y_speed, h_spread, v_spread, coupling, x_spacing, z_spacing,
    )


def stencil(middle, eastward, westward, x_speed, y_speed, h_spread, v_spread, coupling,
            x_spacing, z_spacing):
    y_widths = [(0, 0)] * (middle.ndim - 1) + [(1, 1)]
    y_padded = jnp.pad(middle, y_widths)
    northward = y_padded[..., 2:]
    southward = y_padded[..., :-2]
    z_widths = [(0, 0)] * (middle.ndim - 3) + [(1, 1), (0, 0), (0, 0)]
    z_padded = jnp.pad(middle, z_widths)
    upward = z_padded[..., 2:, :, :]
    downward = z_padded[..., :-2, :, :]
    advection = (
        x_speed * (eastward - westward) / (2.0 * x_spacing)
        + y_speed * (northward - southward) * 0.5
    )
    diffusion = h_spread * (
        (eastward - 2.0 * middle + westward) / (x_spacing * x_spacing)
        + (northward - 2.0 * middle + southward)
    )
    vertical = v_spread * (upward - 2.0 * middle + downward) / (z_spacing * z_spacing)
    tracer = lax.broadcasted_iota(jnp.int32, (2, 1, 1, 1), 0)
    own = jnp.where(tracer == 0, coupling[0, 0], coupling[1, 1])
    other = jnp.where(tracer == 0, coupling[0, 1], coupling[1, 0])
    reaction = own * middle + other * middle[::-1]
    return diffusion + vertical - advection + reaction


def pair_sum(field):
    row = lax.broadcasted_iota(jnp.int32, field.shape, field.ndim - 2)
    partner = jnp.where(
        row % 2 == 0, jnp.roll(field, -1, axis=-2), jnp.roll(field, 1, axis=-2)
    )
    return field + partner


def shrink(field):
    levels = field[..., 0::2, :, :] + field[..., 1::2, :, :]
    return pair_sum(levels) * 0.25


def expand(field):
    return jnp.repeat(field, 2, axis=-3)


def add_coarse(fine, coarse):
    shape = fine.shape
    paired = fine.reshape(shape[:-3] + (shape[-3] // 2, 2) + shape[-2:])
    return (paired + jnp.expand_dims(coarse, -3)).reshape(shape)


def pick(items, index):
    out = items[0]
    for k in range(1, len(items)):
        out = jax.tree.map(lambda new, old: jnp.where(index == k, new, old), items[k], out)
    return out


def pair_map(fn, *halos):
    return fn(*halos)


def body(initial, x_velocity, y_velocity, h_diffusion, v_diffusion, coupling):
    coarse_x = shrink(x_velocity)
    coarse_y = shrink(y_velocity)
    coarse_h = shrink(h_diffusion)
    coarse_v = shrink(v_diffusion)
    slabs = lax.axis_size("tm")
    columns = lax.axis_size("space")
    slab = lax.axis_index("tm")
    first = slab == 0

    def fine_rate(field, halo):
        return tendency(
            field, halo, x_velocity, y_velocity, h_diffusion, v_diffusion, coupling, 1.0, 1.0
        )

    def coarse_rate(field, halo):
        return tendency(field, halo, coarse_x, coarse_y, coarse_h, coarse_v, coupling, 2.0, 2.0)

    def first_node(node_zero, rate_zero, s0, s1, s2):
        return (
            node_zero
            + half_step * (rate_zero - s0)
            + slab_step * (s0 * (5.0 / 24.0) + s1 * (1.0 / 3.0) - s2 * (1.0 / 24.0))
        )

    def second_node(node_one, rate_one, s0, s1, s2):
        return (
            node_one
            + half_step * (rate_one - s1)
            + slab_step * (s0 * (-1.0 / 24.0) + s1 * (1.0 / 3.0) + s2 * (5.0 / 24.0))
        )

    coarse_first = shrink(initial)
    levels = initial.shape[-3]

    def joined(fine, coarse):
        return jnp.concatenate([fine, coarse], axis=-3)

    coarse_coefs = (coarse_x, coarse_y, coarse_h, coarse_v)
    coarse_levels = coarse_first.shape[-3]

    def coef_edge(edge):
        stacked = jnp.stack([edge(c) for c in coarse_coefs])
        return stacked.reshape((2, -1) + stacked.shape[-2:])

    before, after = exchange(
        joined(joined(hi(initial), hi(coarse_first)), coef_edge(hi)),
        joined(joined(lo(initial), lo(coarse_first)), coef_edge(lo)),
    )
    split = (levels, levels + coarse_levels)
    init_b, first_b = before[..., : split[0], :, :], before[..., split[0] : split[1], :, :]
    init_a, first_a = after[..., : split[0], :, :], after[..., split[0] : split[1], :, :]
    edge_coefs = pack(before[..., split[1] :, :, :], after[..., split[1] :, :, :])
    edge_coefs = edge_coefs.reshape((4, coarse_levels) + edge_coefs.shape[-2:])
    halo_zero = pack(init_b, init_a)
    halo_first = pack(first_b, first_a)
    first_rate = fine_rate(initial, halo_zero)
    coarse_first_rate = coarse_rate(coarse_first, halo_first)

    node_zero = initial
    rate_zero = first_rate
    node_one = first_node(node_zero, rate_zero, first_rate, first_rate, first_rate)
    halo_one = halo_of(node_one)
    rate_one = fine_rate(node_one, halo_one)
    node_two = second_node(node_one, rate_one, first_rate, first_rate, first_rate)
    two_b, two_a = exchange(hi(node_two, 2), lo(node_two, 2))
    halo_two = pack(hi(two_b), lo(two_a))
    coarse_end = shrink(node_two)
    halo_end = pack(hi(shrink(two_b)), lo(shrink(two_a)))
    rate_two = fine_rate(node_two, halo_two)
    source = shrink(slab_step * (rate_zero + 4.0 * rate_one + rate_two) / 6.0)
    offset = source - slab_step * coarse_first_rate

    chain = [coarse_first]
    chain_halo = [halo_first]
    rate = coarse_first_rate
    wide = None
    for count in range(slabs):
        after = chain[-1] + slab_step * rate + offset
        if wide is not None:
            strip_b, strip_a, offset_edge = wide
            edge = pack(strip_b[..., 2:3, :], strip_a[..., 0:1, :])
            edge_rate = stencil(
                edge,
                pack(lo(chain[-1]), strip_a[..., 2:3, :]),
                pack(strip_b[..., 0:1, :], hi(chain[-1])),
                *(edge_coefs[k] for k in range(4)),
                coupling, 2.0, 2.0,
            )
            after_halo = edge + slab_step * edge_rate + offset_edge
        elif count + 2 == slabs:
            packed_b, packed_a = exchange(
                jnp.concatenate([hi(after, 3), hi(offset)], axis=-2),
                jnp.concatenate([lo(after, 3), lo(offset)], axis=-2),
            )
            strip_b, strip_a = packed_b[..., :3, :], packed_a[..., :3, :]
            wide = (strip_b, strip_a, pack(packed_b[..., 3:, :], packed_a[..., 3:, :]))
            after_halo = pack(strip_b[..., 2:3, :], strip_a[..., 0:1, :])
        else:
            after_halo = halo_of(after)
        chain.append(after)
        chain_halo.append(after_halo)
        if count + 1 < slabs:
            rate = coarse_rate(after, after_halo)
    begins = pick(chain, slab)
    finals = pick(chain, slab + 1)
    begins_halo = pick(chain_halo, slab)
    finals_halo = pick(chain_halo, slab + 1)

    delta_zero = begins - coarse_first
    delta_one = finals - coarse_end
    fixed_zero = add_coarse(node_zero, delta_zero)
    fixed_one = add_coarse(node_one, (delta_zero + delta_one) * 0.5)
    fixed_two = add_coarse(node_two, delta_one)
    halo_dz = pair_map(lambda y, v: y - v, begins_halo, halo_first)
    halo_d1 = pair_map(lambda y, v: y - v, finals_halo, halo_end)
    halo_f0 = add_coarse(halo_zero, halo_dz)
    halo_f1 = add_coarse(halo_one, (halo_dz + halo_d1) * 0.5)
    halo_f2 = add_coarse(halo_two, halo_d1)

    earlier_delta = begins - coarse_end
    earlier_end = add_coarse(node_two, earlier_delta)
    halo_earlier_delta = pair_map(lambda y, v: y - v, begins_halo, halo_end)
    halo_earlier = add_coarse(halo_two, halo_earlier_delta)
    wide_earlier = (
        add_coarse(two_b, west(halo_earlier_delta)),
        add_coarse(two_a, east(halo_earlier_delta)),
    )
    start = jnp.where(first, initial, earlier_end)
    halo_start = pair_map(lambda a, b: jnp.where(first, a, b), halo_zero, halo_earlier)
    halo_start_coarse = jnp.where(
        first, halo_first, pack(lo(shrink(wide_earlier[0])), lo(shrink(wide_earlier[1])))
    )

    slope_zero = fine_rate(fixed_zero, halo_f0)
    slope_one = fine_rate(fixed_one, halo_f1)
    slope_two = fine_rate(fixed_two, halo_f2)
    node_zero = start
    rate_zero = fine_rate(node_zero, halo_start)
    node_one = first_node(node_zero, rate_zero, slope_zero, slope_one, slope_two)
    rate_one = fine_rate(node_one, halo_of(node_one))
    node_two = second_node(node_one, rate_one, slope_zero, slope_one, slope_two)
    rate_two = fine_rate(node_two, halo_of(node_two))
    coarse_zero = shrink(node_zero)
    coarse_end = shrink(node_two)
    source = shrink(slab_step * (rate_zero + 4.0 * rate_one + rate_two) / 6.0)
    offset = source - slab_step * coarse_rate(coarse_zero, halo_start_coarse)

    down = shift_pairs(slabs, 1)
    to_east = [
        (t * columns + c, (t + 1) * columns + c + 1)
        for t in range(slabs - 1)
        for c in range(columns - 1)
    ]
    to_west = [
        (t * columns + c, (t + 1) * columns + c - 1)
        for t in range(slabs - 1)
        for c in range(1, columns)
    ]
    carried = coarse_first
    carried_halo = halo_first
    rate = coarse_first_rate
    for count in range(slabs - 1):
        after = carried + slab_step * rate + offset
        passed = lax.ppermute(after, "tm", down)
        passed_b = lax.ppermute(hi(after), ("tm", "space"), to_east)
        passed_a = lax.ppermute(lo(after), ("tm", "space"), to_west)
        carried = jnp.where(first, coarse_first, passed)
        carried_halo = jnp.where(first, halo_first, pack(passed_b, passed_a))
        rate = coarse_rate(carried, carried_halo)
    finals = carried + slab_step * rate + offset
    result = add_coarse(node_two, finals - coarse_end)
    return result[None]


def solution(mesh):
    return jax.shard_map(
        body,
        mesh=mesh,
        in_specs=(
            P(None, None, "space", None),
            P(None, "space", None),
            P(None, "space", None),
            P(None, "space", None),
            P(None, "space", None),
            P(),
        ),
        out_specs=P("tm", None, None, "space", None),
        check_vma=False,
    )
```

```python
import jax
import jax.numpy as jnp
from jax import lax
from jax.sharding import PartitionSpec as P

ITERS = 2


slab_step = 0.5
half_step = 0.25


def shift_pairs(count, steps):
    return [(i, i + steps) for i in range(max(0, -steps), min(count, count - steps))]


def exchange(to_right, to_left):
    count = lax.axis_size("space")
    before = lax.ppermute(to_right, "space", shift_pairs(count, 1))
    after = lax.ppermute(to_left, "space", shift_pairs(count, -1))
    return before, after


def lo(field, width=1):
    return field[..., :width, :]


def hi(field, width=1):
    return field[..., field.shape[-2] - width:, :]


def pack(before, after):
    return jnp.concatenate([before, after], axis=-2)


def west(halo):
    return halo[..., 0:1, :]


def east(halo):
    return halo[..., 1:2, :]


def halo_of(field):
    return pack(*exchange(hi(field), lo(field)))


def tendency(field, halo, x_speed, y_speed, h_spread, v_spread, coupling, x_spacing, z_spacing):
    reach = int(x_spacing)
    padded = jnp.concatenate([west(halo)] * reach + [field] + [east(halo)] * reach, axis=-2)
    width = field.shape[-2]
    return stencil(
        field, padded[..., 2 * reach:, :], padded[..., :width, :],
        x_speed, y_speed, h_spread, v_spread, coupling, x_spacing, z_spacing,
    )


def stencil(middle, eastward, westward, x_speed, y_speed, h_spread, v_spread, coupling,
            x_spacing, z_spacing):
    y_widths = [(0, 0)] * (middle.ndim - 1) + [(1, 1)]
    y_padded = jnp.pad(middle, y_widths)
    northward = y_padded[..., 2:]
    southward = y_padded[..., :-2]
    z_widths = [(0, 0)] * (middle.ndim - 3) + [(1, 1), (0, 0), (0, 0)]
    z_padded = jnp.pad(middle, z_widths)
    upward = z_padded[..., 2:, :, :]
    downward = z_padded[..., :-2, :, :]
    advection = (
        x_speed * (eastward - westward) / (2.0 * x_spacing)
        + y_speed * (northward - southward) * 0.5
    )
    diffusion = h_spread * (
        (eastward - 2.0 * middle + westward) / (x_spacing * x_spacing)
        + (northward - 2.0 * middle + southward)
    )
    vertical = v_spread * (upward - 2.0 * middle + downward) / (z_spacing * z_spacing)
    tracer = lax.broadcasted_iota(jnp.int32, (2, 1, 1, 1), 0)
    own = jnp.where(tracer == 0, coupling[0, 0], coupling[1, 1])
    other = jnp.where(tracer == 0, coupling[0, 1], coupling[1, 0])
    reaction = own * middle + other * middle[::-1]
    return diffusion + vertical - advection + reaction


def pair_sum(field):
    row = lax.broadcasted_iota(jnp.int32, field.shape, field.ndim - 2)
    partner = jnp.where(
        row % 2 == 0, jnp.roll(field, -1, axis=-2), jnp.roll(field, 1, axis=-2)
    )
    return field + partner


def shrink(field):
    levels = field[..., 0::2, :, :] + field[..., 1::2, :, :]
    return pair_sum(levels) * 0.25


def expand(field):
    return jnp.repeat(field, 2, axis=-3)


def add_coarse(fine, coarse):
    shape = fine.shape
    paired = fine.reshape(shape[:-3] + (shape[-3] // 2, 2) + shape[-2:])
    return (paired + jnp.expand_dims(coarse, -3)).reshape(shape)


def pick(items, index):
    out = items[0]
    for k in range(1, len(items)):
        out = jax.tree.map(lambda new, old: jnp.where(index == k, new, old), items[k], out)
    return out


def pair_map(fn, *halos):
    return fn(*halos)


def body(initial, x_velocity, y_velocity, h_diffusion, v_diffusion, coupling):
    coarse_x = shrink(x_velocity)
    coarse_y = shrink(y_velocity)
    coarse_h = shrink(h_diffusion)
    coarse_v = shrink(v_diffusion)
    slabs = lax.axis_size("tm")
    columns = lax.axis_size("space")
    slab = lax.axis_index("tm")
    first = slab == 0

    def fine_rate(field, halo):
        return tendency(
            field, halo, x_velocity, y_velocity, h_diffusion, v_diffusion, coupling, 1.0, 1.0
        )

    def coarse_rate(field, halo):
        return tendency(field, halo, coarse_x, coarse_y, coarse_h, coarse_v, coupling, 2.0, 2.0)

    def first_node(node_zero, rate_zero, s0, s1, s2):
        return (
            node_zero
            + half_step * (rate_zero - s0)
            + slab_step * (s0 * (5.0 / 24.0) + s1 * (1.0 / 3.0) - s2 * (1.0 / 24.0))
        )

    def second_node(node_one, rate_one, s0, s1, s2):
        return (
            node_one
            + half_step * (rate_one - s1)
            + slab_step * (s0 * (-1.0 / 24.0) + s1 * (1.0 / 3.0) + s2 * (5.0 / 24.0))
        )

    coarse_first = shrink(initial)
    levels = initial.shape[-3]

    def joined(fine, coarse):
        return jnp.concatenate([fine, coarse], axis=-3)

    coarse_coefs = (coarse_x, coarse_y, coarse_h, coarse_v)
    coarse_levels = coarse_first.shape[-3]

    def coef_edge(edge):
        stacked = jnp.stack([edge(c) for c in coarse_coefs])
        return stacked.reshape((2, -1) + stacked.shape[-2:])

    before, after = exchange(
        joined(joined(hi(initial), hi(coarse_first)), coef_edge(hi)),
        joined(joined(lo(initial), lo(coarse_first)), coef_edge(lo)),
    )
    split = (levels, levels + coarse_levels)
    init_b, first_b = before[..., : split[0], :, :], before[..., split[0] : split[1], :, :]
    init_a, first_a = after[..., : split[0], :, :], after[..., split[0] : split[1], :, :]
    edge_coefs = pack(before[..., split[1] :, :, :], after[..., split[1] :, :, :])
    edge_coefs = edge_coefs.reshape((4, coarse_levels) + edge_coefs.shape[-2:])
    halo_zero = pack(init_b, init_a)
    halo_first = pack(first_b, first_a)
    first_rate = fine_rate(initial, halo_zero)
    coarse_first_rate = coarse_rate(coarse_first, halo_first)

    node_zero = initial
    rate_zero = first_rate
    node_one = first_node(node_zero, rate_zero, first_rate, first_rate, first_rate)
    halo_one = halo_of(node_one)
    rate_one = fine_rate(node_one, halo_one)
    node_two = second_node(node_one, rate_one, first_rate, first_rate, first_rate)
    two_b, two_a = exchange(hi(node_two, 2), lo(node_two, 2))
    halo_two = pack(hi(two_b), lo(two_a))
    coarse_end = shrink(node_two)
    halo_end = pack(hi(shrink(two_b)), lo(shrink(two_a)))
    rate_two = fine_rate(node_two, halo_two)
    source = shrink(slab_step * (rate_zero + 4.0 * rate_one + rate_two) / 6.0)
    offset = source - slab_step * coarse_first_rate

    chain = [coarse_first]
    chain_halo = [halo_first]
    rate = coarse_first_rate
    rates = [rate]
    wide = None
    for count in range(slabs):
        after = chain[-1] + slab_step * rate + offset
        if wide is not None:
            strip_b, strip_a, offset_edge = wide
            edge = pack(strip_b[..., 2:3, :], strip_a[..., 0:1, :])
            edge_rate = stencil(
                edge,
                pack(lo(chain[-1]), strip_a[..., 2:3, :]),
                pack(strip_b[..., 0:1, :], hi(chain[-1])),
                *(edge_coefs[k] for k in range(4)),
                coupling, 2.0, 2.0,
            )
            after_halo = edge + slab_step * edge_rate + offset_edge
        elif count + 2 == slabs:
            packed_b, packed_a = exchange(
                jnp.concatenate([hi(after, 3), hi(offset)], axis=-2),
                jnp.concatenate([lo(after, 3), lo(offset)], axis=-2),
            )
            strip_b, strip_a = packed_b[..., :3, :], packed_a[..., :3, :]
            wide = (strip_b, strip_a, pack(packed_b[..., 3:, :], packed_a[..., 3:, :]))
            after_halo = pack(strip_b[..., 2:3, :], strip_a[..., 0:1, :])
        else:
            after_halo = halo_of(after)
        chain.append(after)
        chain_halo.append(after_halo)
        if count + 1 < slabs:
            rate = coarse_rate(after, after_halo)
            rates.append(rate)
    begins = pick(chain, slab)
    finals = pick(chain, slab + 1)
    begins_halo = pick(chain_halo, slab)
    finals_halo = pick(chain_halo, slab + 1)

    delta_zero = begins - coarse_first
    delta_one = finals - coarse_end
    fixed_zero = add_coarse(node_zero, delta_zero)
    fixed_one = add_coarse(node_one, (delta_zero + delta_one) * 0.5)
    fixed_two = add_coarse(node_two, delta_one)
    halo_dz = pair_map(lambda y, v: y - v, begins_halo, halo_first)
    halo_d1 = pair_map(lambda y, v: y - v, finals_halo, halo_end)
    halo_f0 = add_coarse(halo_zero, halo_dz)
    halo_f1 = add_coarse(halo_one, (halo_dz + halo_d1) * 0.5)
    halo_f2 = add_coarse(halo_two, halo_d1)

    earlier_delta = begins - coarse_end
    earlier_end = add_coarse(node_two, earlier_delta)
    halo_earlier_delta = pair_map(lambda y, v: y - v, begins_halo, halo_end)
    halo_earlier = add_coarse(halo_two, halo_earlier_delta)
    start = jnp.where(first, initial, earlier_end)
    halo_start = pair_map(lambda a, b: jnp.where(first, a, b), halo_zero, halo_earlier)
    start_rate = pick(rates, slab)

    slope_zero = fine_rate(fixed_zero, halo_f0)
    slope_one = fine_rate(fixed_one, halo_f1)
    slope_two = fine_rate(fixed_two, halo_f2)
    node_zero = start
    rate_zero = fine_rate(node_zero, halo_start)
    node_one = first_node(node_zero, rate_zero, slope_zero, slope_one, slope_two)
    rate_one = fine_rate(node_one, halo_of(node_one))
    node_two = second_node(node_one, rate_one, slope_zero, slope_one, slope_two)
    rate_two = fine_rate(node_two, halo_of(node_two))
    coarse_end = shrink(node_two)
    source = shrink(slab_step * (rate_zero + 4.0 * rate_one + rate_two) / 6.0)
    offset = source - slab_step * start_rate

    down = shift_pairs(slabs, 1)
    to_east = [
        (t * columns + c, (t + 1) * columns + c + 1)
        for t in range(slabs - 1)
        for c in range(columns - 1)
    ]
    to_west = [
        (t * columns + c, (t + 1) * columns + c - 1)
        for t in range(slabs - 1)
        for c in range(1, columns)
    ]
    carried = coarse_first
    carried_halo = halo_first
    rate = coarse_first_rate
    for count in range(slabs - 1):
        after = carried + slab_step * rate + offset
        passed = lax.ppermute(after, "tm", down)
        passed_b = lax.ppermute(hi(after), ("tm", "space"), to_east)
        passed_a = lax.ppermute(lo(after), ("tm", "space"), to_west)
        carried = jnp.where(first, coarse_first, passed)
        carried_halo = jnp.where(first, halo_first, pack(passed_b, passed_a))
        rate = coarse_rate(carried, carried_halo)
    finals = carried + slab_step * rate + offset
    result = add_coarse(node_two, finals - coarse_end)
    return result[None]


def solution(mesh):
    return jax.shard_map(
        body,
        mesh=mesh,
        in_specs=(
            P(None, None, "space", None),
            P(None, "space", None),
            P(None, "space", None),
            P(None, "space", None),
            P(None, "space", None),
            P(),
        ),
        out_specs=P("tm", None, None, "space", None),
        check_vma=False,
    )
```

```python
import jax
import jax.numpy as jnp
from jax import lax
from jax.sharding import PartitionSpec as P

ITERS = 2


slab_step = 0.5
half_step = 0.25


def shift_pairs(count, steps):
    return [(i, i + steps) for i in range(max(0, -steps), min(count, count - steps))]


def exchange(to_right, to_left):
    count = lax.axis_size("space")
    before = lax.ppermute(to_right, "space", shift_pairs(count, 1))
    after = lax.ppermute(to_left, "space", shift_pairs(count, -1))
    return before, after


def lo(field, width=1):
    return field[..., :width, :]


def hi(field, width=1):
    return field[..., field.shape[-2] - width:, :]


def pack(before, after):
    return jnp.concatenate([before, after], axis=-2)


def west(halo):
    return halo[..., 0:1, :]


def east(halo):
    return halo[..., 1:2, :]


def halo_of(field):
    return pack(*exchange(hi(field), lo(field)))


def tendency(field, halo, x_speed, y_speed, h_spread, v_spread, coupling, x_spacing, z_spacing):
    reach = int(x_spacing)
    padded = jnp.concatenate([west(halo)] * reach + [field] + [east(halo)] * reach, axis=-2)
    width = field.shape[-2]
    return stencil(
        field, padded[..., 2 * reach:, :], padded[..., :width, :],
        x_speed, y_speed, h_spread, v_spread, coupling, x_spacing, z_spacing,
    )


def stencil(middle, eastward, westward, x_speed, y_speed, h_spread, v_spread, coupling,
            x_spacing, z_spacing):
    y_widths = [(0, 0)] * (middle.ndim - 1) + [(1, 1)]
    y_padded = jnp.pad(middle, y_widths)
    northward = y_padded[..., 2:]
    southward = y_padded[..., :-2]
    z_widths = [(0, 0)] * (middle.ndim - 3) + [(1, 1), (0, 0), (0, 0)]
    z_padded = jnp.pad(middle, z_widths)
    upward = z_padded[..., 2:, :, :]
    downward = z_padded[..., :-2, :, :]
    advection = (
        x_speed * (eastward - westward) / (2.0 * x_spacing)
        + y_speed * (northward - southward) * 0.5
    )
    diffusion = h_spread * (
        (eastward - 2.0 * middle + westward) / (x_spacing * x_spacing)
        + (northward - 2.0 * middle + southward)
    )
    vertical = v_spread * (upward - 2.0 * middle + downward) / (z_spacing * z_spacing)
    tracer = lax.broadcasted_iota(jnp.int32, (2, 1, 1, 1), 0)
    own = jnp.where(tracer == 0, coupling[0, 0], coupling[1, 1])
    other = jnp.where(tracer == 0, coupling[0, 1], coupling[1, 0])
    reaction = own * middle + other * middle[::-1]
    return diffusion + vertical - advection + reaction


def pair_sum(field):
    row = lax.broadcasted_iota(jnp.int32, field.shape, field.ndim - 2)
    partner = jnp.where(
        row % 2 == 0, jnp.roll(field, -1, axis=-2), jnp.roll(field, 1, axis=-2)
    )
    return field + partner


def shrink(field):
    levels = field[..., 0::2, :, :] + field[..., 1::2, :, :]
    return pair_sum(levels) * 0.25


def expand(field):
    return jnp.repeat(field, 2, axis=-3)


def add_coarse(fine, coarse):
    shape = fine.shape
    paired = fine.reshape(shape[:-3] + (shape[-3] // 2, 2) + shape[-2:])
    return (paired + jnp.expand_dims(coarse, -3)).reshape(shape)


def pick(items, index):
    out = items[0]
    for k in range(1, len(items)):
        out = jax.tree.map(lambda new, old: jnp.where(index == k, new, old), items[k], out)
    return out


def pair_map(fn, *halos):
    return fn(*halos)


def body(initial, x_velocity, y_velocity, h_diffusion, v_diffusion, coupling):
    coarse_x = shrink(x_velocity)
    coarse_y = shrink(y_velocity)
    coarse_h = shrink(h_diffusion)
    coarse_v = shrink(v_diffusion)
    slabs = lax.axis_size("tm")
    columns = lax.axis_size("space")
    slab = lax.axis_index("tm")
    first = slab == 0

    def fine_rate(field, halo):
        return tendency(
            field, halo, x_velocity, y_velocity, h_diffusion, v_diffusion, coupling, 1.0, 1.0
        )

    def coarse_rate(field, halo):
        return tendency(field, halo, coarse_x, coarse_y, coarse_h, coarse_v, coupling, 2.0, 2.0)

    def first_node(node_zero, rate_zero, s0, s1, s2):
        return (
            node_zero
            + half_step * (rate_zero - s0)
            + slab_step * (s0 * (5.0 / 24.0) + s1 * (1.0 / 3.0) - s2 * (1.0 / 24.0))
        )

    def second_node(node_one, rate_one, s0, s1, s2):
        return (
            node_one
            + half_step * (rate_one - s1)
            + slab_step * (s0 * (-1.0 / 24.0) + s1 * (1.0 / 3.0) + s2 * (5.0 / 24.0))
        )

    coarse_first = shrink(initial)
    levels = initial.shape[-3]

    def joined(fine, coarse):
        return jnp.concatenate([fine, coarse], axis=-3)

    coarse_coefs = (coarse_x, coarse_y, coarse_h, coarse_v)
    coarse_levels = coarse_first.shape[-3]

    def coef_edge(edge):
        stacked = jnp.stack([edge(c) for c in coarse_coefs])
        return stacked.reshape((2, -1) + stacked.shape[-2:])

    before, after = exchange(
        joined(joined(hi(initial), hi(coarse_first)), coef_edge(hi)),
        joined(joined(lo(initial), lo(coarse_first)), coef_edge(lo)),
    )
    split = (levels, levels + coarse_levels)
    init_b, first_b = before[..., : split[0], :, :], before[..., split[0] : split[1], :, :]
    init_a, first_a = after[..., : split[0], :, :], after[..., split[0] : split[1], :, :]
    edge_coefs = pack(before[..., split[1] :, :, :], after[..., split[1] :, :, :])
    edge_coefs = edge_coefs.reshape((4, coarse_levels) + edge_coefs.shape[-2:])
    halo_zero = pack(init_b, init_a)
    halo_first = pack(first_b, first_a)
    first_rate = fine_rate(initial, halo_zero)
    coarse_first_rate = coarse_rate(coarse_first, halo_first)

    node_zero = initial
    rate_zero = first_rate
    node_one = first_node(node_zero, rate_zero, first_rate, first_rate, first_rate)
    halo_one = halo_of(node_one)
    rate_one = fine_rate(node_one, halo_one)
    node_two = second_node(node_one, rate_one, first_rate, first_rate, first_rate)
    two_b, two_a = exchange(hi(node_two, 2), lo(node_two, 2))
    halo_two = pack(hi(two_b), lo(two_a))
    coarse_end = shrink(node_two)
    halo_end = pack(hi(shrink(two_b)), lo(shrink(two_a)))
    rate_two = fine_rate(node_two, halo_two)
    source = shrink(slab_step * (rate_zero + 4.0 * rate_one + rate_two) / 6.0)
    offset = source - slab_step * coarse_first_rate

    chain = [coarse_first]
    chain_halo = [halo_first]
    rate = coarse_first_rate
    rates = [rate]
    wide = None
    for count in range(slabs):
        after = chain[-1] + slab_step * rate + offset
        if wide is not None:
            strip_b, strip_a, offset_edge = wide
            edge = pack(strip_b[..., 2:3, :], strip_a[..., 0:1, :])
            edge_rate = stencil(
                edge,
                pack(lo(chain[-1]), strip_a[..., 2:3, :]),
                pack(strip_b[..., 0:1, :], hi(chain[-1])),
                *(edge_coefs[k] for k in range(4)),
                coupling, 2.0, 2.0,
            )
            after_halo = edge + slab_step * edge_rate + offset_edge
        elif count + 2 == slabs:
            packed_b, packed_a = exchange(
                jnp.concatenate([hi(after, 3), hi(offset)], axis=-2),
                jnp.concatenate([lo(after, 3), lo(offset)], axis=-2),
            )
            strip_b, strip_a = packed_b[..., :3, :], packed_a[..., :3, :]
            wide = (strip_b, strip_a, pack(packed_b[..., 3:, :], packed_a[..., 3:, :]))
            after_halo = pack(strip_b[..., 2:3, :], strip_a[..., 0:1, :])
        else:
            after_halo = halo_of(after)
        chain.append(after)
        chain_halo.append(after_halo)
        if count + 1 < slabs:
            rate = coarse_rate(after, after_halo)
            rates.append(rate)
    begins = pick(chain, slab)
    finals = pick(chain, slab + 1)
    begins_halo = pick(chain_halo, slab)
    finals_halo = pick(chain_halo, slab + 1)

    delta_zero = begins - coarse_first
    delta_one = finals - coarse_end
    fixed_zero = add_coarse(node_zero, delta_zero)
    fixed_one = add_coarse(node_one, (delta_zero + delta_one) * 0.5)
    fixed_two = add_coarse(node_two, delta_one)
    halo_dz = pair_map(lambda y, v: y - v, begins_halo, halo_first)
    halo_d1 = pair_map(lambda y, v: y - v, finals_halo, halo_end)
    halo_f0 = add_coarse(halo_zero, halo_dz)
    halo_f1 = add_coarse(halo_one, (halo_dz + halo_d1) * 0.5)
    halo_f2 = add_coarse(halo_two, halo_d1)

    earlier_delta = begins - coarse_end
    earlier_end = add_coarse(node_two, earlier_delta)
    halo_earlier_delta = pair_map(lambda y, v: y - v, begins_halo, halo_end)
    halo_earlier = add_coarse(halo_two, halo_earlier_delta)
    start = jnp.where(first, initial, earlier_end)
    halo_start = pair_map(lambda a, b: jnp.where(first, a, b), halo_zero, halo_earlier)
    start_rate = pick(rates, slab)

    def combined(c0, c1, c2):
        return lambda u0, u1, u2: c0 * u0 + c1 * u1 + c2 * u2

    to_one = combined(-7.0 / 48.0, 1.0 / 6.0, -1.0 / 48.0)
    to_two = combined(-1.0 / 48.0, -1.0 / 12.0, 5.0 / 48.0)
    slopes_one = fine_rate(
        to_one(fixed_zero, fixed_one, fixed_two), to_one(halo_f0, halo_f1, halo_f2)
    )
    slopes_two = fine_rate(
        to_two(fixed_zero, fixed_one, fixed_two), to_two(halo_f0, halo_f1, halo_f2)
    )
    node_zero = start
    rate_zero = fine_rate(node_zero, halo_start)
    node_one = node_zero + half_step * rate_zero + slopes_one
    rate_one = fine_rate(node_one, halo_of(node_one))
    node_two = node_one + half_step * rate_one + slopes_two
    rate_two = fine_rate(node_two, halo_of(node_two))
    coarse_end = shrink(node_two)
    source = shrink(slab_step * (rate_zero + 4.0 * rate_one + rate_two) / 6.0)
    offset = source - slab_step * start_rate

    down = shift_pairs(slabs, 1)
    to_east = [
        (t * columns + c, (t + 1) * columns + c + 1)
        for t in range(slabs - 1)
        for c in range(columns - 1)
    ]
    to_west = [
        (t * columns + c, (t + 1) * columns + c - 1)
        for t in range(slabs - 1)
        for c in range(1, columns)
    ]
    carried = coarse_first
    carried_halo = halo_first
    rate = coarse_first_rate
    for count in range(slabs - 1):
        after = carried + slab_step * rate + offset
        passed = lax.ppermute(after, "tm", down)
        passed_b = lax.ppermute(hi(after), ("tm", "space"), to_east)
        passed_a = lax.ppermute(lo(after), ("tm", "space"), to_west)
        carried = jnp.where(first, coarse_first, passed)
        carried_halo = jnp.where(first, halo_first, pack(passed_b, passed_a))
        rate = coarse_rate(carried, carried_halo)
    finals = carried + slab_step * rate + offset
    result = add_coarse(node_two, finals - coarse_end)
    return result[None]


def solution(mesh):
    return jax.shard_map(
        body,
        mesh=mesh,
        in_specs=(
            P(None, None, "space", None),
            P(None, "space", None),
            P(None, "space", None),
            P(None, "space", None),
            P(None, "space", None),
            P(),
        ),
        out_specs=P("tm", None, None, "space", None),
        check_vma=False,
    )
```

```python
import jax
import jax.numpy as jnp
from jax import lax
from jax.sharding import PartitionSpec as P

ITERS = 2


slab_step = 0.5
half_step = 0.25


def shift_pairs(count, steps):
    return [(i, i + steps) for i in range(max(0, -steps), min(count, count - steps))]


def exchange(to_right, to_left):
    count = lax.axis_size("space")
    before = lax.ppermute(to_right, "space", shift_pairs(count, 1))
    after = lax.ppermute(to_left, "space", shift_pairs(count, -1))
    return before, after


def lo(field, width=1):
    return field[..., :width, :]


def hi(field, width=1):
    return field[..., field.shape[-2] - width:, :]


def pack(before, after):
    return jnp.concatenate([before, after], axis=-2)


def west(halo):
    return halo[..., 0:1, :]


def east(halo):
    return halo[..., 1:2, :]


def halo_of(field):
    return pack(*exchange(hi(field), lo(field)))


def tendency(field, halo, x_speed, y_speed, h_spread, v_spread, coupling, x_spacing, z_spacing):
    reach = int(x_spacing)
    padded = jnp.concatenate([west(halo)] * reach + [field] + [east(halo)] * reach, axis=-2)
    width = field.shape[-2]
    return stencil(
        field, padded[..., 2 * reach:, :], padded[..., :width, :],
        x_speed, y_speed, h_spread, v_spread, coupling, x_spacing, z_spacing,
    )


def stencil(middle, eastward, westward, x_speed, y_speed, h_spread, v_spread, coupling,
            x_spacing, z_spacing):
    y_widths = [(0, 0)] * (middle.ndim - 1) + [(1, 1)]
    y_padded = jnp.pad(middle, y_widths)
    northward = y_padded[..., 2:]
    southward = y_padded[..., :-2]
    z_widths = [(0, 0)] * (middle.ndim - 3) + [(1, 1), (0, 0), (0, 0)]
    z_padded = jnp.pad(middle, z_widths)
    upward = z_padded[..., 2:, :, :]
    downward = z_padded[..., :-2, :, :]
    advection = (
        x_speed * (eastward - westward) / (2.0 * x_spacing)
        + y_speed * (northward - southward) * 0.5
    )
    diffusion = h_spread * (
        (eastward - 2.0 * middle + westward) / (x_spacing * x_spacing)
        + (northward - 2.0 * middle + southward)
    )
    vertical = v_spread * (upward - 2.0 * middle + downward) / (z_spacing * z_spacing)
    tracer = lax.broadcasted_iota(jnp.int32, (2, 1, 1, 1), 0)
    own = jnp.where(tracer == 0, coupling[0, 0], coupling[1, 1])
    other = jnp.where(tracer == 0, coupling[0, 1], coupling[1, 0])
    reaction = own * middle + other * middle[::-1]
    return diffusion + vertical - advection + reaction


def pair_sum(field):
    row = lax.broadcasted_iota(jnp.int32, field.shape, field.ndim - 2)
    partner = jnp.where(
        row % 2 == 0, jnp.roll(field, -1, axis=-2), jnp.roll(field, 1, axis=-2)
    )
    return field + partner


def shrink(field):
    levels = field[..., 0::2, :, :] + field[..., 1::2, :, :]
    return pair_sum(levels) * 0.25


def expand(field):
    return jnp.repeat(field, 2, axis=-3)


def add_coarse(fine, coarse):
    shape = fine.shape
    paired = fine.reshape(shape[:-3] + (shape[-3] // 2, 2) + shape[-2:])
    return (paired + jnp.expand_dims(coarse, -3)).reshape(shape)


def pick(items, index):
    out = items[0]
    for k in range(1, len(items)):
        out = jax.tree.map(lambda new, old: jnp.where(index == k, new, old), items[k], out)
    return out


def pair_map(fn, *halos):
    return fn(*halos)


def body(initial, x_velocity, y_velocity, h_diffusion, v_diffusion, coupling):
    coarse_x = shrink(x_velocity)
    coarse_y = shrink(y_velocity)
    coarse_h = shrink(h_diffusion)
    coarse_v = shrink(v_diffusion)
    slabs = lax.axis_size("tm")
    columns = lax.axis_size("space")
    slab = lax.axis_index("tm")
    first = slab == 0

    def fine_rate(field, halo):
        return tendency(
            field, halo, x_velocity, y_velocity, h_diffusion, v_diffusion, coupling, 1.0, 1.0
        )

    def coarse_rate(field, halo):
        return tendency(field, halo, coarse_x, coarse_y, coarse_h, coarse_v, coupling, 2.0, 2.0)

    def first_node(node_zero, rate_zero, s0, s1, s2):
        return (
            node_zero
            + half_step * (rate_zero - s0)
            + slab_step * (s0 * (5.0 / 24.0) + s1 * (1.0 / 3.0) - s2 * (1.0 / 24.0))
        )

    def second_node(node_one, rate_one, s0, s1, s2):
        return (
            node_one
            + half_step * (rate_one - s1)
            + slab_step * (s0 * (-1.0 / 24.0) + s1 * (1.0 / 3.0) + s2 * (5.0 / 24.0))
        )

    coarse_first = shrink(initial)
    levels = initial.shape[-3]

    def joined(fine, coarse):
        return jnp.concatenate([fine, coarse], axis=-3)

    coarse_coefs = (coarse_x, coarse_y, coarse_h, coarse_v)
    coarse_levels = coarse_first.shape[-3]

    def coef_edge(edge):
        stacked = jnp.stack([edge(c) for c in coarse_coefs])
        return stacked.reshape((2, -1) + stacked.shape[-2:])

    before, after = exchange(
        joined(joined(hi(initial), hi(coarse_first)), coef_edge(hi)),
        joined(joined(lo(initial), lo(coarse_first)), coef_edge(lo)),
    )
    split = (levels, levels + coarse_levels)
    init_b, first_b = before[..., : split[0], :, :], before[..., split[0] : split[1], :, :]
    init_a, first_a = after[..., : split[0], :, :], after[..., split[0] : split[1], :, :]
    edge_coefs = pack(before[..., split[1] :, :, :], after[..., split[1] :, :, :])
    edge_coefs = edge_coefs.reshape((4, coarse_levels) + edge_coefs.shape[-2:])
    halo_zero = pack(init_b, init_a)
    halo_first = pack(first_b, first_a)
    first_rate = fine_rate(initial, halo_zero)
    coarse_first_rate = coarse_rate(coarse_first, halo_first)

    node_zero = initial
    rate_zero = first_rate
    node_one = first_node(node_zero, rate_zero, first_rate, first_rate, first_rate)
    halo_one = halo_of(node_one)
    rate_one = fine_rate(node_one, halo_one)
    node_two = second_node(node_one, rate_one, first_rate, first_rate, first_rate)
    two_b, two_a = exchange(hi(node_two, 2), lo(node_two, 2))
    halo_two = pack(hi(two_b), lo(two_a))
    coarse_end = shrink(node_two)
    halo_end = pack(hi(shrink(two_b)), lo(shrink(two_a)))
    rate_two = fine_rate(node_two, halo_two)
    source = shrink(slab_step * (rate_zero + 4.0 * rate_one + rate_two) / 6.0)
    offset = source - slab_step * coarse_first_rate

    chain = [coarse_first]
    chain_halo = [halo_first]
    rate = coarse_first_rate
    rates = [rate]
    wide = None
    for count in range(slabs):
        after = chain[-1] + slab_step * rate + offset
        if wide is not None:
            strip_b, strip_a, offset_edge = wide
            edge = pack(strip_b[..., 2:3, :], strip_a[..., 0:1, :])
            edge_rate = stencil(
                edge,
                pack(lo(chain[-1]), strip_a[..., 2:3, :]),
                pack(strip_b[..., 0:1, :], hi(chain[-1])),
                *(edge_coefs[k] for k in range(4)),
                coupling, 2.0, 2.0,
            )
            after_halo = edge + slab_step * edge_rate + offset_edge
        elif count + 2 == slabs:
            packed_b, packed_a = exchange(
                jnp.concatenate([hi(after, 3), hi(offset)], axis=-2),
                jnp.concatenate([lo(after, 3), lo(offset)], axis=-2),
            )
            strip_b, strip_a = packed_b[..., :3, :], packed_a[..., :3, :]
            wide = (strip_b, strip_a, pack(packed_b[..., 3:, :], packed_a[..., 3:, :]))
            after_halo = pack(strip_b[..., 2:3, :], strip_a[..., 0:1, :])
        else:
            after_halo = halo_of(after)
        chain.append(after)
        chain_halo.append(after_halo)
        if count + 1 < slabs:
            rate = coarse_rate(after, after_halo)
            rates.append(rate)
    begins = pick(chain, slab)
    finals = pick(chain, slab + 1)
    begins_halo = pick(chain_halo, slab)
    finals_halo = pick(chain_halo, slab + 1)

    delta_zero = begins - coarse_first
    delta_one = finals - coarse_end
    fixed_zero = add_coarse(node_zero, delta_zero)
    fixed_one = add_coarse(node_one, (delta_zero + delta_one) * 0.5)
    fixed_two = add_coarse(node_two, delta_one)
    halo_dz = pair_map(lambda y, v: y - v, begins_halo, halo_first)
    halo_d1 = pair_map(lambda y, v: y - v, finals_halo, halo_end)
    halo_f0 = add_coarse(halo_zero, halo_dz)
    halo_f1 = add_coarse(halo_one, (halo_dz + halo_d1) * 0.5)
    halo_f2 = add_coarse(halo_two, halo_d1)

    earlier_delta = begins - coarse_end
    earlier_end = add_coarse(node_two, earlier_delta)
    halo_earlier_delta = pair_map(lambda y, v: y - v, begins_halo, halo_end)
    halo_earlier = add_coarse(halo_two, halo_earlier_delta)
    start = jnp.where(first, initial, earlier_end)
    halo_start = pair_map(lambda a, b: jnp.where(first, a, b), halo_zero, halo_earlier)
    start_rate = pick(rates, slab)

    def combined(c0, c1, c2):
        return lambda u0, u1, u2: c0 * u0 + c1 * u1 + c2 * u2

    to_one = combined(-7.0 / 48.0, 1.0 / 6.0, -1.0 / 48.0)
    to_two = combined(-1.0 / 48.0, -1.0 / 12.0, 5.0 / 48.0)
    node_zero = start
    node_one = node_zero + fine_rate(
        half_step * node_zero + to_one(fixed_zero, fixed_one, fixed_two),
        half_step * halo_start + to_one(halo_f0, halo_f1, halo_f2),
    )
    halo_one = halo_of(node_one)
    node_two = node_one + fine_rate(
        half_step * node_one + to_two(fixed_zero, fixed_one, fixed_two),
        half_step * halo_one + to_two(halo_f0, halo_f1, halo_f2),
    )
    halo_two = halo_of(node_two)
    coarse_end = shrink(node_two)
    quadrature = fine_rate(
        node_zero + 4.0 * node_one + node_two, halo_start + 4.0 * halo_one + halo_two
    )
    source = shrink(slab_step * quadrature / 6.0)
    offset = source - slab_step * start_rate

    down = shift_pairs(slabs, 1)
    to_east = [
        (t * columns + c, (t + 1) * columns + c + 1)
        for t in range(slabs - 1)
        for c in range(columns - 1)
    ]
    to_west = [
        (t * columns + c, (t + 1) * columns + c - 1)
        for t in range(slabs - 1)
        for c in range(1, columns)
    ]
    carried = coarse_first
    carried_halo = halo_first
    rate = coarse_first_rate
    for count in range(slabs - 1):
        after = carried + slab_step * rate + offset
        passed = lax.ppermute(after, "tm", down)
        passed_b = lax.ppermute(hi(after), ("tm", "space"), to_east)
        passed_a = lax.ppermute(lo(after), ("tm", "space"), to_west)
        carried = jnp.where(first, coarse_first, passed)
        carried_halo = jnp.where(first, halo_first, pack(passed_b, passed_a))
        rate = coarse_rate(carried, carried_halo)
    finals = carried + slab_step * rate + offset
    result = add_coarse(node_two, finals - coarse_end)
    return result[None]


def solution(mesh):
    return jax.shard_map(
        body,
        mesh=mesh,
        in_specs=(
            P(None, None, "space", None),
            P(None, "space", None),
            P(None, "space", None),
            P(None, "space", None),
            P(None, "space", None),
            P(),
        ),
        out_specs=P("tm", None, None, "space", None),
        check_vma=False,
    )
```

```python
import jax
import jax.numpy as jnp
from jax import lax
from jax.sharding import PartitionSpec as P

ITERS = 2


slab_step = 0.5
half_step = 0.25


def shift_pairs(count, steps):
    return [(i, i + steps) for i in range(max(0, -steps), min(count, count - steps))]


def exchange(to_right, to_left):
    count = lax.axis_size("space")
    before = lax.ppermute(to_right, "space", shift_pairs(count, 1))
    after = lax.ppermute(to_left, "space", shift_pairs(count, -1))
    return before, after


def lo(field, width=1):
    return field[..., :width, :]


def hi(field, width=1):
    return field[..., field.shape[-2] - width:, :]


def pack(before, after):
    return jnp.concatenate([before, after], axis=-2)


def west(halo):
    return halo[..., 0:1, :]


def east(halo):
    return halo[..., 1:2, :]


def halo_of(field):
    return pack(*exchange(hi(field), lo(field)))


def tendency(field, halo, x_speed, y_speed, h_spread, v_spread, coupling, x_spacing, z_spacing):
    reach = int(x_spacing)
    padded = jnp.concatenate([west(halo)] * reach + [field] + [east(halo)] * reach, axis=-2)
    width = field.shape[-2]
    return stencil(
        field, padded[..., 2 * reach:, :], padded[..., :width, :],
        x_speed, y_speed, h_spread, v_spread, coupling, x_spacing, z_spacing,
    )


def stencil(middle, eastward, westward, x_speed, y_speed, h_spread, v_spread, coupling,
            x_spacing, z_spacing):
    y_widths = [(0, 0)] * (middle.ndim - 1) + [(1, 1)]
    y_padded = jnp.pad(middle, y_widths)
    northward = y_padded[..., 2:]
    southward = y_padded[..., :-2]
    z_widths = [(0, 0)] * (middle.ndim - 3) + [(1, 1), (0, 0), (0, 0)]
    z_padded = jnp.pad(middle, z_widths)
    upward = z_padded[..., 2:, :, :]
    downward = z_padded[..., :-2, :, :]
    advection = (
        x_speed * (eastward - westward) / (2.0 * x_spacing)
        + y_speed * (northward - southward) * 0.5
    )
    diffusion = h_spread * (
        (eastward - 2.0 * middle + westward) / (x_spacing * x_spacing)
        + (northward - 2.0 * middle + southward)
    )
    vertical = v_spread * (upward - 2.0 * middle + downward) / (z_spacing * z_spacing)
    tracer = lax.broadcasted_iota(jnp.int32, (2, 1, 1, 1), 0)
    own = jnp.where(tracer == 0, coupling[0, 0], coupling[1, 1])
    other = jnp.where(tracer == 0, coupling[0, 1], coupling[1, 0])
    reaction = own * middle + other * middle[::-1]
    return diffusion + vertical - advection + reaction


def pair_sum(field):
    row = lax.broadcasted_iota(jnp.int32, field.shape, field.ndim - 2)
    partner = jnp.where(
        row % 2 == 0, jnp.roll(field, -1, axis=-2), jnp.roll(field, 1, axis=-2)
    )
    return field + partner


def shrink(field):
    levels = field[..., 0::2, :, :] + field[..., 1::2, :, :]
    return pair_sum(levels) * 0.25


def expand(field):
    return jnp.repeat(field, 2, axis=-3)


def add_coarse(fine, coarse):
    shape = fine.shape
    paired = fine.reshape(shape[:-3] + (shape[-3] // 2, 2) + shape[-2:])
    return (paired + jnp.expand_dims(coarse, -3)).reshape(shape)


def pick(items, index):
    out = items[0]
    for k in range(1, len(items)):
        out = jax.tree.map(lambda new, old: jnp.where(index == k, new, old), items[k], out)
    return out


def pair_map(fn, *halos):
    return fn(*halos)


def body(initial, x_velocity, y_velocity, h_diffusion, v_diffusion, coupling):
    coarse_x = shrink(x_velocity)
    coarse_y = shrink(y_velocity)
    coarse_h = shrink(h_diffusion)
    coarse_v = shrink(v_diffusion)
    slabs = lax.axis_size("tm")
    columns = lax.axis_size("space")
    slab = lax.axis_index("tm")
    first = slab == 0

    def fine_rate(field, halo):
        return tendency(
            field, halo, x_velocity, y_velocity, h_diffusion, v_diffusion, coupling, 1.0, 1.0
        )

    def coarse_rate(field, halo):
        return tendency(field, halo, coarse_x, coarse_y, coarse_h, coarse_v, coupling, 2.0, 2.0)

    def first_node(node_zero, rate_zero, s0, s1, s2):
        return (
            node_zero
            + half_step * (rate_zero - s0)
            + slab_step * (s0 * (5.0 / 24.0) + s1 * (1.0 / 3.0) - s2 * (1.0 / 24.0))
        )

    def second_node(node_one, rate_one, s0, s1, s2):
        return (
            node_one
            + half_step * (rate_one - s1)
            + slab_step * (s0 * (-1.0 / 24.0) + s1 * (1.0 / 3.0) + s2 * (5.0 / 24.0))
        )

    coarse_first = shrink(initial)
    levels = initial.shape[-3]

    def joined(fine, coarse):
        return jnp.concatenate([fine, coarse], axis=-3)

    coarse_coefs = (coarse_x, coarse_y, coarse_h, coarse_v)
    coarse_levels = coarse_first.shape[-3]

    fine_coefs = (x_velocity, y_velocity, h_diffusion, v_diffusion)

    def coef_edge(edge, coefs):
        stacked = jnp.stack([edge(c) for c in coefs])
        return stacked.reshape((2, -1) + stacked.shape[-2:])

    def inner_hi(field):
        return hi(field, 2)[..., 0:1, :]

    def inner_lo(field):
        return lo(field, 2)[..., 1:2, :]

    sent = [
        (hi(initial), lo(initial)),
        (hi(coarse_first), lo(coarse_first)),
        (coef_edge(hi, coarse_coefs), coef_edge(lo, coarse_coefs)),
        (inner_hi(initial), inner_lo(initial)),
        (coef_edge(hi, fine_coefs), coef_edge(lo, fine_coefs)),
    ]
    before, after = exchange(
        jnp.concatenate([pair[0] for pair in sent], axis=-3),
        jnp.concatenate([pair[1] for pair in sent], axis=-3),
    )
    bounds = [0]
    for pair in sent:
        bounds.append(bounds[-1] + pair[0].shape[-3])

    def piece(k):
        return pack(
            before[..., bounds[k] : bounds[k + 1], :, :],
            after[..., bounds[k] : bounds[k + 1], :, :],
        )

    halo_zero = piece(0)
    halo_first = piece(1)
    edge_coefs = piece(2).reshape((4, coarse_levels) + halo_first.shape[-2:])
    fine_edge_coefs = piece(4).reshape((4, levels) + halo_zero.shape[-2:])
    init_inner = piece(3)
    first_rate = fine_rate(initial, halo_zero)
    coarse_first_rate = coarse_rate(coarse_first, halo_first)

    node_zero = initial
    rate_zero = first_rate
    node_one = first_node(node_zero, rate_zero, first_rate, first_rate, first_rate)
    edge_rate = stencil(
        halo_zero,
        pack(lo(initial), east(init_inner)),
        pack(west(init_inner), hi(initial)),
        *(fine_edge_coefs[k] for k in range(4)),
        coupling, 1.0, 1.0,
    )
    halo_one = first_node(halo_zero, edge_rate, edge_rate, edge_rate, edge_rate)
    rate_one = fine_rate(node_one, halo_one)
    node_two = second_node(node_one, rate_one, first_rate, first_rate, first_rate)
    two_b, two_a = exchange(hi(node_two, 2), lo(node_two, 2))
    halo_two = pack(hi(two_b), lo(two_a))
    coarse_end = shrink(node_two)
    halo_end = pack(hi(shrink(two_b)), lo(shrink(two_a)))
    rate_two = fine_rate(node_two, halo_two)
    source = shrink(slab_step * (rate_zero + 4.0 * rate_one + rate_two) / 6.0)
    offset = source - slab_step * coarse_first_rate

    chain = [coarse_first]
    chain_halo = [halo_first]
    rate = coarse_first_rate
    rates = [rate]
    wide = None
    for count in range(slabs):
        after = chain[-1] + slab_step * rate + offset
        if wide is not None:
            strip_b, strip_a, offset_edge = wide
            edge = pack(strip_b[..., 2:3, :], strip_a[..., 0:1, :])
            edge_rate = stencil(
                edge,
                pack(lo(chain[-1]), strip_a[..., 2:3, :]),
                pack(strip_b[..., 0:1, :], hi(chain[-1])),
                *(edge_coefs[k] for k in range(4)),
                coupling, 2.0, 2.0,
            )
            after_halo = edge + slab_step * edge_rate + offset_edge
        elif count + 2 == slabs:
            packed_b, packed_a = exchange(
                jnp.concatenate([hi(after, 3), hi(offset)], axis=-2),
                jnp.concatenate([lo(after, 3), lo(offset)], axis=-2),
            )
            strip_b, strip_a = packed_b[..., :3, :], packed_a[..., :3, :]
            wide = (strip_b, strip_a, pack(packed_b[..., 3:, :], packed_a[..., 3:, :]))
            after_halo = pack(strip_b[..., 2:3, :], strip_a[..., 0:1, :])
        else:
            after_halo = halo_of(after)
        chain.append(after)
        chain_halo.append(after_halo)
        if count + 1 < slabs:
            rate = coarse_rate(after, after_halo)
            rates.append(rate)
    begins = pick(chain, slab)
    finals = pick(chain, slab + 1)
    begins_halo = pick(chain_halo, slab)
    finals_halo = pick(chain_halo, slab + 1)

    delta_zero = begins - coarse_first
    delta_one = finals - coarse_end
    fixed_zero = add_coarse(node_zero, delta_zero)
    fixed_one = add_coarse(node_one, (delta_zero + delta_one) * 0.5)
    fixed_two = add_coarse(node_two, delta_one)
    halo_dz = pair_map(lambda y, v: y - v, begins_halo, halo_first)
    halo_d1 = pair_map(lambda y, v: y - v, finals_halo, halo_end)
    halo_f0 = add_coarse(halo_zero, halo_dz)
    halo_f1 = add_coarse(halo_one, (halo_dz + halo_d1) * 0.5)
    halo_f2 = add_coarse(halo_two, halo_d1)

    earlier_delta = begins - coarse_end
    earlier_end = add_coarse(node_two, earlier_delta)
    halo_earlier_delta = pair_map(lambda y, v: y - v, begins_halo, halo_end)
    halo_earlier = add_coarse(halo_two, halo_earlier_delta)
    start = jnp.where(first, initial, earlier_end)
    halo_start = pair_map(lambda a, b: jnp.where(first, a, b), halo_zero, halo_earlier)
    start_rate = pick(rates, slab)

    def combined(c0, c1, c2):
        return lambda u0, u1, u2: c0 * u0 + c1 * u1 + c2 * u2

    to_one = combined(-7.0 / 48.0, 1.0 / 6.0, -1.0 / 48.0)
    to_two = combined(-1.0 / 48.0, -1.0 / 12.0, 5.0 / 48.0)
    node_zero = start
    node_one = node_zero + fine_rate(
        half_step * node_zero + to_one(fixed_zero, fixed_one, fixed_two),
        half_step * halo_start + to_one(halo_f0, halo_f1, halo_f2),
    )
    halo_one = halo_of(node_one)
    node_two = node_one + fine_rate(
        half_step * node_one + to_two(fixed_zero, fixed_one, fixed_two),
        half_step * halo_one + to_two(halo_f0, halo_f1, halo_f2),
    )
    halo_two = halo_of(node_two)
    coarse_end = shrink(node_two)
    quadrature = fine_rate(
        node_zero + 4.0 * node_one + node_two, halo_start + 4.0 * halo_one + halo_two
    )
    source = shrink(slab_step * quadrature / 6.0)
    offset = source - slab_step * start_rate

    down = shift_pairs(slabs, 1)
    to_east = [
        (t * columns + c, (t + 1) * columns + c + 1)
        for t in range(slabs - 1)
        for c in range(columns - 1)
    ]
    to_west = [
        (t * columns + c, (t + 1) * columns + c - 1)
        for t in range(slabs - 1)
        for c in range(1, columns)
    ]
    carried = coarse_first
    carried_halo = halo_first
    rate = coarse_first_rate
    for count in range(slabs - 1):
        after = carried + slab_step * rate + offset
        passed = lax.ppermute(after, "tm", down)
        passed_b = lax.ppermute(hi(after), ("tm", "space"), to_east)
        passed_a = lax.ppermute(lo(after), ("tm", "space"), to_west)
        carried = jnp.where(first, coarse_first, passed)
        carried_halo = jnp.where(first, halo_first, pack(passed_b, passed_a))
        rate = coarse_rate(carried, carried_halo)
    finals = carried + slab_step * rate + offset
    result = add_coarse(node_two, finals - coarse_end)
    return result[None]


def solution(mesh):
    return jax.shard_map(
        body,
        mesh=mesh,
        in_specs=(
            P(None, None, "space", None),
            P(None, "space", None),
            P(None, "space", None),
            P(None, "space", None),
            P(None, "space", None),
            P(),
        ),
        out_specs=P("tm", None, None, "space", None),
        check_vma=False,
    )
```

```python
import jax
import jax.numpy as jnp
from jax import lax
from jax.sharding import PartitionSpec as P

ITERS = 2


slab_step = 0.5
half_step = 0.25


def shift_pairs(count, steps):
    return [(i, i + steps) for i in range(max(0, -steps), min(count, count - steps))]


def exchange(to_right, to_left):
    count = lax.axis_size("space")
    before = lax.ppermute(to_right, "space", shift_pairs(count, 1))
    after = lax.ppermute(to_left, "space", shift_pairs(count, -1))
    return before, after


def lo(field, width=1):
    return field[..., :width, :]


def hi(field, width=1):
    return field[..., field.shape[-2] - width:, :]


def pack(before, after):
    return jnp.concatenate([before, after], axis=-2)


def west(halo):
    return halo[..., 0:1, :]


def east(halo):
    return halo[..., 1:2, :]


def halo_of(field):
    return pack(*exchange(hi(field), lo(field)))


def tendency(field, halo, x_speed, y_speed, h_spread, v_spread, coupling, x_spacing, z_spacing):
    reach = int(x_spacing)
    padded = jnp.concatenate([west(halo)] * reach + [field] + [east(halo)] * reach, axis=-2)
    width = field.shape[-2]
    return stencil(
        field, padded[..., 2 * reach:, :], padded[..., :width, :],
        x_speed, y_speed, h_spread, v_spread, coupling, x_spacing, z_spacing,
    )


def stencil(middle, eastward, westward, x_speed, y_speed, h_spread, v_spread, coupling,
            x_spacing, z_spacing):
    y_widths = [(0, 0)] * (middle.ndim - 1) + [(1, 1)]
    y_padded = jnp.pad(middle, y_widths)
    northward = y_padded[..., 2:]
    southward = y_padded[..., :-2]
    z_widths = [(0, 0)] * (middle.ndim - 3) + [(1, 1), (0, 0), (0, 0)]
    z_padded = jnp.pad(middle, z_widths)
    upward = z_padded[..., 2:, :, :]
    downward = z_padded[..., :-2, :, :]
    advection = (
        x_speed * (eastward - westward) / (2.0 * x_spacing)
        + y_speed * (northward - southward) * 0.5
    )
    diffusion = h_spread * (
        (eastward - 2.0 * middle + westward) / (x_spacing * x_spacing)
        + (northward - 2.0 * middle + southward)
    )
    vertical = v_spread * (upward - 2.0 * middle + downward) / (z_spacing * z_spacing)
    tracer = lax.broadcasted_iota(jnp.int32, (2, 1, 1, 1), 0)
    own = jnp.where(tracer == 0, coupling[0, 0], coupling[1, 1])
    other = jnp.where(tracer == 0, coupling[0, 1], coupling[1, 0])
    reaction = own * middle + other * middle[::-1]
    return diffusion + vertical - advection + reaction


def pair_sum(field):
    row = lax.broadcasted_iota(jnp.int32, field.shape, field.ndim - 2)
    partner = jnp.where(
        row % 2 == 0, jnp.roll(field, -1, axis=-2), jnp.roll(field, 1, axis=-2)
    )
    return field + partner


def shrink(field):
    levels = field[..., 0::2, :, :] + field[..., 1::2, :, :]
    return pair_sum(levels) * 0.25


def expand(field):
    return jnp.repeat(field, 2, axis=-3)


def add_coarse(fine, coarse):
    shape = fine.shape
    paired = fine.reshape(shape[:-3] + (shape[-3] // 2, 2) + shape[-2:])
    return (paired + jnp.expand_dims(coarse, -3)).reshape(shape)


def pick(items, index):
    out = items[0]
    for k in range(1, len(items)):
        out = jax.tree.map(lambda new, old: jnp.where(index == k, new, old), items[k], out)
    return out


def pair_map(fn, *halos):
    return fn(*halos)


def body(initial, x_velocity, y_velocity, h_diffusion, v_diffusion, coupling):
    coarse_x = shrink(x_velocity)
    coarse_y = shrink(y_velocity)
    coarse_h = shrink(h_diffusion)
    coarse_v = shrink(v_diffusion)
    slabs = lax.axis_size("tm")
    columns = lax.axis_size("space")
    slab = lax.axis_index("tm")
    first = slab == 0

    def fine_rate(field, halo):
        return tendency(
            field, halo, x_velocity, y_velocity, h_diffusion, v_diffusion, coupling, 1.0, 1.0
        )

    def coarse_rate(field, halo):
        return tendency(field, halo, coarse_x, coarse_y, coarse_h, coarse_v, coupling, 2.0, 2.0)

    def first_node(node_zero, rate_zero, s0, s1, s2):
        return (
            node_zero
            + half_step * (rate_zero - s0)
            + slab_step * (s0 * (5.0 / 24.0) + s1 * (1.0 / 3.0) - s2 * (1.0 / 24.0))
        )

    def second_node(node_one, rate_one, s0, s1, s2):
        return (
            node_one
            + half_step * (rate_one - s1)
            + slab_step * (s0 * (-1.0 / 24.0) + s1 * (1.0 / 3.0) + s2 * (5.0 / 24.0))
        )

    coarse_first = shrink(initial)
    levels = initial.shape[-3]

    def joined(fine, coarse):
        return jnp.concatenate([fine, coarse], axis=-3)

    coarse_coefs = (coarse_x, coarse_y, coarse_h, coarse_v)
    coarse_levels = coarse_first.shape[-3]

    def coef_edge(edge):
        stacked = jnp.stack([edge(c) for c in coarse_coefs])
        return stacked.reshape((2, -1) + stacked.shape[-2:])

    before, after = exchange(
        joined(joined(hi(initial), hi(coarse_first)), coef_edge(hi)),
        joined(joined(lo(initial), lo(coarse_first)), coef_edge(lo)),
    )
    split = (levels, levels + coarse_levels)
    init_b, first_b = before[..., : split[0], :, :], before[..., split[0] : split[1], :, :]
    init_a, first_a = after[..., : split[0], :, :], after[..., split[0] : split[1], :, :]
    edge_coefs = pack(before[..., split[1] :, :, :], after[..., split[1] :, :, :])
    edge_coefs = edge_coefs.reshape((4, coarse_levels) + edge_coefs.shape[-2:])
    halo_zero = pack(init_b, init_a)
    halo_first = pack(first_b, first_a)
    first_rate = fine_rate(initial, halo_zero)
    coarse_first_rate = coarse_rate(coarse_first, halo_first)

    node_zero = initial
    rate_zero = first_rate
    node_one = first_node(node_zero, rate_zero, first_rate, first_rate, first_rate)
    halo_one = halo_of(node_one)
    rate_one = fine_rate(node_one, halo_one)
    node_two = second_node(node_one, rate_one, first_rate, first_rate, first_rate)
    coarse_end = shrink(node_two)
    two_b, two_a = exchange(
        joined(hi(node_two), hi(coarse_end)), joined(lo(node_two), lo(coarse_end))
    )
    halo_two = pack(two_b[..., :levels, :, :], two_a[..., :levels, :, :])
    halo_end = pack(two_b[..., levels:, :, :], two_a[..., levels:, :, :])
    rate_two = fine_rate(node_two, halo_two)
    source = shrink(slab_step * (rate_zero + 4.0 * rate_one + rate_two) / 6.0)
    offset = source - slab_step * coarse_first_rate

    chain = [coarse_first]
    chain_halo = [halo_first]
    rate = coarse_first_rate
    rates = [rate]
    wide = None
    for count in range(slabs):
        after = chain[-1] + slab_step * rate + offset
        if wide is not None:
            strip_b, strip_a, offset_edge = wide
            edge = pack(strip_b[..., 2:3, :], strip_a[..., 0:1, :])
            edge_rate = stencil(
                edge,
                pack(lo(chain[-1]), strip_a[..., 2:3, :]),
                pack(strip_b[..., 0:1, :], hi(chain[-1])),
                *(edge_coefs[k] for k in range(4)),
                coupling, 2.0, 2.0,
            )
            after_halo = edge + slab_step * edge_rate + offset_edge
        elif count + 2 == slabs:
            packed_b, packed_a = exchange(
                jnp.concatenate([hi(after, 3), hi(offset)], axis=-2),
                jnp.concatenate([lo(after, 3), lo(offset)], axis=-2),
            )
            strip_b, strip_a = packed_b[..., :3, :], packed_a[..., :3, :]
            wide = (strip_b, strip_a, pack(packed_b[..., 3:, :], packed_a[..., 3:, :]))
            after_halo = pack(strip_b[..., 2:3, :], strip_a[..., 0:1, :])
        else:
            after_halo = halo_of(after)
        chain.append(after)
        chain_halo.append(after_halo)
        if count + 1 < slabs:
            rate = coarse_rate(after, after_halo)
            rates.append(rate)
    begins = pick(chain, slab)
    finals = pick(chain, slab + 1)
    begins_halo = pick(chain_halo, slab)
    finals_halo = pick(chain_halo, slab + 1)

    delta_zero = begins - coarse_first
    delta_one = finals - coarse_end
    fixed_zero = add_coarse(node_zero, delta_zero)
    fixed_one = add_coarse(node_one, (delta_zero + delta_one) * 0.5)
    fixed_two = add_coarse(node_two, delta_one)
    halo_dz = pair_map(lambda y, v: y - v, begins_halo, halo_first)
    halo_d1 = pair_map(lambda y, v: y - v, finals_halo, halo_end)
    halo_f0 = add_coarse(halo_zero, halo_dz)
    halo_f1 = add_coarse(halo_one, (halo_dz + halo_d1) * 0.5)
    halo_f2 = add_coarse(halo_two, halo_d1)

    earlier_delta = begins - coarse_end
    earlier_end = add_coarse(node_two, earlier_delta)
    halo_earlier_delta = pair_map(lambda y, v: y - v, begins_halo, halo_end)
    halo_earlier = add_coarse(halo_two, halo_earlier_delta)
    start = jnp.where(first, initial, earlier_end)
    halo_start = pair_map(lambda a, b: jnp.where(first, a, b), halo_zero, halo_earlier)
    start_rate = pick(rates, slab)

    def combined(c0, c1, c2):
        return lambda u0, u1, u2: c0 * u0 + c1 * u1 + c2 * u2

    to_one = combined(-7.0 / 48.0, 1.0 / 6.0, -1.0 / 48.0)
    to_two = combined(-1.0 / 48.0, -1.0 / 12.0, 5.0 / 48.0)
    node_zero = start
    node_one = node_zero + fine_rate(
        half_step * node_zero + to_one(fixed_zero, fixed_one, fixed_two),
        half_step * halo_start + to_one(halo_f0, halo_f1, halo_f2),
    )
    halo_one = halo_of(node_one)
    node_two = node_one + fine_rate(
        half_step * node_one + to_two(fixed_zero, fixed_one, fixed_two),
        half_step * halo_one + to_two(halo_f0, halo_f1, halo_f2),
    )
    halo_two = halo_of(node_two)
    coarse_end = shrink(node_two)
    quadrature = fine_rate(
        node_zero + 4.0 * node_one + node_two, halo_start + 4.0 * halo_one + halo_two
    )
    source = shrink(slab_step * quadrature / 6.0)
    offset = source - slab_step * start_rate

    down = shift_pairs(slabs, 1)
    to_east = [
        (t * columns + c, (t + 1) * columns + c + 1)
        for t in range(slabs - 1)
        for c in range(columns - 1)
    ]
    to_west = [
        (t * columns + c, (t + 1) * columns + c - 1)
        for t in range(slabs - 1)
        for c in range(1, columns)
    ]
    carried = coarse_first
    carried_halo = halo_first
    rate = coarse_first_rate
    for count in range(slabs - 1):
        after = carried + slab_step * rate + offset
        passed = lax.ppermute(after, "tm", down)
        passed_b = lax.ppermute(hi(after), ("tm", "space"), to_east)
        passed_a = lax.ppermute(lo(after), ("tm", "space"), to_west)
        carried = jnp.where(first, coarse_first, passed)
        carried_halo = jnp.where(first, halo_first, pack(passed_b, passed_a))
        rate = coarse_rate(carried, carried_halo)
    finals = carried + slab_step * rate + offset
    result = add_coarse(node_two, finals - coarse_end)
    return result[None]


def solution(mesh):
    return jax.shard_map(
        body,
        mesh=mesh,
        in_specs=(
            P(None, None, "space", None),
            P(None, "space", None),
            P(None, "space", None),
            P(None, "space", None),
            P(None, "space", None),
            P(),
        ),
        out_specs=P("tm", None, None, "space", None),
        check_vma=False,
    )
```

```python
import jax
import jax.numpy as jnp
from jax import lax
from jax.sharding import PartitionSpec as P

ITERS = 2


slab_step = 0.5
half_step = 0.25


def shift_pairs(count, steps):
    return [(i, i + steps) for i in range(max(0, -steps), min(count, count - steps))]


def exchange(to_right, to_left):
    count = lax.axis_size("space")
    before = lax.ppermute(to_right, "space", shift_pairs(count, 1))
    after = lax.ppermute(to_left, "space", shift_pairs(count, -1))
    return before, after


def lo(field, width=1):
    return field[..., :width, :]


def hi(field, width=1):
    return field[..., field.shape[-2] - width:, :]


def pack(before, after):
    return jnp.concatenate([before, after], axis=-2)


def west(halo):
    return halo[..., 0:1, :]


def east(halo):
    return halo[..., 1:2, :]


def halo_of(field):
    return pack(*exchange(hi(field), lo(field)))


def tendency(field, halo, x_speed, y_speed, h_spread, v_spread, coupling, x_spacing, z_spacing):
    reach = int(x_spacing)
    padded = jnp.concatenate([west(halo)] * reach + [field] + [east(halo)] * reach, axis=-2)
    width = field.shape[-2]
    return stencil(
        field, padded[..., 2 * reach:, :], padded[..., :width, :],
        x_speed, y_speed, h_spread, v_spread, coupling, x_spacing, z_spacing,
    )


def stencil(middle, eastward, westward, x_speed, y_speed, h_spread, v_spread, coupling,
            x_spacing, z_spacing):
    y_widths = [(0, 0)] * (middle.ndim - 1) + [(1, 1)]
    y_padded = jnp.pad(middle, y_widths)
    northward = y_padded[..., 2:]
    southward = y_padded[..., :-2]
    z_widths = [(0, 0)] * (middle.ndim - 3) + [(1, 1), (0, 0), (0, 0)]
    z_padded = jnp.pad(middle, z_widths)
    upward = z_padded[..., 2:, :, :]
    downward = z_padded[..., :-2, :, :]
    advection = (
        x_speed * (eastward - westward) / (2.0 * x_spacing)
        + y_speed * (northward - southward) * 0.5
    )
    diffusion = h_spread * (
        (eastward - 2.0 * middle + westward) / (x_spacing * x_spacing)
        + (northward - 2.0 * middle + southward)
    )
    vertical = v_spread * (upward - 2.0 * middle + downward) / (z_spacing * z_spacing)
    tracer = lax.broadcasted_iota(jnp.int32, (2, 1, 1, 1), 0)
    own = jnp.where(tracer == 0, coupling[0, 0], coupling[1, 1])
    other = jnp.where(tracer == 0, coupling[0, 1], coupling[1, 0])
    reaction = own * middle + other * middle[::-1]
    return diffusion + vertical - advection + reaction


def pair_sum(field):
    row = lax.broadcasted_iota(jnp.int32, field.shape, field.ndim - 2)
    partner = jnp.where(
        row % 2 == 0, jnp.roll(field, -1, axis=-2), jnp.roll(field, 1, axis=-2)
    )
    return field + partner


def shrink(field):
    levels = field[..., 0::2, :, :] + field[..., 1::2, :, :]
    return pair_sum(levels) * 0.25


def expand(field):
    return jnp.repeat(field, 2, axis=-3)


def add_coarse(fine, coarse):
    shape = fine.shape
    paired = fine.reshape(shape[:-3] + (shape[-3] // 2, 2) + shape[-2:])
    return (paired + jnp.expand_dims(coarse, -3)).reshape(shape)


def pick(items, index):
    out = items[0]
    for k in range(1, len(items)):
        out = jax.tree.map(lambda new, old: jnp.where(index == k, new, old), items[k], out)
    return out


def pair_map(fn, *halos):
    return fn(*halos)


def body(initial, x_velocity, y_velocity, h_diffusion, v_diffusion, coupling):
    coarse_x = shrink(x_velocity)
    coarse_y = shrink(y_velocity)
    coarse_h = shrink(h_diffusion)
    coarse_v = shrink(v_diffusion)
    slabs = lax.axis_size("tm")
    columns = lax.axis_size("space")
    slab = lax.axis_index("tm")
    first = slab == 0

    def fine_rate(field, halo):
        return tendency(
            field, halo, x_velocity, y_velocity, h_diffusion, v_diffusion, coupling, 1.0, 1.0
        )

    def coarse_rate(field, halo):
        return tendency(field, halo, coarse_x, coarse_y, coarse_h, coarse_v, coupling, 2.0, 2.0)

    def first_node(node_zero, rate_zero, s0, s1, s2):
        return (
            node_zero
            + half_step * (rate_zero - s0)
            + slab_step * (s0 * (5.0 / 24.0) + s1 * (1.0 / 3.0) - s2 * (1.0 / 24.0))
        )

    def second_node(node_one, rate_one, s0, s1, s2):
        return (
            node_one
            + half_step * (rate_one - s1)
            + slab_step * (s0 * (-1.0 / 24.0) + s1 * (1.0 / 3.0) + s2 * (5.0 / 24.0))
        )

    coarse_first = shrink(initial)
    levels = initial.shape[-3]

    def joined(fine, coarse):
        return jnp.concatenate([fine, coarse], axis=-3)

    coarse_coefs = (coarse_x, coarse_y, coarse_h, coarse_v)
    coarse_levels = coarse_first.shape[-3]

    def coef_edge(edge):
        stacked = jnp.stack([edge(c) for c in coarse_coefs])
        return stacked.reshape((2, -1) + stacked.shape[-2:])

    before, after = exchange(
        joined(joined(hi(initial), hi(coarse_first)), coef_edge(hi)),
        joined(joined(lo(initial), lo(coarse_first)), coef_edge(lo)),
    )
    split = (levels, levels + coarse_levels)
    init_b, first_b = before[..., : split[0], :, :], before[..., split[0] : split[1], :, :]
    init_a, first_a = after[..., : split[0], :, :], after[..., split[0] : split[1], :, :]
    edge_coefs = pack(before[..., split[1] :, :, :], after[..., split[1] :, :, :])
    edge_coefs = edge_coefs.reshape((4, coarse_levels) + edge_coefs.shape[-2:])
    halo_zero = pack(init_b, init_a)
    halo_first = pack(first_b, first_a)
    first_rate = fine_rate(initial, halo_zero)
    coarse_first_rate = coarse_rate(coarse_first, halo_first)

    node_zero = initial
    rate_zero = first_rate
    node_one = first_node(node_zero, rate_zero, first_rate, first_rate, first_rate)
    halo_one = halo_of(node_one)
    rate_one = fine_rate(node_one, halo_one)
    node_two = second_node(node_one, rate_one, first_rate, first_rate, first_rate)
    two_b, two_a = exchange(hi(node_two, 2), lo(node_two, 2))
    halo_two = pack(hi(two_b), lo(two_a))
    coarse_end = shrink(node_two)
    halo_end = pack(hi(shrink(two_b)), lo(shrink(two_a)))
    rate_two = fine_rate(node_two, halo_two)
    source = shrink(slab_step * (rate_zero + 4.0 * rate_one + rate_two) / 6.0)
    offset = source - slab_step * coarse_first_rate

    chain = [coarse_first]
    chain_halo = [halo_first]
    rate = coarse_first_rate
    rates = [rate]
    wide = None
    for count in range(slabs):
        after = chain[-1] + slab_step * rate + offset
        if wide is not None:
            strip_b, strip_a, offset_edge = wide
            edge = pack(strip_b[..., 2:3, :], strip_a[..., 0:1, :])
            edge_rate = stencil(
                edge,
                pack(lo(chain[-1]), strip_a[..., 2:3, :]),
                pack(strip_b[..., 0:1, :], hi(chain[-1])),
                *(edge_coefs[k] for k in range(4)),
                coupling, 2.0, 2.0,
            )
            after_halo = edge + slab_step * edge_rate + offset_edge
        elif count + 2 == slabs:
            packed_b, packed_a = exchange(
                jnp.concatenate([hi(after, 3), hi(offset)], axis=-2),
                jnp.concatenate([lo(after, 3), lo(offset)], axis=-2),
            )
            strip_b, strip_a = packed_b[..., :3, :], packed_a[..., :3, :]
            wide = (strip_b, strip_a, pack(packed_b[..., 3:, :], packed_a[..., 3:, :]))
            after_halo = pack(strip_b[..., 2:3, :], strip_a[..., 0:1, :])
        else:
            after_halo = halo_of(after)
        chain.append(after)
        chain_halo.append(after_halo)
        if count + 1 < slabs:
            rate = coarse_rate(after, after_halo)
            rates.append(rate)
    begins = pick(chain, slab)
    finals = pick(chain, slab + 1)
    begins_halo = pick(chain_halo, slab)
    finals_halo = pick(chain_halo, slab + 1)

    delta_zero = begins - coarse_first
    delta_one = finals - coarse_end
    fixed_zero = add_coarse(node_zero, delta_zero)
    fixed_one = add_coarse(node_one, (delta_zero + delta_one) * 0.5)
    fixed_two = add_coarse(node_two, delta_one)
    halo_dz = pair_map(lambda y, v: y - v, begins_halo, halo_first)
    halo_d1 = pair_map(lambda y, v: y - v, finals_halo, halo_end)
    halo_f0 = add_coarse(halo_zero, halo_dz)
    halo_f1 = add_coarse(halo_one, (halo_dz + halo_d1) * 0.5)
    halo_f2 = add_coarse(halo_two, halo_d1)

    earlier_delta = begins - coarse_end
    earlier_end = add_coarse(node_two, earlier_delta)
    halo_earlier_delta = pair_map(lambda y, v: y - v, begins_halo, halo_end)
    halo_earlier = add_coarse(halo_two, halo_earlier_delta)
    start = jnp.where(first, initial, earlier_end)
    halo_start = pair_map(lambda a, b: jnp.where(first, a, b), halo_zero, halo_earlier)
    start_rate = pick(rates, slab)

    def combined(c0, c1, c2):
        return lambda u0, u1, u2: c0 * u0 + c1 * u1 + c2 * u2

    to_one = combined(-7.0 / 48.0, 1.0 / 6.0, -1.0 / 48.0)
    to_two = combined(-1.0 / 48.0, -1.0 / 12.0, 5.0 / 48.0)
    node_zero = start
    node_one = node_zero + fine_rate(
        half_step * node_zero + to_one(fixed_zero, fixed_one, fixed_two),
        half_step * halo_start + to_one(halo_f0, halo_f1, halo_f2),
    )
    halo_one = halo_of(node_one)
    node_two = node_one + fine_rate(
        half_step * node_one + to_two(fixed_zero, fixed_one, fixed_two),
        half_step * halo_one + to_two(halo_f0, halo_f1, halo_f2),
    )
    halo_two = halo_of(node_two)
    coarse_end = shrink(node_two)
    quadrature = fine_rate(
        node_zero + 4.0 * node_one + node_two, halo_start + 4.0 * halo_one + halo_two
    )
    source = shrink(slab_step * quadrature / 6.0)
    offset = source - slab_step * start_rate

    down = shift_pairs(slabs, 1)
    to_east = [
        (t * columns + c, (t + 1) * columns + c + 1)
        for t in range(slabs - 1)
        for c in range(columns - 1)
    ]
    to_west = [
        (t * columns + c, (t + 1) * columns + c - 1)
        for t in range(slabs - 1)
        for c in range(1, columns)
    ]
    carried = coarse_first
    carried_halo = halo_first
    rate = coarse_first_rate
    for count in range(slabs - 1):
        after = carried + slab_step * rate + offset
        rows = after.reshape(after.shape[:-2] + (after.shape[-2] // 2, 2, after.shape[-1]))
        passed = jnp.repeat(lax.ppermute(rows[..., 0, :], "tm", down), 2, axis=-2)
        passed_b = lax.ppermute(hi(after), ("tm", "space"), to_east)
        passed_a = lax.ppermute(lo(after), ("tm", "space"), to_west)
        carried = jnp.where(first, coarse_first, passed)
        carried_halo = jnp.where(first, halo_first, pack(passed_b, passed_a))
        rate = coarse_rate(carried, carried_halo)
    finals = carried + slab_step * rate + offset
    result = add_coarse(node_two, finals - coarse_end)
    return result[None]


def solution(mesh):
    return jax.shard_map(
        body,
        mesh=mesh,
        in_specs=(
            P(None, None, "space", None),
            P(None, "space", None),
            P(None, "space", None),
            P(None, "space", None),
            P(None, "space", None),
            P(),
        ),
        out_specs=P("tm", None, None, "space", None),
        check_vma=False,
    )
```

```python
import jax
import jax.numpy as jnp
from jax import lax
from jax.sharding import PartitionSpec as P

ITERS = 2


slab_step = 0.5
half_step = 0.25


def shift_pairs(count, steps):
    return [(i, i + steps) for i in range(max(0, -steps), min(count, count - steps))]


def exchange(to_right, to_left):
    count = lax.axis_size("space")
    before = lax.ppermute(to_right, "space", shift_pairs(count, 1))
    after = lax.ppermute(to_left, "space", shift_pairs(count, -1))
    return before, after


def lo(field, width=1):
    return field[..., :width, :]


def hi(field, width=1):
    return field[..., field.shape[-2] - width:, :]


def pack(before, after):
    return jnp.concatenate([before, after], axis=-2)


def west(halo):
    return halo[..., 0:1, :]


def east(halo):
    return halo[..., 1:2, :]


def halo_of(field):
    return pack(*exchange(hi(field), lo(field)))


def tendency(field, halo, x_speed, y_speed, h_spread, v_spread, coupling, x_spacing, z_spacing):
    reach = int(x_spacing)
    padded = jnp.concatenate([west(halo)] * reach + [field] + [east(halo)] * reach, axis=-2)
    width = field.shape[-2]
    return stencil(
        field, padded[..., 2 * reach:, :], padded[..., :width, :],
        x_speed, y_speed, h_spread, v_spread, coupling, x_spacing, z_spacing,
    )


def stencil(middle, eastward, westward, x_speed, y_speed, h_spread, v_spread, coupling,
            x_spacing, z_spacing):
    y_widths = [(0, 0)] * (middle.ndim - 1) + [(1, 1)]
    y_padded = jnp.pad(middle, y_widths)
    northward = y_padded[..., 2:]
    southward = y_padded[..., :-2]
    z_widths = [(0, 0)] * (middle.ndim - 3) + [(1, 1), (0, 0), (0, 0)]
    z_padded = jnp.pad(middle, z_widths)
    upward = z_padded[..., 2:, :, :]
    downward = z_padded[..., :-2, :, :]
    advection = (
        x_speed * (eastward - westward) / (2.0 * x_spacing)
        + y_speed * (northward - southward) * 0.5
    )
    diffusion = h_spread * (
        (eastward - 2.0 * middle + westward) / (x_spacing * x_spacing)
        + (northward - 2.0 * middle + southward)
    )
    vertical = v_spread * (upward - 2.0 * middle + downward) / (z_spacing * z_spacing)
    tracer = lax.broadcasted_iota(jnp.int32, (2, 1, 1, 1), 0)
    own = jnp.where(tracer == 0, coupling[0, 0], coupling[1, 1])
    other = jnp.where(tracer == 0, coupling[0, 1], coupling[1, 0])
    reaction = own * middle + other * middle[::-1]
    return diffusion + vertical - advection + reaction


def pair_sum(field):
    row = lax.broadcasted_iota(jnp.int32, field.shape, field.ndim - 2)
    partner = jnp.where(
        row % 2 == 0, jnp.roll(field, -1, axis=-2), jnp.roll(field, 1, axis=-2)
    )
    return field + partner


def shrink(field):
    levels = field[..., 0::2, :, :] + field[..., 1::2, :, :]
    return pair_sum(levels) * 0.25


def expand(field):
    return jnp.repeat(field, 2, axis=-3)


def add_coarse(fine, coarse):
    shape = fine.shape
    paired = fine.reshape(shape[:-3] + (shape[-3] // 2, 2) + shape[-2:])
    return (paired + jnp.expand_dims(coarse, -3)).reshape(shape)


def pick(items, index):
    out = items[0]
    for k in range(1, len(items)):
        out = jax.tree.map(lambda new, old: jnp.where(index == k, new, old), items[k], out)
    return out


def pair_map(fn, *halos):
    return fn(*halos)


def body(initial, x_velocity, y_velocity, h_diffusion, v_diffusion, coupling):
    coarse_x = shrink(x_velocity)
    coarse_y = shrink(y_velocity)
    coarse_h = shrink(h_diffusion)
    coarse_v = shrink(v_diffusion)
    slabs = lax.axis_size("tm")
    columns = lax.axis_size("space")
    slab = lax.axis_index("tm")
    first = slab == 0

    def fine_rate(field, halo):
        return tendency(
            field, halo, x_velocity, y_velocity, h_diffusion, v_diffusion, coupling, 1.0, 1.0
        )

    def coarse_rate(field, halo):
        return tendency(field, halo, coarse_x, coarse_y, coarse_h, coarse_v, coupling, 2.0, 2.0)

    def first_node(node_zero, rate_zero, s0, s1, s2):
        return (
            node_zero
            + half_step * (rate_zero - s0)
            + slab_step * (s0 * (5.0 / 24.0) + s1 * (1.0 / 3.0) - s2 * (1.0 / 24.0))
        )

    def second_node(node_one, rate_one, s0, s1, s2):
        return (
            node_one
            + half_step * (rate_one - s1)
            + slab_step * (s0 * (-1.0 / 24.0) + s1 * (1.0 / 3.0) + s2 * (5.0 / 24.0))
        )

    coarse_first = shrink(initial)
    levels = initial.shape[-3]

    def joined(fine, coarse):
        return jnp.concatenate([fine, coarse], axis=-3)

    coarse_coefs = (coarse_x, coarse_y, coarse_h, coarse_v)
    coarse_levels = coarse_first.shape[-3]

    def coef_edge(edge):
        stacked = jnp.stack([edge(c) for c in coarse_coefs])
        return stacked.reshape((2, -1) + stacked.shape[-2:])

    before, after = exchange(
        joined(joined(hi(initial), hi(coarse_first)), coef_edge(hi)),
        joined(joined(lo(initial), lo(coarse_first)), coef_edge(lo)),
    )
    split = (levels, levels + coarse_levels)
    init_b, first_b = before[..., : split[0], :, :], before[..., split[0] : split[1], :, :]
    init_a, first_a = after[..., : split[0], :, :], after[..., split[0] : split[1], :, :]
    edge_coefs = pack(before[..., split[1] :, :, :], after[..., split[1] :, :, :])
    edge_coefs = edge_coefs.reshape((4, coarse_levels) + edge_coefs.shape[-2:])
    halo_zero = pack(init_b, init_a)
    halo_first = pack(first_b, first_a)
    first_rate = fine_rate(initial, halo_zero)
    coarse_first_rate = coarse_rate(coarse_first, halo_first)

    node_zero = initial
    rate_zero = first_rate
    node_one = first_node(node_zero, rate_zero, first_rate, first_rate, first_rate)
    halo_one = halo_of(node_one)
    rate_one = fine_rate(node_one, halo_one)
    node_two = second_node(node_one, rate_one, first_rate, first_rate, first_rate)
    two_b, two_a = exchange(hi(node_two, 2), lo(node_two, 2))
    halo_two = pack(hi(two_b), lo(two_a))
    coarse_end = shrink(node_two)
    halo_end = pack(hi(shrink(two_b)), lo(shrink(two_a)))
    quadrature = fine_rate(
        node_zero + 4.0 * node_one + node_two, halo_zero + 4.0 * halo_one + halo_two
    )
    source = shrink(slab_step * quadrature / 6.0)
    offset = source - slab_step * coarse_first_rate

    chain = [coarse_first]
    chain_halo = [halo_first]
    rate = coarse_first_rate
    rates = [rate]
    wide = None
    for count in range(slabs):
        after = chain[-1] + slab_step * rate + offset
        if wide is not None:
            strip_b, strip_a, offset_edge = wide
            edge = pack(strip_b[..., 2:3, :], strip_a[..., 0:1, :])
            edge_rate = stencil(
                edge,
                pack(lo(chain[-1]), strip_a[..., 2:3, :]),
                pack(strip_b[..., 0:1, :], hi(chain[-1])),
                *(edge_coefs[k] for k in range(4)),
                coupling, 2.0, 2.0,
            )
            after_halo = edge + slab_step * edge_rate + offset_edge
        elif count + 2 == slabs:
            packed_b, packed_a = exchange(
                jnp.concatenate([hi(after, 3), hi(offset)], axis=-2),
                jnp.concatenate([lo(after, 3), lo(offset)], axis=-2),
            )
            strip_b, strip_a = packed_b[..., :3, :], packed_a[..., :3, :]
            wide = (strip_b, strip_a, pack(packed_b[..., 3:, :], packed_a[..., 3:, :]))
            after_halo = pack(strip_b[..., 2:3, :], strip_a[..., 0:1, :])
        else:
            after_halo = halo_of(after)
        chain.append(after)
        chain_halo.append(after_halo)
        if count + 1 < slabs:
            rate = coarse_rate(after, after_halo)
            rates.append(rate)
    begins = pick(chain, slab)
    finals = pick(chain, slab + 1)
    begins_halo = pick(chain_halo, slab)
    finals_halo = pick(chain_halo, slab + 1)

    delta_zero = begins - coarse_first
    delta_one = finals - coarse_end
    fixed_zero = add_coarse(node_zero, delta_zero)
    fixed_one = add_coarse(node_one, (delta_zero + delta_one) * 0.5)
    fixed_two = add_coarse(node_two, delta_one)
    halo_dz = pair_map(lambda y, v: y - v, begins_halo, halo_first)
    halo_d1 = pair_map(lambda y, v: y - v, finals_halo, halo_end)
    halo_f0 = add_coarse(halo_zero, halo_dz)
    halo_f1 = add_coarse(halo_one, (halo_dz + halo_d1) * 0.5)
    halo_f2 = add_coarse(halo_two, halo_d1)

    earlier_delta = begins - coarse_end
    earlier_end = add_coarse(node_two, earlier_delta)
    halo_earlier_delta = pair_map(lambda y, v: y - v, begins_halo, halo_end)
    halo_earlier = add_coarse(halo_two, halo_earlier_delta)
    start = jnp.where(first, initial, earlier_end)
    halo_start = pair_map(lambda a, b: jnp.where(first, a, b), halo_zero, halo_earlier)
    start_rate = pick(rates, slab)

    def combined(c0, c1, c2):
        return lambda u0, u1, u2: c0 * u0 + c1 * u1 + c2 * u2

    to_one = combined(-7.0 / 48.0, 1.0 / 6.0, -1.0 / 48.0)
    to_two = combined(-1.0 / 48.0, -1.0 / 12.0, 5.0 / 48.0)
    node_zero = start
    node_one = node_zero + fine_rate(
        half_step * node_zero + to_one(fixed_zero, fixed_one, fixed_two),
        half_step * halo_start + to_one(halo_f0, halo_f1, halo_f2),
    )
    halo_one = halo_of(node_one)
    node_two = node_one + fine_rate(
        half_step * node_one + to_two(fixed_zero, fixed_one, fixed_two),
        half_step * halo_one + to_two(halo_f0, halo_f1, halo_f2),
    )
    halo_two = halo_of(node_two)
    coarse_end = shrink(node_two)
    quadrature = fine_rate(
        node_zero + 4.0 * node_one + node_two, halo_start + 4.0 * halo_one + halo_two
    )
    source = shrink(slab_step * quadrature / 6.0)
    offset = source - slab_step * start_rate

    down = shift_pairs(slabs, 1)
    to_east = [
        (t * columns + c, (t + 1) * columns + c + 1)
        for t in range(slabs - 1)
        for c in range(columns - 1)
    ]
    to_west = [
        (t * columns + c, (t + 1) * columns + c - 1)
        for t in range(slabs - 1)
        for c in range(1, columns)
    ]
    carried = coarse_first
    carried_halo = halo_first
    rate = coarse_first_rate
    for count in range(slabs - 1):
        after = carried + slab_step * rate + offset
        passed = lax.ppermute(after, "tm", down)
        passed_b = lax.ppermute(hi(after), ("tm", "space"), to_east)
        passed_a = lax.ppermute(lo(after), ("tm", "space"), to_west)
        carried = jnp.where(first, coarse_first, passed)
        carried_halo = jnp.where(first, halo_first, pack(passed_b, passed_a))
        rate = coarse_rate(carried, carried_halo)
    finals = carried + slab_step * rate + offset
    result = add_coarse(node_two, finals - coarse_end)
    return result[None]


def solution(mesh):
    return jax.shard_map(
        body,
        mesh=mesh,
        in_specs=(
            P(None, None, "space", None),
            P(None, "space", None),
            P(None, "space", None),
            P(None, "space", None),
            P(None, "space", None),
            P(),
        ),
        out_specs=P("tm", None, None, "space", None),
        check_vma=False,
    )
```

```python
import jax
import jax.numpy as jnp
from jax import lax
from jax.sharding import PartitionSpec as P

ITERS = 2


slab_step = 0.5
half_step = 0.25


def shift_pairs(count, steps):
    return [(i, i + steps) for i in range(max(0, -steps), min(count, count - steps))]


def exchange(to_right, to_left):
    count = lax.axis_size("space")
    before = lax.ppermute(to_right, "space", shift_pairs(count, 1))
    after = lax.ppermute(to_left, "space", shift_pairs(count, -1))
    return before, after


def lo(field, width=1):
    return field[..., :width, :]


def hi(field, width=1):
    return field[..., field.shape[-2] - width:, :]


def pack(before, after):
    return jnp.concatenate([before, after], axis=-2)


def west(halo):
    return halo[..., 0:1, :]


def east(halo):
    return halo[..., 1:2, :]


def halo_of(field):
    return pack(*exchange(hi(field), lo(field)))


def tendency(field, halo, x_speed, y_speed, h_spread, v_spread, coupling, x_spacing, z_spacing):
    reach = int(x_spacing)
    padded = jnp.concatenate([west(halo)] * reach + [field] + [east(halo)] * reach, axis=-2)
    width = field.shape[-2]
    return stencil(
        field, padded[..., 2 * reach:, :], padded[..., :width, :],
        x_speed, y_speed, h_spread, v_spread, coupling, x_spacing, z_spacing,
    )


def stencil(middle, eastward, westward, x_speed, y_speed, h_spread, v_spread, coupling,
            x_spacing, z_spacing):
    y_widths = [(0, 0)] * (middle.ndim - 1) + [(1, 1)]
    y_padded = jnp.pad(middle, y_widths)
    northward = y_padded[..., 2:]
    southward = y_padded[..., :-2]
    z_widths = [(0, 0)] * (middle.ndim - 3) + [(1, 1), (0, 0), (0, 0)]
    z_padded = jnp.pad(middle, z_widths)
    upward = z_padded[..., 2:, :, :]
    downward = z_padded[..., :-2, :, :]
    advection = (
        x_speed * (eastward - westward) / (2.0 * x_spacing)
        + y_speed * (northward - southward) * 0.5
    )
    diffusion = h_spread * (
        (eastward - 2.0 * middle + westward) / (x_spacing * x_spacing)
        + (northward - 2.0 * middle + southward)
    )
    vertical = v_spread * (upward - 2.0 * middle + downward) / (z_spacing * z_spacing)
    tracer = lax.broadcasted_iota(jnp.int32, (2, 1, 1, 1), 0)
    swapped = middle[::-1]
    reaction = jnp.where(
        tracer == 0,
        coupling[0, 0] * middle + coupling[0, 1] * swapped,
        coupling[1, 1] * middle + coupling[1, 0] * swapped,
    )
    return diffusion + vertical - advection + reaction


def pair_sum(field):
    row = lax.broadcasted_iota(jnp.int32, field.shape, field.ndim - 2)
    partner = jnp.where(
        row % 2 == 0, jnp.roll(field, -1, axis=-2), jnp.roll(field, 1, axis=-2)
    )
    return field + partner


def shrink(field):
    levels = field[..., 0::2, :, :] + field[..., 1::2, :, :]
    return pair_sum(levels) * 0.25


def expand(field):
    return jnp.repeat(field, 2, axis=-3)


def add_coarse(fine, coarse):
    shape = fine.shape
    paired = fine.reshape(shape[:-3] + (shape[-3] // 2, 2) + shape[-2:])
    return (paired + jnp.expand_dims(coarse, -3)).reshape(shape)


def pick(items, index):
    out = items[0]
    for k in range(1, len(items)):
        out = jax.tree.map(lambda new, old: jnp.where(index == k, new, old), items[k], out)
    return out


def pair_map(fn, *halos):
    return fn(*halos)


def body(initial, x_velocity, y_velocity, h_diffusion, v_diffusion, coupling):
    coarse_x = shrink(x_velocity)
    coarse_y = shrink(y_velocity)
    coarse_h = shrink(h_diffusion)
    coarse_v = shrink(v_diffusion)
    slabs = lax.axis_size("tm")
    columns = lax.axis_size("space")
    slab = lax.axis_index("tm")
    first = slab == 0

    def fine_rate(field, halo):
        return tendency(
            field, halo, x_velocity, y_velocity, h_diffusion, v_diffusion, coupling, 1.0, 1.0
        )

    def coarse_rate(field, halo):
        return tendency(field, halo, coarse_x, coarse_y, coarse_h, coarse_v, coupling, 2.0, 2.0)

    def first_node(node_zero, rate_zero, s0, s1, s2):
        return (
            node_zero
            + half_step * (rate_zero - s0)
            + slab_step * (s0 * (5.0 / 24.0) + s1 * (1.0 / 3.0) - s2 * (1.0 / 24.0))
        )

    def second_node(node_one, rate_one, s0, s1, s2):
        return (
            node_one
            + half_step * (rate_one - s1)
            + slab_step * (s0 * (-1.0 / 24.0) + s1 * (1.0 / 3.0) + s2 * (5.0 / 24.0))
        )

    coarse_first = shrink(initial)
    levels = initial.shape[-3]

    def joined(fine, coarse):
        return jnp.concatenate([fine, coarse], axis=-3)

    coarse_coefs = (coarse_x, coarse_y, coarse_h, coarse_v)
    coarse_levels = coarse_first.shape[-3]

    def coef_edge(edge):
        stacked = jnp.stack([edge(c) for c in coarse_coefs])
        return stacked.reshape((2, -1) + stacked.shape[-2:])

    before, after = exchange(
        joined(joined(hi(initial), hi(coarse_first)), coef_edge(hi)),
        joined(joined(lo(initial), lo(coarse_first)), coef_edge(lo)),
    )
    split = (levels, levels + coarse_levels)
    init_b, first_b = before[..., : split[0], :, :], before[..., split[0] : split[1], :, :]
    init_a, first_a = after[..., : split[0], :, :], after[..., split[0] : split[1], :, :]
    edge_coefs = pack(before[..., split[1] :, :, :], after[..., split[1] :, :, :])
    edge_coefs = edge_coefs.reshape((4, coarse_levels) + edge_coefs.shape[-2:])
    halo_zero = pack(init_b, init_a)
    halo_first = pack(first_b, first_a)
    first_rate = fine_rate(initial, halo_zero)
    coarse_first_rate = coarse_rate(coarse_first, halo_first)

    node_zero = initial
    rate_zero = first_rate
    node_one = first_node(node_zero, rate_zero, first_rate, first_rate, first_rate)
    halo_one = halo_of(node_one)
    rate_one = fine_rate(node_one, halo_one)
    node_two = second_node(node_one, rate_one, first_rate, first_rate, first_rate)
    two_b, two_a = exchange(hi(node_two, 2), lo(node_two, 2))
    halo_two = pack(hi(two_b), lo(two_a))
    coarse_end = shrink(node_two)
    halo_end = pack(hi(shrink(two_b)), lo(shrink(two_a)))
    rate_two = fine_rate(node_two, halo_two)
    source = shrink(slab_step * (rate_zero + 4.0 * rate_one + rate_two) / 6.0)
    offset = source - slab_step * coarse_first_rate

    chain = [coarse_first]
    chain_halo = [halo_first]
    rate = coarse_first_rate
    rates = [rate]
    wide = None
    for count in range(slabs):
        after = chain[-1] + slab_step * rate + offset
        if wide is not None:
            strip_b, strip_a, offset_edge = wide
            edge = pack(strip_b[..., 2:3, :], strip_a[..., 0:1, :])
            edge_rate = stencil(
                edge,
                pack(lo(chain[-1]), strip_a[..., 2:3, :]),
                pack(strip_b[..., 0:1, :], hi(chain[-1])),
                *(edge_coefs[k] for k in range(4)),
                coupling, 2.0, 2.0,
            )
            after_halo = edge + slab_step * edge_rate + offset_edge
        elif count + 2 == slabs:
            packed_b, packed_a = exchange(
                jnp.concatenate([hi(after, 3), hi(offset)], axis=-2),
                jnp.concatenate([lo(after, 3), lo(offset)], axis=-2),
            )
            strip_b, strip_a = packed_b[..., :3, :], packed_a[..., :3, :]
            wide = (strip_b, strip_a, pack(packed_b[..., 3:, :], packed_a[..., 3:, :]))
            after_halo = pack(strip_b[..., 2:3, :], strip_a[..., 0:1, :])
        else:
            after_halo = halo_of(after)
        chain.append(after)
        chain_halo.append(after_halo)
        if count + 1 < slabs:
            rate = coarse_rate(after, after_halo)
            rates.append(rate)
    begins = pick(chain, slab)
    finals = pick(chain, slab + 1)
    begins_halo = pick(chain_halo, slab)
    finals_halo = pick(chain_halo, slab + 1)

    delta_zero = begins - coarse_first
    delta_one = finals - coarse_end
    fixed_zero = add_coarse(node_zero, delta_zero)
    fixed_one = add_coarse(node_one, (delta_zero + delta_one) * 0.5)
    fixed_two = add_coarse(node_two, delta_one)
    halo_dz = pair_map(lambda y, v: y - v, begins_halo, halo_first)
    halo_d1 = pair_map(lambda y, v: y - v, finals_halo, halo_end)
    halo_f0 = add_coarse(halo_zero, halo_dz)
    halo_f1 = add_coarse(halo_one, (halo_dz + halo_d1) * 0.5)
    halo_f2 = add_coarse(halo_two, halo_d1)

    earlier_delta = begins - coarse_end
    earlier_end = add_coarse(node_two, earlier_delta)
    halo_earlier_delta = pair_map(lambda y, v: y - v, begins_halo, halo_end)
    halo_earlier = add_coarse(halo_two, halo_earlier_delta)
    start = jnp.where(first, initial, earlier_end)
    halo_start = pair_map(lambda a, b: jnp.where(first, a, b), halo_zero, halo_earlier)
    start_rate = pick(rates, slab)

    def combined(c0, c1, c2):
        return lambda u0, u1, u2: c0 * u0 + c1 * u1 + c2 * u2

    to_one = combined(-7.0 / 48.0, 1.0 / 6.0, -1.0 / 48.0)
    to_two = combined(-1.0 / 48.0, -1.0 / 12.0, 5.0 / 48.0)
    node_zero = start
    node_one = node_zero + fine_rate(
        half_step * node_zero + to_one(fixed_zero, fixed_one, fixed_two),
        half_step * halo_start + to_one(halo_f0, halo_f1, halo_f2),
    )
    halo_one = halo_of(node_one)
    node_two = node_one + fine_rate(
        half_step * node_one + to_two(fixed_zero, fixed_one, fixed_two),
        half_step * halo_one + to_two(halo_f0, halo_f1, halo_f2),
    )
    halo_two = halo_of(node_two)
    coarse_end = shrink(node_two)
    quadrature = fine_rate(
        node_zero + 4.0 * node_one + node_two, halo_start + 4.0 * halo_one + halo_two
    )
    source = shrink(slab_step * quadrature / 6.0)
    offset = source - slab_step * start_rate

    down = shift_pairs(slabs, 1)
    to_east = [
        (t * columns + c, (t + 1) * columns + c + 1)
        for t in range(slabs - 1)
        for c in range(columns - 1)
    ]
    to_west = [
        (t * columns + c, (t + 1) * columns + c - 1)
        for t in range(slabs - 1)
        for c in range(1, columns)
    ]
    carried = coarse_first
    carried_halo = halo_first
    rate = coarse_first_rate
    for count in range(slabs - 1):
        after = carried + slab_step * rate + offset
        passed = lax.ppermute(after, "tm", down)
        passed_b = lax.ppermute(hi(after), ("tm", "space"), to_east)
        passed_a = lax.ppermute(lo(after), ("tm", "space"), to_west)
        carried = jnp.where(first, coarse_first, passed)
        carried_halo = jnp.where(first, halo_first, pack(passed_b, passed_a))
        rate = coarse_rate(carried, carried_halo)
    finals = carried + slab_step * rate + offset
    result = add_coarse(node_two, finals - coarse_end)
    return result[None]


def solution(mesh):
    return jax.shard_map(
        body,
        mesh=mesh,
        in_specs=(
            P(None, None, "space", None),
            P(None, "space", None),
            P(None, "space", None),
            P(None, "space", None),
            P(None, "space", None),
            P(),
        ),
        out_specs=P("tm", None, None, "space", None),
        check_vma=False,
    )
```

```python
import jax
import jax.numpy as jnp
from jax import lax
from jax.sharding import PartitionSpec as P

ITERS = 2


slab_step = 0.5
half_step = 0.25


def shift_pairs(count, steps):
    return [(i, i + steps) for i in range(max(0, -steps), min(count, count - steps))]


def exchange(to_right, to_left):
    count = lax.axis_size("space")
    before = lax.ppermute(to_right, "space", shift_pairs(count, 1))
    after = lax.ppermute(to_left, "space", shift_pairs(count, -1))
    return before, after


def lo(field, width=1):
    return field[..., :width, :]


def hi(field, width=1):
    return field[..., field.shape[-2] - width:, :]


def pack(before, after):
    return jnp.concatenate([before, after], axis=-2)


def west(halo):
    return halo[..., 0:1, :]


def east(halo):
    return halo[..., 1:2, :]


def halo_of(field):
    return pack(*exchange(hi(field), lo(field)))


def tendency(field, halo, x_speed, y_speed, h_spread, v_spread, coupling, x_spacing, z_spacing):
    reach = int(x_spacing)
    padded = jnp.concatenate([west(halo)] * reach + [field] + [east(halo)] * reach, axis=-2)
    width = field.shape[-2]
    return stencil(
        field, padded[..., 2 * reach:, :], padded[..., :width, :],
        x_speed, y_speed, h_spread, v_spread, coupling, x_spacing, z_spacing,
    )


def stencil(middle, eastward, westward, x_speed, y_speed, h_spread, v_spread, coupling,
            x_spacing, z_spacing):
    y_widths = [(0, 0)] * (middle.ndim - 1) + [(1, 1)]
    y_padded = jnp.pad(middle, y_widths)
    northward = y_padded[..., 2:]
    southward = y_padded[..., :-2]
    z_widths = [(0, 0)] * (middle.ndim - 3) + [(1, 1), (0, 0), (0, 0)]
    z_padded = jnp.pad(middle, z_widths)
    upward = z_padded[..., 2:, :, :]
    downward = z_padded[..., :-2, :, :]
    advection = (
        x_speed * (eastward - westward) / (2.0 * x_spacing)
        + y_speed * (northward - southward) * 0.5
    )
    diffusion = h_spread * (
        (eastward - 2.0 * middle + westward) / (x_spacing * x_spacing)
        + (northward - 2.0 * middle + southward)
    )
    vertical = v_spread * (upward - 2.0 * middle + downward) / (z_spacing * z_spacing)
    tracer = lax.broadcasted_iota(jnp.int32, (2, 1, 1, 1), 0)
    own = jnp.where(tracer == 0, coupling[0, 0], coupling[1, 1])
    other = jnp.where(tracer == 0, coupling[0, 1], coupling[1, 0])
    reaction = own * middle + other * middle[::-1]
    return diffusion + vertical - advection + reaction


def pair_sum(field):
    row = lax.broadcasted_iota(jnp.int32, field.shape, field.ndim - 2)
    partner = jnp.where(
        row % 2 == 0, jnp.roll(field, -1, axis=-2), jnp.roll(field, 1, axis=-2)
    )
    return field + partner


def shrink(field):
    levels = field[..., 0::2, :, :] + field[..., 1::2, :, :]
    return pair_sum(levels) * 0.25


def expand(field):
    return jnp.repeat(field, 2, axis=-3)


def add_coarse(fine, coarse):
    shape = fine.shape
    paired = fine.reshape(shape[:-3] + (shape[-3] // 2, 2) + shape[-2:])
    return (paired + jnp.expand_dims(coarse, -3)).reshape(shape)


def pick(items, index):
    out = items[0]
    for k in range(1, len(items)):
        out = jax.tree.map(lambda new, old: jnp.where(index == k, new, old), items[k], out)
    return out


def pair_map(fn, *halos):
    return fn(*halos)


def body(initial, x_velocity, y_velocity, h_diffusion, v_diffusion, coupling):
    coarse_x = shrink(x_velocity)
    coarse_y = shrink(y_velocity)
    coarse_h = shrink(h_diffusion)
    coarse_v = shrink(v_diffusion)
    slabs = lax.axis_size("tm")
    columns = lax.axis_size("space")
    slab = lax.axis_index("tm")
    first = slab == 0

    def fine_rate(field, halo):
        return tendency(
            field, halo, x_velocity, y_velocity, h_diffusion, v_diffusion, coupling, 1.0, 1.0
        )

    def coarse_rate(field, halo):
        return tendency(field, halo, coarse_x, coarse_y, coarse_h, coarse_v, coupling, 2.0, 2.0)

    def first_node(node_zero, rate_zero, s0, s1, s2):
        return (
            node_zero
            + half_step * (rate_zero - s0)
            + slab_step * (s0 * (5.0 / 24.0) + s1 * (1.0 / 3.0) - s2 * (1.0 / 24.0))
        )

    def second_node(node_one, rate_one, s0, s1, s2):
        return (
            node_one
            + half_step * (rate_one - s1)
            + slab_step * (s0 * (-1.0 / 24.0) + s1 * (1.0 / 3.0) + s2 * (5.0 / 24.0))
        )

    coarse_first = shrink(initial)
    levels = initial.shape[-3]

    def joined(fine, coarse):
        return jnp.concatenate([fine, coarse], axis=-3)

    coarse_coefs = (coarse_x, coarse_y, coarse_h, coarse_v)
    coarse_levels = coarse_first.shape[-3]

    def coef_edge(edge):
        stacked = jnp.stack([edge(c) for c in coarse_coefs])
        return stacked.reshape((2, -1) + stacked.shape[-2:])

    before, after = exchange(
        joined(joined(hi(initial), hi(coarse_first)), coef_edge(hi)),
        joined(joined(lo(initial), lo(coarse_first)), coef_edge(lo)),
    )
    split = (levels, levels + coarse_levels)
    init_b, first_b = before[..., : split[0], :, :], before[..., split[0] : split[1], :, :]
    init_a, first_a = after[..., : split[0], :, :], after[..., split[0] : split[1], :, :]
    edge_coefs = pack(before[..., split[1] :, :, :], after[..., split[1] :, :, :])
    edge_coefs = edge_coefs.reshape((4, coarse_levels) + edge_coefs.shape[-2:])
    halo_zero = pack(init_b, init_a)
    halo_first = pack(first_b, first_a)
    first_rate = fine_rate(initial, halo_zero)
    coarse_first_rate = coarse_rate(coarse_first, halo_first)

    node_zero = initial
    rate_zero = first_rate
    node_one = node_zero + half_step * rate_zero
    halo_one = halo_of(node_one)
    rate_one = fine_rate(node_one, halo_one)
    node_two = node_one + half_step * rate_one
    two_b, two_a = exchange(hi(node_two, 2), lo(node_two, 2))
    halo_two = pack(hi(two_b), lo(two_a))
    coarse_end = shrink(node_two)
    halo_end = pack(hi(shrink(two_b)), lo(shrink(two_a)))
    rate_two = fine_rate(node_two, halo_two)
    source = shrink(slab_step * (rate_zero + 4.0 * rate_one + rate_two) / 6.0)
    offset = source - slab_step * coarse_first_rate

    chain = [coarse_first]
    chain_halo = [halo_first]
    rate = coarse_first_rate
    rates = [rate]
    wide = None
    for count in range(slabs):
        after = chain[-1] + slab_step * rate + offset
        if wide is not None:
            strip_b, strip_a, offset_edge = wide
            edge = pack(strip_b[..., 2:3, :], strip_a[..., 0:1, :])
            edge_rate = stencil(
                edge,
                pack(lo(chain[-1]), strip_a[..., 2:3, :]),
                pack(strip_b[..., 0:1, :], hi(chain[-1])),
                *(edge_coefs[k] for k in range(4)),
                coupling, 2.0, 2.0,
            )
            after_halo = edge + slab_step * edge_rate + offset_edge
        elif count + 2 == slabs:
            packed_b, packed_a = exchange(
                jnp.concatenate([hi(after, 3), hi(offset)], axis=-2),
                jnp.concatenate([lo(after, 3), lo(offset)], axis=-2),
            )
            strip_b, strip_a = packed_b[..., :3, :], packed_a[..., :3, :]
            wide = (strip_b, strip_a, pack(packed_b[..., 3:, :], packed_a[..., 3:, :]))
            after_halo = pack(strip_b[..., 2:3, :], strip_a[..., 0:1, :])
        else:
            after_halo = halo_of(after)
        chain.append(after)
        chain_halo.append(after_halo)
        if count + 1 < slabs:
            rate = coarse_rate(after, after_halo)
            rates.append(rate)
    begins = pick(chain, slab)
    finals = pick(chain, slab + 1)
    begins_halo = pick(chain_halo, slab)
    finals_halo = pick(chain_halo, slab + 1)

    delta_zero = begins - coarse_first
    delta_one = finals - coarse_end
    fixed_zero = add_coarse(node_zero, delta_zero)
    fixed_one = add_coarse(node_one, (delta_zero + delta_one) * 0.5)
    fixed_two = add_coarse(node_two, delta_one)
    halo_dz = pair_map(lambda y, v: y - v, begins_halo, halo_first)
    halo_d1 = pair_map(lambda y, v: y - v, finals_halo, halo_end)
    halo_f0 = add_coarse(halo_zero, halo_dz)
    halo_f1 = add_coarse(halo_one, (halo_dz + halo_d1) * 0.5)
    halo_f2 = add_coarse(halo_two, halo_d1)

    earlier_delta = begins - coarse_end
    earlier_end = add_coarse(node_two, earlier_delta)
    halo_earlier_delta = pair_map(lambda y, v: y - v, begins_halo, halo_end)
    halo_earlier = add_coarse(halo_two, halo_earlier_delta)
    start = jnp.where(first, initial, earlier_end)
    halo_start = pair_map(lambda a, b: jnp.where(first, a, b), halo_zero, halo_earlier)
    start_rate = pick(rates, slab)

    def combined(c0, c1, c2):
        return lambda u0, u1, u2: c0 * u0 + c1 * u1 + c2 * u2

    to_one = combined(-7.0 / 48.0, 1.0 / 6.0, -1.0 / 48.0)
    to_two = combined(-1.0 / 48.0, -1.0 / 12.0, 5.0 / 48.0)
    node_zero = start
    node_one = node_zero + fine_rate(
        half_step * node_zero + to_one(fixed_zero, fixed_one, fixed_two),
        half_step * halo_start + to_one(halo_f0, halo_f1, halo_f2),
    )
    halo_one = halo_of(node_one)
    node_two = node_one + fine_rate(
        half_step * node_one + to_two(fixed_zero, fixed_one, fixed_two),
        half_step * halo_one + to_two(halo_f0, halo_f1, halo_f2),
    )
    halo_two = halo_of(node_two)
    coarse_end = shrink(node_two)
    quadrature = fine_rate(
        node_zero + 4.0 * node_one + node_two, halo_start + 4.0 * halo_one + halo_two
    )
    source = shrink(slab_step * quadrature / 6.0)
    offset = source - slab_step * start_rate

    down = shift_pairs(slabs, 1)
    to_east = [
        (t * columns + c, (t + 1) * columns + c + 1)
        for t in range(slabs - 1)
        for c in range(columns - 1)
    ]
    to_west = [
        (t * columns + c, (t + 1) * columns + c - 1)
        for t in range(slabs - 1)
        for c in range(1, columns)
    ]
    carried = coarse_first
    carried_halo = halo_first
    rate = coarse_first_rate
    for count in range(slabs - 1):
        after = carried + slab_step * rate + offset
        passed = lax.ppermute(after, "tm", down)
        passed_b = lax.ppermute(hi(after), ("tm", "space"), to_east)
        passed_a = lax.ppermute(lo(after), ("tm", "space"), to_west)
        carried = jnp.where(first, coarse_first, passed)
        carried_halo = jnp.where(first, halo_first, pack(passed_b, passed_a))
        rate = coarse_rate(carried, carried_halo)
    finals = carried + slab_step * rate + offset
    result = add_coarse(node_two, finals - coarse_end)
    return result[None]


def solution(mesh):
    return jax.shard_map(
        body,
        mesh=mesh,
        in_specs=(
            P(None, None, "space", None),
            P(None, "space", None),
            P(None, "space", None),
            P(None, "space", None),
            P(None, "space", None),
            P(),
        ),
        out_specs=P("tm", None, None, "space", None),
        check_vma=False,
    )
```
